32 devices in a mesh: xy: 16 (over z, y, core), gz: 2 (over x).
Axes of the slice: x: 2, y: 2, z: 4, core: 2. Of those that a mesh axis runs over, the one named last changes fastest.
Arguments:
- volume: float32 [32, 262144], P('gz', 'xy'), may hold values from -4 to 4
- measured: float32 [2, 32, 4096], P(None, 'gz', 'xy'), may hold values from -12 to 12
- band_start: int32 [2, 16], P(None, 'xy'), may hold values from 0 to 3584
- column_offset: int32 [2, 262144], P(None, 'xy'), may hold values from 0 to 509
- column_width: int32 [2, 262144], P(None, 'xy'), may hold values from 1 to 3
- amplitude: float32 [2, 262144], P(None, 'xy'), may hold values from 0.01 to 0.1
- axial_weight: float32 [3, 2, 32], P(None, None, 'gz'), may hold values from 0.2 to 1
Outputs:
- volume_next: float32 [32, 262144], P('gz', 'xy')
- residual: float32 [2, 32, 4096], P(None, 'gz', 'xy')
The draws below stay inside these ranges and needn't reach their ends.
All inputs are finite; a program needn't handle non-finite values.
Results may differ from the reference program's by a relative error of at most 0.0003.
Values sent between devices are 32-bit elements; how exact they have to be, the bound alone decides.
No kernel may reach another device: no remote copies, remote signals or barrier semaphores. Data moves between devices by JAX's collectives and lax.ppermute only.
A program may use at most 64 MiB of HBM per device.

```python
import math
import jax
import jax.numpy as jnp
from jax import lax

V = 2
C = 16384
U = 4096
B = 512
WMAX = 3
S = 32
NCOL = 262144
NTILE = 16
N_XY = 16


def place_ends(array, stream_key, smallest, top_value):
    longest = array.shape.index(max(array.shape))
    spots = []
    for shift in (0, 1):
        where = [jax.random.randint(jax.random.fold_in(stream_key, axis), (), 0, length) for axis, length in enumerate(array.shape)]
        where[longest] = (where[longest] + shift) % array.shape[longest]
        spots.append(tuple(where))
    return array.at[spots[0]].set(smallest).at[spots[1]].set(top_value)


def levels(stream_key, dims, pieces, least, high):
    level, own = 1.0, jax.random.fold_in(stream_key, 6)
    for dim, parts in pieces:
        heights = jnp.exp(jax.random.uniform(jax.random.fold_in(own, dim), (parts,), jnp.float32, least / len(pieces), high / len(pieces)))
        level = level * jnp.repeat(heights, dims[dim] // parts).reshape([-1 if axis == dim else 1 for axis in range(len(dims))])
    return level


def normal_values(stream_key, extent, spread, limit, pieces=(), kind=jnp.bfloat16):
    entries = spread * jax.random.normal(stream_key, extent, jnp.float32)
    if pieces:
        entries = entries * levels(stream_key, extent, pieces, -0.22, 0.18)
    return jnp.clip(entries, -limit, limit).astype(kind)


def setup_inputs(seed: int = 0) -> dict:
    streams_of = jax.random.split(jax.random.key(seed), 8)
    volume = normal_values(streams_of[0], (S, NCOL), 0.5, 4.0, ((0, 2), (1, 16)), jnp.float32)
    measured = normal_values(streams_of[1], (V, S, U), 2.0, 12.0, ((1, 2), (2, 16)), jnp.float32)
    band_start = place_ends(jax.random.randint(streams_of[2], (V, NTILE), 0, U - B + 1), jax.random.fold_in(streams_of[2], 1), 0, U - B).astype(jnp.int32)
    column_offset = place_ends(jax.random.randint(streams_of[3], (V, NCOL), 0, B - WMAX + 1), jax.random.fold_in(streams_of[3], 1), 0, B - WMAX).astype(jnp.int32)
    column_width = place_ends(jax.random.randint(streams_of[4], (V, NCOL), 1, WMAX + 1), jax.random.fold_in(streams_of[4], 1), 1, WMAX).astype(jnp.int32)
    amplitude = jnp.clip(jnp.exp(math.log(0.1) - 2.3025851 * jax.random.uniform(streams_of[5], (V, NCOL), jnp.float32) ** levels(streams_of[5], (V, NCOL), ((1, 16),), -0.2, 0.2)), 0.01, 0.1)
    axial_weight = jnp.clip(0.2 + 0.8 * jax.random.uniform(streams_of[6], (3, V, S), jnp.float32) ** levels(streams_of[6], (3, V, S), ((2, 2),), -0.2, 0.2), 0.2, 1.0)
    return dict(volume=volume, measured=measured, band_start=band_start, column_offset=column_offset, column_width=column_width, amplitude=amplitude, axial_weight=axial_weight)


RELAX = 0.9


def footprint(amp_block, off_block, wid_block, band_width):
    positions = jnp.arange(band_width, dtype=jnp.int32)[None, :]
    inside = (positions >= off_block[:, None]) & (positions < (off_block + wid_block)[:, None])
    return jnp.where(inside, amp_block[:, None], jnp.zeros((), jnp.float32))


def spread_rows(field, weight_rows):
    lower_part = weight_rows[0][:, :, None] * field
    upper_part = weight_rows[2][:, :, None] * field
    zero_row = jnp.zeros_like(field[:, :1])
    return (weight_rows[1][:, :, None] * field
            + jnp.concatenate([lower_part[:, 1:], zero_row], axis=1)
            + jnp.concatenate([zero_row, upper_part[:, :-1]], axis=1))


def gather_rows(field, weight_rows):
    zero_row = jnp.zeros_like(field[:, :1])
    before = jnp.concatenate([zero_row, field[:, :-1]], axis=1)
    after = jnp.concatenate([field[:, 1:], zero_row], axis=1)
    return (weight_rows[0][:, :, None] * before + weight_rows[1][:, :, None] * field
            + weight_rows[2][:, :, None] * after)


def reference(volume, measured, band_start, column_offset, column_width, amplitude, axial_weight):
    highest = lax.Precision.HIGHEST
    tile_cells = volume.reshape(S, N_XY, C).transpose(1, 0, 2)
    tile_amp = amplitude.reshape(V, N_XY, C).transpose(1, 0, 2)
    tile_off = column_offset.reshape(V, N_XY, C).transpose(1, 0, 2)
    tile_wid = column_width.reshape(V, N_XY, C).transpose(1, 0, 2)
    tile_start = band_start.T

    def project_tile(running, item):
        proj_cols, cover = running
        slab_cells, amp_rows, off_rows, wid_rows, starts = item
        next_proj = []
        next_cover = []
        for view_index in range(V):
            weights = footprint(amp_rows[view_index], off_rows[view_index], wid_rows[view_index], B)
            partial_value = jnp.dot(slab_cells, weights, precision=highest)
            anchor = starts[view_index]
            current = lax.dynamic_slice(proj_cols[view_index], (jnp.int32(0), anchor), (S, B))
            next_proj.append(lax.dynamic_update_slice(proj_cols[view_index], current + partial_value, (jnp.int32(0), anchor)))
            covered = lax.dynamic_slice_in_dim(cover[view_index], anchor, B, 0)
            next_cover.append(lax.dynamic_update_slice_in_dim(cover[view_index], covered + jnp.sum(weights, axis=0), anchor, 0))
        return (jnp.stack(next_proj), jnp.stack(next_cover)), None

    starting = (jnp.zeros((V, S, U), jnp.float32), jnp.zeros((V, U), jnp.float32))
    outcome = lax.scan(project_tile, starting, (tile_cells, tile_amp, tile_off, tile_wid, tile_start))
    proj_cols, cover = outcome[0]
    projection = spread_rows(proj_cols, axial_weight)
    coverage = spread_rows(jnp.broadcast_to(cover[:, None, :], (V, S, U)), axial_weight)
    residual = (measured - projection) / jnp.maximum(coverage, 1.0)
    back_rows = gather_rows(residual, axial_weight)

    global_rows = jnp.arange(S, dtype=jnp.int32)
    row_weight = (jnp.where(global_rows[None, :] > 0, axial_weight[0], 0.0) + axial_weight[1]
                  + jnp.where(global_rows[None, :] < S - 1, axial_weight[2], 0.0))

    def update_tile(slab_cells, amp_rows, off_rows, wid_rows, starts):
        correction = jnp.zeros((S, C), jnp.float32)
        normalizer = jnp.zeros((S, C), jnp.float32)
        column_mass = amp_rows * wid_rows.astype(jnp.float32)
        for view_index in range(V):
            weights = footprint(amp_rows[view_index], off_rows[view_index], wid_rows[view_index], B)
            band_rows = lax.dynamic_slice(back_rows[view_index], (jnp.int32(0), starts[view_index]), (S, B))
            correction = correction + jnp.einsum("sj,cj->sc", band_rows, weights, precision=highest)
        for view_index in range(V):
            normalizer = normalizer + row_weight[view_index][:, None] * column_mass[view_index][None, :]
        return slab_cells + RELAX * correction / normalizer

    def update_step(running, item):
        return running, update_tile(*item)

    updated = lax.scan(update_step, jnp.zeros((), jnp.float32), (tile_cells, tile_amp, tile_off, tile_wid, tile_start))[1]
    volume_next = updated.transpose(1, 0, 2).reshape(S, N_XY * C)
    return volume_next, residual
```

```python
import jax
import jax.numpy as jnp
from jax import lax
from jax.experimental import pallas as pl
from jax.experimental.pallas import tpu as pltpu
from jax.sharding import PartitionSpec as P

B = 512
RELAX = 0.9
CHUNK = 512
INTERPRET = False


def _band_mask(off, wid, rows, width):
    u = lax.broadcasted_iota(jnp.int32, (rows, width), 0)
    inside = (u >= off) & (u < off + wid)
    return jnp.where(inside, 1.0, 0.0).astype(jnp.bfloat16)


def _split(x):
    hi = x.astype(jnp.bfloat16)
    lo = (x - hi.astype(jnp.float32)).astype(jnp.bfloat16)
    return hi, lo


def _forward_kernel(vol_ref, amp_ref, off_ref, wid_ref, out_ref):
    slab_rows, columns = vol_ref.shape
    view_count = amp_ref.shape[0]
    band = out_ref.shape[2]
    out_ref[...] = jnp.zeros(out_ref.shape, jnp.float32)
    row = lax.broadcasted_iota(jnp.int32, (slab_rows, CHUNK), 0)

    def body(j, carry):
        c0 = pl.multiple_of(j * CHUNK, CHUNK)
        cells = vol_ref[:, pl.ds(c0, CHUNK)]
        for v in range(view_count):
            amp = amp_ref[pl.ds(v, 1), pl.ds(c0, CHUNK)]
            off = off_ref[pl.ds(v, 1), pl.ds(c0, CHUNK)]
            wid = wid_ref[pl.ds(v, 1), pl.ds(c0, CHUNK)]
            x = jnp.concatenate([cells * amp, jnp.where(row == 0, amp, 0.0)], axis=0)
            hi, lo = _split(x)
            lhs = jnp.concatenate([hi, lo], axis=0)
            mask = _band_mask(off, wid, band, CHUNK)
            out_ref[v] += lax.dot_general(
                lhs, mask, (((1,), (1,)), ((), ())), preferred_element_type=jnp.float32
            )
        return carry

    lax.fori_loop(0, columns // CHUNK, body, 0)


def forward_band(volume, amplitude, column_offset, column_width):
    slab_rows = volume.shape[0]
    view_count = amplitude.shape[0]
    acc = pl.pallas_call(
        _forward_kernel,
        out_shape=jax.ShapeDtypeStruct((view_count, 4 * slab_rows, B), jnp.float32),
        interpret=INTERPRET,
    )(volume, amplitude, column_offset, column_width)
    summed = acc[:, : 2 * slab_rows] + acc[:, 2 * slab_rows :]
    return summed[:, : slab_rows + 1]


def _backward_kernel(back_ref, vol_ref, amp_ref, off_ref, wid_ref, rw_ref, out_ref, split_ref):
    slab_rows, columns = vol_ref.shape
    view_count, _, band = back_ref.shape
    for v in range(view_count):
        hi, lo = _split(back_ref[v])
        split_ref[v] = jnp.concatenate([hi, lo], axis=0)

    def body(j, carry):
        c0 = pl.multiple_of(j * CHUNK, CHUNK)
        correction = None
        normalizer = None
        for v in range(view_count):
            amp = amp_ref[pl.ds(v, 1), pl.ds(c0, CHUNK)]
            off = off_ref[pl.ds(v, 1), pl.ds(c0, CHUNK)]
            wid = wid_ref[pl.ds(v, 1), pl.ds(c0, CHUNK)]
            mask = _band_mask(off, wid, band, CHUNK)
            r = jnp.dot(split_ref[v], mask, preferred_element_type=jnp.float32)
            part = amp * (r[:slab_rows] + r[slab_rows:])
            mass = rw_ref[v] * (amp * wid.astype(jnp.float32))
            correction = part if correction is None else correction + part
            normalizer = mass if normalizer is None else normalizer + mass
        cells = vol_ref[:, pl.ds(c0, CHUNK)]
        out_ref[:, pl.ds(c0, CHUNK)] = cells + RELAX * correction / normalizer
        return carry

    lax.fori_loop(0, columns // CHUNK, body, 0)


def backward_update(back_band, volume, amplitude, column_offset, column_width, row_weight):
    view_count, slab_rows, band = back_band.shape
    return pl.pallas_call(
        _backward_kernel,
        out_shape=jax.ShapeDtypeStruct(volume.shape, jnp.float32),
        scratch_shapes=[pltpu.VMEM((view_count, 2 * slab_rows, band), jnp.bfloat16)],
        interpret=INTERPRET,
    )(back_band, volume, amplitude, column_offset, column_width, row_weight[:, :, None])


def local(volume, measured, band_start, column_offset, column_width, amplitude, axial_weight):
    slab_rows = volume.shape[0]
    view_count = amplitude.shape[0]
    xy_count = lax.axis_size("xy")
    gz_count = lax.axis_size("gz")
    shard_width = measured.shape[2]
    detector_width = shard_width * xy_count
    total_rows = slab_rows * gz_count
    first_row = lax.axis_index("gz") * slab_rows
    up_pairs = [(i, i + 1) for i in range(gz_count - 1)]
    down_pairs = [(i + 1, i) for i in range(gz_count - 1)]

    weights_all = lax.all_gather(axial_weight, "gz", axis=2, tiled=True)
    padded_weights = jnp.pad(weights_all, ((0, 0), (0, 0), (2, 2)))
    measured_ext = jnp.concatenate(
        [
            lax.ppermute(measured[:, slab_rows - 1 :], "gz", up_pairs),
            measured,
            lax.ppermute(measured[:, :1], "gz", down_pairs),
        ],
        axis=1,
    )

    band_rows = forward_band(volume, amplitude, column_offset, column_width)
    placed = []
    for v in range(view_count):
        blank = jnp.zeros((slab_rows + 1, detector_width), jnp.float32)
        placed.append(lax.dynamic_update_slice(blank, band_rows[v], (jnp.int32(0), band_start[v, 0])))
    reduced = lax.psum_scatter(jnp.stack(placed), "xy", scatter_dimension=2, tiled=True)
    proj_cols = reduced[:, :slab_rows]
    cover = reduced[:, slab_rows : slab_rows + 1]
    proj_ext = jnp.concatenate(
        [
            lax.ppermute(proj_cols[:, slab_rows - 2 :], "gz", up_pairs),
            proj_cols,
            lax.ppermute(proj_cols[:, :2], "gz", down_pairs),
        ],
        axis=1,
    )

    ext_rows = slab_rows + 2

    def weight_rows(kind, shift):
        return lax.dynamic_slice_in_dim(padded_weights[kind], first_row + 1 + shift, ext_rows, 1)[:, :, None]

    mid_w = weight_rows(1, 0)
    next_w = weight_rows(0, 1)
    prev_w = weight_rows(2, -1)
    centre = proj_ext[:, 1 : ext_rows + 1]
    after = proj_ext[:, 2 : ext_rows + 2]
    before = proj_ext[:, 0:ext_rows]
    projection = mid_w * centre + next_w * after + prev_w * before
    coverage = mid_w * cover + next_w * cover + prev_w * cover
    residual_ext = (measured_ext - projection) / jnp.maximum(coverage, 1.0)
    global_rows = first_row - 1 + jnp.arange(ext_rows, dtype=jnp.int32)
    valid = (global_rows >= 0) & (global_rows < total_rows)
    residual_ext = jnp.where(valid[None, :, None], residual_ext, 0.0)
    residual = residual_ext[:, 1 : slab_rows + 1]

    back_rows = (
        axial_weight[0][:, :, None] * residual_ext[:, 0:slab_rows]
        + axial_weight[1][:, :, None] * residual
        + axial_weight[2][:, :, None] * residual_ext[:, 2 : slab_rows + 2]
    )
    back_full = lax.all_gather(back_rows, "xy", axis=2, tiled=True)
    back_band = jnp.stack(
        [
            lax.dynamic_slice(back_full[v], (jnp.int32(0), band_start[v, 0]), (slab_rows, B))
            for v in range(view_count)
        ]
    )

    own_rows = first_row + jnp.arange(slab_rows, dtype=jnp.int32)
    row_weight = (
        jnp.where(own_rows[None, :] > 0, axial_weight[0], 0.0)
        + axial_weight[1]
        + jnp.where(own_rows[None, :] < total_rows - 1, axial_weight[2], 0.0)
    )
    volume_next = backward_update(back_band, volume, amplitude, column_offset, column_width, row_weight)
    return (volume_next, residual)


def solution(mesh):
    return jax.shard_map(
        local,
        mesh=mesh,
        in_specs=(
            P("gz", "xy"),
            P(None, "gz", "xy"),
            P(None, "xy"),
            P(None, "xy"),
            P(None, "xy"),
            P(None, "xy"),
            P(None, None, "gz"),
        ),
        out_specs=(P("gz", "xy"), P(None, "gz", "xy")),
        check_vma=False,
    )
```

```python
import jax
import jax.numpy as jnp
from jax import lax
from jax.experimental import pallas as pl
from jax.experimental.pallas import tpu as pltpu
from jax.sharding import PartitionSpec as P

B = 512
RELAX = 0.9
CHUNK = 512
INTERPRET = False


def _band_mask(off, wid, rows, width):
    u = lax.broadcasted_iota(jnp.int32, (rows, width), 0)
    inside = (u >= off) & (u < off + wid)
    return jnp.where(inside, 1.0, 0.0).astype(jnp.bfloat16)


def _split(x):
    hi = x.astype(jnp.bfloat16)
    lo = (x - hi.astype(jnp.float32)).astype(jnp.bfloat16)
    return hi, lo


def _forward_kernel(vol_ref, amp_ref, off_ref, wid_ref, out_ref):
    slab_rows, columns = vol_ref.shape
    view_count = amp_ref.shape[0]
    band = out_ref.shape[2]
    out_ref[...] = jnp.zeros(out_ref.shape, jnp.float32)
    row = lax.broadcasted_iota(jnp.int32, (slab_rows, CHUNK), 0)

    def body(j, carry):
        c0 = pl.multiple_of(j * CHUNK, CHUNK)
        cells = vol_ref[:, pl.ds(c0, CHUNK)]
        for v in range(view_count):
            amp = amp_ref[pl.ds(v, 1), pl.ds(c0, CHUNK)]
            off = off_ref[pl.ds(v, 1), pl.ds(c0, CHUNK)]
            wid = wid_ref[pl.ds(v, 1), pl.ds(c0, CHUNK)]
            x = jnp.concatenate([cells * amp, jnp.where(row == 0, amp, 0.0)], axis=0)
            hi, lo = _split(x)
            lhs = jnp.concatenate([hi, lo], axis=0)
            mask = _band_mask(off, wid, band, CHUNK)
            out_ref[v] += lax.dot_general(
                lhs, mask, (((1,), (1,)), ((), ())), preferred_element_type=jnp.float32
            )
        return carry

    lax.fori_loop(0, columns // CHUNK, body, 0)


def forward_band(volume, amplitude, column_offset, column_width):
    slab_rows = volume.shape[0]
    view_count = amplitude.shape[0]
    acc = pl.pallas_call(
        _forward_kernel,
        out_shape=jax.ShapeDtypeStruct((view_count, 4 * slab_rows, B), jnp.float32),
        interpret=INTERPRET,
    )(volume, amplitude, column_offset, column_width)
    summed = acc[:, : 2 * slab_rows] + acc[:, 2 * slab_rows :]
    return summed[:, : slab_rows + 1]


def _backward_kernel(back_ref, vol_ref, amp_ref, off_ref, wid_ref, rw_ref, out_ref, split_ref):
    slab_rows, columns = vol_ref.shape
    view_count, _, band = back_ref.shape
    for v in range(view_count):
        hi, lo = _split(back_ref[v])
        split_ref[v] = jnp.concatenate([hi, lo], axis=0)

    def body(j, carry):
        c0 = pl.multiple_of(j * CHUNK, CHUNK)
        correction = None
        normalizer = None
        for v in range(view_count):
            amp = amp_ref[pl.ds(v, 1), pl.ds(c0, CHUNK)]
            off = off_ref[pl.ds(v, 1), pl.ds(c0, CHUNK)]
            wid = wid_ref[pl.ds(v, 1), pl.ds(c0, CHUNK)]
            mask = _band_mask(off, wid, band, CHUNK)
            r = jnp.dot(split_ref[v], mask, preferred_element_type=jnp.float32)
            part = amp * (r[:slab_rows] + r[slab_rows:])
            mass = rw_ref[v] * (amp * wid.astype(jnp.float32))
            correction = part if correction is None else correction + part
            normalizer = mass if normalizer is None else normalizer + mass
        cells = vol_ref[:, pl.ds(c0, CHUNK)]
        out_ref[:, pl.ds(c0, CHUNK)] = cells + RELAX * correction / normalizer
        return carry

    lax.fori_loop(0, columns // CHUNK, body, 0)


def backward_update(back_band, volume, amplitude, column_offset, column_width, row_weight):
    view_count, slab_rows, band = back_band.shape
    return pl.pallas_call(
        _backward_kernel,
        out_shape=jax.ShapeDtypeStruct(volume.shape, jnp.float32),
        scratch_shapes=[pltpu.VMEM((view_count, 2 * slab_rows, band), jnp.bfloat16)],
        interpret=INTERPRET,
    )(back_band, volume, amplitude, column_offset, column_width, row_weight[:, :, None])


def _bit_count(count):
    bits = count.bit_length() - 1
    assert 1 << bits == count
    return bits


def reduce_scatter_xy(x, count):
    lead = x.shape[:-1]
    width = x.shape[-1] // count
    bits = _bit_count(count)
    idx = lax.axis_index("xy")
    y = x.reshape(lead + (2,) * bits + (width,))
    for j in range(bits):
        axis = len(lead) + bits - 1 - j
        bit = (idx >> j) & 1
        keep = lax.dynamic_index_in_dim(y, bit, axis, keepdims=False)
        send = lax.dynamic_index_in_dim(y, 1 - bit, axis, keepdims=False)
        y = keep + lax.ppermute(send, "xy", [(i, i ^ (1 << j)) for i in range(count)])
    return y


def all_gather_xy(x, count):
    lead = x.shape[:-1]
    bits = _bit_count(count)
    idx = lax.axis_index("xy")
    y = x
    for step, j in enumerate(reversed(range(bits))):
        bit = (idx >> j) & 1
        other = lax.ppermute(y, "xy", [(i, i ^ (1 << j)) for i in range(count)])
        low = jnp.where(bit == 0, y, other)
        high = jnp.where(bit == 0, other, y)
        y = jnp.stack([low, high], axis=len(lead) + step)
    return y.reshape(lead + (count * x.shape[-1],))


def local(volume, measured, band_start, column_offset, column_width, amplitude, axial_weight):
    slab_rows = volume.shape[0]
    view_count = amplitude.shape[0]
    xy_count = lax.axis_size("xy")
    gz_count = lax.axis_size("gz")
    shard_width = measured.shape[2]
    detector_width = shard_width * xy_count
    total_rows = slab_rows * gz_count
    first_row = lax.axis_index("gz") * slab_rows
    up_pairs = [(i, i + 1) for i in range(gz_count - 1)]
    down_pairs = [(i + 1, i) for i in range(gz_count - 1)]

    def pack(meas_rows, weight_cols):
        flat = jnp.transpose(weight_cols, (1, 0, 2)).reshape(view_count, 1, -1)
        flat = jnp.pad(flat, ((0, 0), (0, 0), (0, shard_width - flat.shape[2])))
        return jnp.concatenate([meas_rows, flat], axis=1)

    def unpack(packed):
        cols = packed[:, 1, : 3 * 2].reshape(view_count, 3, 2)
        return packed[:, :1], jnp.transpose(cols, (1, 0, 2))

    from_below = lax.ppermute(
        pack(measured[:, slab_rows - 1 :], axial_weight[:, :, slab_rows - 2 :]), "gz", up_pairs
    )
    from_above = lax.ppermute(pack(measured[:, :1], axial_weight[:, :, :2]), "gz", down_pairs)
    meas_below, weight_below = unpack(from_below)
    meas_above, weight_above = unpack(from_above)
    measured_ext = jnp.concatenate([meas_below, measured, meas_above], axis=1)
    weight_ext = jnp.concatenate([weight_below, axial_weight, weight_above], axis=2)

    band_rows = forward_band(volume, amplitude, column_offset, column_width)
    placed = []
    for v in range(view_count):
        blank = jnp.zeros((slab_rows + 1, detector_width), jnp.float32)
        placed.append(lax.dynamic_update_slice(blank, band_rows[v], (jnp.int32(0), band_start[v, 0])))
    reduced = reduce_scatter_xy(jnp.stack(placed), xy_count)
    proj_cols = reduced[:, :slab_rows]
    cover = reduced[:, slab_rows : slab_rows + 1]
    proj_ext = jnp.concatenate(
        [
            lax.ppermute(proj_cols[:, slab_rows - 2 :], "gz", up_pairs),
            proj_cols,
            lax.ppermute(proj_cols[:, :2], "gz", down_pairs),
        ],
        axis=1,
    )

    ext_rows = slab_rows + 2
    mid_w = weight_ext[1, :, 1 : ext_rows + 1][:, :, None]
    next_w = weight_ext[0, :, 2 : ext_rows + 2][:, :, None]
    prev_w = weight_ext[2, :, 0:ext_rows][:, :, None]
    centre = proj_ext[:, 1 : ext_rows + 1]
    after = proj_ext[:, 2 : ext_rows + 2]
    before = proj_ext[:, 0:ext_rows]
    projection = mid_w * centre + next_w * after + prev_w * before
    coverage = mid_w * cover + next_w * cover + prev_w * cover
    residual_ext = (measured_ext - projection) / jnp.maximum(coverage, 1.0)
    global_rows = first_row - 1 + jnp.arange(ext_rows, dtype=jnp.int32)
    valid = (global_rows >= 0) & (global_rows < total_rows)
    residual_ext = jnp.where(valid[None, :, None], residual_ext, 0.0)
    residual = residual_ext[:, 1 : slab_rows + 1]

    back_rows = (
        axial_weight[0][:, :, None] * residual_ext[:, 0:slab_rows]
        + axial_weight[1][:, :, None] * residual
        + axial_weight[2][:, :, None] * residual_ext[:, 2 : slab_rows + 2]
    )
    back_full = all_gather_xy(back_rows, xy_count)
    back_band = jnp.stack(
        [
            lax.dynamic_slice(back_full[v], (jnp.int32(0), band_start[v, 0]), (slab_rows, B))
            for v in range(view_count)
        ]
    )

    own_rows = first_row + jnp.arange(slab_rows, dtype=jnp.int32)
    row_weight = (
        jnp.where(own_rows[None, :] > 0, axial_weight[0], 0.0)
        + axial_weight[1]
        + jnp.where(own_rows[None, :] < total_rows - 1, axial_weight[2], 0.0)
    )
    volume_next = backward_update(back_band, volume, amplitude, column_offset, column_width, row_weight)
    return (volume_next, residual)


def solution(mesh):
    return jax.shard_map(
        local,
        mesh=mesh,
        in_specs=(
            P("gz", "xy"),
            P(None, "gz", "xy"),
            P(None, "xy"),
            P(None, "xy"),
            P(None, "xy"),
            P(None, "xy"),
            P(None, None, "gz"),
        ),
        out_specs=(P("gz", "xy"), P(None, "gz", "xy")),
        check_vma=False,
    )
```

```python
import jax
import jax.numpy as jnp
from jax import lax
from jax.experimental import pallas as pl
from jax.experimental.pallas import tpu as pltpu
from jax.sharding import PartitionSpec as P

B = 512
RELAX = 0.9
CHUNK = 512
INTERPRET = False


def _band_mask(off, wid, rows, width):
    u = lax.broadcasted_iota(jnp.int32, (rows, width), 0)
    inside = (u >= off) & (u < off + wid)
    return jnp.where(inside, 1.0, 0.0).astype(jnp.bfloat16)


def _split(x):
    hi = x.astype(jnp.bfloat16)
    lo = (x - hi.astype(jnp.float32)).astype(jnp.bfloat16)
    return hi, lo


def _forward_kernel(vol_ref, amp_ref, off_ref, wid_ref, out_ref):
    slab_rows, columns = vol_ref.shape
    view_count = amp_ref.shape[0]
    band = out_ref.shape[2]
    out_ref[...] = jnp.zeros(out_ref.shape, jnp.float32)
    row = lax.broadcasted_iota(jnp.int32, (slab_rows, CHUNK), 0)

    def body(j, carry):
        c0 = pl.multiple_of(j * CHUNK, CHUNK)
        cells = vol_ref[:, pl.ds(c0, CHUNK)]
        for v in range(view_count):
            amp = amp_ref[pl.ds(v, 1), pl.ds(c0, CHUNK)]
            off = off_ref[pl.ds(v, 1), pl.ds(c0, CHUNK)]
            wid = wid_ref[pl.ds(v, 1), pl.ds(c0, CHUNK)]
            x = jnp.concatenate([cells * amp, jnp.where(row == 0, amp, 0.0)], axis=0)
            hi, lo = _split(x)
            lhs = jnp.concatenate([hi, lo], axis=0)
            mask = _band_mask(off, wid, band, CHUNK)
            out_ref[v] += lax.dot_general(
                lhs, mask, (((1,), (1,)), ((), ())), preferred_element_type=jnp.float32
            )
        return carry

    lax.fori_loop(0, columns // CHUNK, body, 0)


def forward_band(volume, amplitude, column_offset, column_width):
    slab_rows = volume.shape[0]
    view_count = amplitude.shape[0]
    acc = pl.pallas_call(
        _forward_kernel,
        out_shape=jax.ShapeDtypeStruct((view_count, 4 * slab_rows, B), jnp.float32),
        interpret=INTERPRET,
    )(volume, amplitude, column_offset, column_width)
    summed = acc[:, : 2 * slab_rows] + acc[:, 2 * slab_rows :]
    return summed[:, : slab_rows + 1]


def _backward_kernel(back_ref, vol_ref, amp_ref, off_ref, wid_ref, rw_ref, out_ref, split_ref):
    slab_rows, columns = vol_ref.shape
    view_count, _, band = back_ref.shape
    for v in range(view_count):
        hi, lo = _split(back_ref[v])
        split_ref[v] = jnp.concatenate([hi, lo], axis=0)

    def body(j, carry):
        c0 = pl.multiple_of(j * CHUNK, CHUNK)
        correction = None
        normalizer = None
        for v in range(view_count):
            amp = amp_ref[pl.ds(v, 1), pl.ds(c0, CHUNK)]
            off = off_ref[pl.ds(v, 1), pl.ds(c0, CHUNK)]
            wid = wid_ref[pl.ds(v, 1), pl.ds(c0, CHUNK)]
            mask = _band_mask(off, wid, band, CHUNK)
            r = jnp.dot(split_ref[v], mask, preferred_element_type=jnp.float32)
            part = amp * (r[:slab_rows] + r[slab_rows:])
            mass = rw_ref[v] * (amp * wid.astype(jnp.float32))
            correction = part if correction is None else correction + part
            normalizer = mass if normalizer is None else normalizer + mass
        cells = vol_ref[:, pl.ds(c0, CHUNK)]
        out_ref[:, pl.ds(c0, CHUNK)] = cells + RELAX * correction / normalizer
        return carry

    lax.fori_loop(0, columns // CHUNK, body, 0)


def backward_update(back_band, volume, amplitude, column_offset, column_width, row_weight):
    view_count, slab_rows, band = back_band.shape
    return pl.pallas_call(
        _backward_kernel,
        out_shape=jax.ShapeDtypeStruct(volume.shape, jnp.float32),
        scratch_shapes=[pltpu.VMEM((view_count, 2 * slab_rows, band), jnp.bfloat16)],
        interpret=INTERPRET,
    )(back_band, volume, amplitude, column_offset, column_width, row_weight[:, :, None])


def _bit_count(count):
    bits = count.bit_length() - 1
    assert 1 << bits == count
    return bits


def reduce_scatter_xy(x, count):
    rows = x.shape[0]
    width = x.shape[1] // count
    bits = _bit_count(count)
    idx = lax.axis_index("xy")
    y = jnp.transpose(x.reshape(rows, count, width), (1, 0, 2)).reshape((2,) * bits + (rows, width))
    for j in range(bits):
        axis = bits - 1 - j
        bit = (idx >> j) & 1
        keep = lax.dynamic_index_in_dim(y, bit, axis, keepdims=False)
        send = lax.dynamic_index_in_dim(y, 1 - bit, axis, keepdims=False)
        y = keep + lax.ppermute(send, "xy", [(i, i ^ (1 << j)) for i in range(count)])
    return y


def all_gather_xy(x, count):
    rows, width = x.shape
    bits = _bit_count(count)
    idx = lax.axis_index("xy")
    y = x
    for step, j in enumerate(reversed(range(bits))):
        bit = (idx >> j) & 1
        other = lax.ppermute(y, "xy", [(i, i ^ (1 << j)) for i in range(count)])
        low = jnp.where(bit == 0, y, other)
        high = jnp.where(bit == 0, other, y)
        y = jnp.stack([low, high], axis=step)
    return jnp.transpose(y.reshape(count, rows, width), (1, 0, 2)).reshape(rows, count * width)


def local(volume, measured, band_start, column_offset, column_width, amplitude, axial_weight):
    slab_rows = volume.shape[0]
    view_count = amplitude.shape[0]
    xy_count = lax.axis_size("xy")
    gz_count = lax.axis_size("gz")
    shard_width = measured.shape[2]
    detector_width = shard_width * xy_count
    total_rows = slab_rows * gz_count
    first_row = lax.axis_index("gz") * slab_rows
    up_pairs = [(i, i + 1) for i in range(gz_count - 1)]
    down_pairs = [(i + 1, i) for i in range(gz_count - 1)]

    def pack(meas_rows, weight_cols):
        flat = jnp.transpose(weight_cols, (1, 0, 2)).reshape(view_count, 1, -1)
        flat = jnp.pad(flat, ((0, 0), (0, 0), (0, shard_width - flat.shape[2])))
        return jnp.concatenate([meas_rows, flat], axis=1)

    def unpack(packed):
        cols = packed[:, 1, : 3 * 2].reshape(view_count, 3, 2)
        return packed[:, :1], jnp.transpose(cols, (1, 0, 2))

    from_below = lax.ppermute(
        pack(measured[:, slab_rows - 1 :], axial_weight[:, :, slab_rows - 2 :]), "gz", up_pairs
    )
    from_above = lax.ppermute(pack(measured[:, :1], axial_weight[:, :, :2]), "gz", down_pairs)
    meas_below, weight_below = unpack(from_below)
    meas_above, weight_above = unpack(from_above)
    measured_ext = jnp.concatenate([meas_below, measured, meas_above], axis=1)
    weight_ext = jnp.concatenate([weight_below, axial_weight, weight_above], axis=2)

    band_rows = forward_band(volume, amplitude, column_offset, column_width)
    band_height = slab_rows + 1
    placed = jnp.zeros((view_count * band_height, detector_width), jnp.float32)
    for v in range(view_count):
        placed = lax.dynamic_update_slice(placed, band_rows[v], (jnp.int32(v * band_height), band_start[v, 0]))
    reduced = reduce_scatter_xy(placed, xy_count).reshape(view_count, band_height, shard_width)
    proj_cols = reduced[:, :slab_rows]
    cover = reduced[:, slab_rows : slab_rows + 1]
    proj_ext = jnp.concatenate(
        [
            lax.ppermute(proj_cols[:, slab_rows - 2 :], "gz", up_pairs),
            proj_cols,
            lax.ppermute(proj_cols[:, :2], "gz", down_pairs),
        ],
        axis=1,
    )

    ext_rows = slab_rows + 2
    mid_w = weight_ext[1, :, 1 : ext_rows + 1][:, :, None]
    next_w = weight_ext[0, :, 2 : ext_rows + 2][:, :, None]
    prev_w = weight_ext[2, :, 0:ext_rows][:, :, None]
    centre = proj_ext[:, 1 : ext_rows + 1]
    after = proj_ext[:, 2 : ext_rows + 2]
    before = proj_ext[:, 0:ext_rows]
    projection = mid_w * centre + next_w * after + prev_w * before
    coverage = mid_w * cover + next_w * cover + prev_w * cover
    residual_ext = (measured_ext - projection) / jnp.maximum(coverage, 1.0)
    global_rows = first_row - 1 + jnp.arange(ext_rows, dtype=jnp.int32)
    valid = (global_rows >= 0) & (global_rows < total_rows)
    residual_ext = jnp.where(valid[None, :, None], residual_ext, 0.0)
    residual = residual_ext[:, 1 : slab_rows + 1]

    back_rows = (
        axial_weight[0][:, :, None] * residual_ext[:, 0:slab_rows]
        + axial_weight[1][:, :, None] * residual
        + axial_weight[2][:, :, None] * residual_ext[:, 2 : slab_rows + 2]
    )
    back_full = all_gather_xy(back_rows.reshape(view_count * slab_rows, shard_width), xy_count)
    back_full = back_full.reshape(view_count, slab_rows, detector_width)
    back_band = jnp.stack(
        [
            lax.dynamic_slice(back_full[v], (jnp.int32(0), band_start[v, 0]), (slab_rows, B))
            for v in range(view_count)
        ]
    )

    own_rows = first_row + jnp.arange(slab_rows, dtype=jnp.int32)
    row_weight = (
        jnp.where(own_rows[None, :] > 0, axial_weight[0], 0.0)
        + axial_weight[1]
        + jnp.where(own_rows[None, :] < total_rows - 1, axial_weight[2], 0.0)
    )
    volume_next = backward_update(back_band, volume, amplitude, column_offset, column_width, row_weight)
    return (volume_next, residual)


def solution(mesh):
    return jax.shard_map(
        local,
        mesh=mesh,
        in_specs=(
            P("gz", "xy"),
            P(None, "gz", "xy"),
            P(None, "xy"),
            P(None, "xy"),
            P(None, "xy"),
            P(None, "xy"),
            P(None, None, "gz"),
        ),
        out_specs=(P("gz", "xy"), P(None, "gz", "xy")),
        check_vma=False,
    )
```

```python
import jax
import jax.numpy as jnp
from jax import lax
from jax.experimental import pallas as pl
from jax.experimental.pallas import tpu as pltpu
from jax.sharding import PartitionSpec as P

B = 512
RELAX = 0.9
CHUNK = 512
INTERPRET = False


def _band_mask(off, wid, rows, width):
    u = lax.broadcasted_iota(jnp.int32, (rows, width), 0)
    inside = (u >= off) & (u < off + wid)
    return jnp.where(inside, 1.0, 0.0).astype(jnp.bfloat16)


def _split(x):
    hi = x.astype(jnp.bfloat16)
    lo = (x - hi.astype(jnp.float32)).astype(jnp.bfloat16)
    return hi, lo


def _forward_kernel(vol_ref, amp_ref, off_ref, wid_ref, out_ref):
    slab_rows, columns = vol_ref.shape
    view_count = amp_ref.shape[0]
    band = out_ref.shape[2]
    out_ref[...] = jnp.zeros(out_ref.shape, jnp.float32)
    row = lax.broadcasted_iota(jnp.int32, (slab_rows, CHUNK), 0)

    def body(j, carry):
        c0 = pl.multiple_of(j * CHUNK, CHUNK)
        cells = vol_ref[:, pl.ds(c0, CHUNK)]
        for v in range(view_count):
            amp = amp_ref[pl.ds(v, 1), pl.ds(c0, CHUNK)]
            off = off_ref[pl.ds(v, 1), pl.ds(c0, CHUNK)]
            wid = wid_ref[pl.ds(v, 1), pl.ds(c0, CHUNK)]
            x = jnp.concatenate([cells * amp, jnp.where(row == 0, amp, 0.0)], axis=0)
            hi, lo = _split(x)
            lhs = jnp.concatenate([hi, lo], axis=0)
            mask = _band_mask(off, wid, band, CHUNK)
            out_ref[v] += lax.dot_general(
                lhs, mask, (((1,), (1,)), ((), ())), preferred_element_type=jnp.float32
            )
        return carry

    lax.fori_loop(0, columns // CHUNK, body, 0)


def forward_band(volume, amplitude, column_offset, column_width):
    slab_rows = volume.shape[0]
    view_count = amplitude.shape[0]
    acc = pl.pallas_call(
        _forward_kernel,
        out_shape=jax.ShapeDtypeStruct((view_count, 4 * slab_rows, B), jnp.float32),
        interpret=INTERPRET,
    )(volume, amplitude, column_offset, column_width)
    summed = acc[:, : 2 * slab_rows] + acc[:, 2 * slab_rows :]
    return summed[:, : slab_rows + 1]


def _backward_kernel(back_ref, vol_ref, amp_ref, off_ref, wid_ref, rw_ref, out_ref, split_ref):
    slab_rows, columns = vol_ref.shape
    view_count, _, band = back_ref.shape
    for v in range(view_count):
        hi, lo = _split(back_ref[v])
        split_ref[v] = jnp.concatenate([hi, lo], axis=0)

    def body(j, carry):
        c0 = pl.multiple_of(j * CHUNK, CHUNK)
        correction = None
        normalizer = None
        for v in range(view_count):
            amp = amp_ref[pl.ds(v, 1), pl.ds(c0, CHUNK)]
            off = off_ref[pl.ds(v, 1), pl.ds(c0, CHUNK)]
            wid = wid_ref[pl.ds(v, 1), pl.ds(c0, CHUNK)]
            mask = _band_mask(off, wid, band, CHUNK)
            r = jnp.dot(split_ref[v], mask, preferred_element_type=jnp.float32)
            part = amp * (r[:slab_rows] + r[slab_rows:])
            mass = rw_ref[v] * (amp * wid.astype(jnp.float32))
            correction = part if correction is None else correction + part
            normalizer = mass if normalizer is None else normalizer + mass
        cells = vol_ref[:, pl.ds(c0, CHUNK)]
        out_ref[:, pl.ds(c0, CHUNK)] = cells + RELAX * correction / normalizer
        return carry

    lax.fori_loop(0, columns // CHUNK, body, 0)


def backward_update(back_band, volume, amplitude, column_offset, column_width, row_weight):
    view_count, slab_rows, band = back_band.shape
    return pl.pallas_call(
        _backward_kernel,
        out_shape=jax.ShapeDtypeStruct(volume.shape, jnp.float32),
        scratch_shapes=[pltpu.VMEM((view_count, 2 * slab_rows, band), jnp.bfloat16)],
        interpret=INTERPRET,
    )(back_band, volume, amplitude, column_offset, column_width, row_weight[:, :, None])


def _bit_count(count):
    bits = count.bit_length() - 1
    assert 1 << bits == count
    return bits


def all_gather_tiles(x, count):
    rows, width = x.shape
    bits = _bit_count(count)
    idx = lax.axis_index("xy")
    y = x
    for step, j in enumerate(reversed(range(bits))):
        bit = (idx >> j) & 1
        other = lax.ppermute(y, "xy", [(i, i ^ (1 << j)) for i in range(count)])
        low = jnp.where(bit == 0, y, other)
        high = jnp.where(bit == 0, other, y)
        y = jnp.stack([low, high], axis=step)
    return y.reshape(count, rows, width)


def window_sum(bands, starts, positions, width):
    tiles, views, rows, band = bands.shape
    padded = jnp.pad(bands, ((0, 0), (0, 0), (0, 0), (width, width)))
    out = []
    for v in range(views):
        total = None
        for t in range(tiles):
            shift = jnp.clip(positions[v] - starts[t, v] + width, 0, band + width)
            piece = lax.dynamic_slice(padded[t, v], (jnp.int32(0), shift), (rows, width))
            total = piece if total is None else total + piece
        out.append(total)
    return jnp.stack(out)


def local(volume, measured, band_start, column_offset, column_width, amplitude, axial_weight):
    slab_rows = volume.shape[0]
    view_count = amplitude.shape[0]
    xy_count = lax.axis_size("xy")
    gz_count = lax.axis_size("gz")
    shard_width = measured.shape[2]
    detector_width = shard_width * xy_count
    total_rows = slab_rows * gz_count
    first_row = lax.axis_index("gz") * slab_rows
    up_pairs = [(i, i + 1) for i in range(gz_count - 1)]
    down_pairs = [(i + 1, i) for i in range(gz_count - 1)]
    ext_rows = slab_rows + 2

    def pack(meas_rows, weight_cols):
        flat = jnp.transpose(weight_cols, (1, 0, 2)).reshape(view_count, 1, -1)
        flat = jnp.pad(flat, ((0, 0), (0, 0), (0, shard_width - flat.shape[2])))
        return jnp.concatenate([meas_rows, flat], axis=1)

    def unpack(packed):
        cols = packed[:, 1, : 3 * 2].reshape(view_count, 3, 2)
        return packed[:, :1], jnp.transpose(cols, (1, 0, 2))

    from_below = lax.ppermute(
        pack(measured[:, slab_rows - 1 :], axial_weight[:, :, slab_rows - 2 :]), "gz", up_pairs
    )
    from_above = lax.ppermute(pack(measured[:, :1], axial_weight[:, :, :2]), "gz", down_pairs)
    meas_below, weight_below = unpack(from_below)
    meas_above, weight_above = unpack(from_above)
    measured_ext = jnp.concatenate([meas_below, measured, meas_above], axis=1)
    weight_ext = jnp.concatenate([weight_below, axial_weight, weight_above], axis=2)
    meas_tiles = all_gather_tiles(measured_ext.reshape(view_count * ext_rows, shard_width), xy_count)
    meas_full = jnp.transpose(meas_tiles, (1, 0, 2)).reshape(view_count, ext_rows, detector_width)

    band_rows = forward_band(volume, amplitude, column_offset, column_width)
    band_height = slab_rows + 1
    start_row = jnp.pad(band_start[:, 0].astype(jnp.float32), (0, B - view_count))[None]
    payload = jnp.concatenate([band_rows.reshape(view_count * band_height, B), start_row], axis=0)
    gathered = all_gather_tiles(payload, xy_count)
    starts = gathered[:, view_count * band_height, :view_count].astype(jnp.int32)
    bands = gathered[:, : view_count * band_height].reshape(xy_count, view_count, band_height, B)
    my_start = [band_start[v, 0] for v in range(view_count)]
    shard_pos = lax.axis_index("xy") * shard_width
    band_win = window_sum(bands, starts, my_start, B)
    shard_win = window_sum(bands, starts, [shard_pos] * view_count, shard_width)

    edge_up = jnp.concatenate([band_win[:, slab_rows - 2 : slab_rows], shard_win[:, slab_rows - 2 : slab_rows]], axis=2)
    edge_down = jnp.concatenate([band_win[:, :2], shard_win[:, :2]], axis=2)
    halo_below = lax.ppermute(edge_up, "gz", up_pairs)
    halo_above = lax.ppermute(edge_down, "gz", down_pairs)

    mid_w = weight_ext[1, :, 1 : ext_rows + 1][:, :, None]
    next_w = weight_ext[0, :, 2 : ext_rows + 2][:, :, None]
    prev_w = weight_ext[2, :, 0:ext_rows][:, :, None]
    global_rows = first_row - 1 + jnp.arange(ext_rows, dtype=jnp.int32)
    valid = (global_rows >= 0) & (global_rows < total_rows)

    def residual_rows(win, lo, hi, meas_ext):
        proj_ext = jnp.concatenate(
            [halo_below[:, :, lo:hi], win[:, :slab_rows], halo_above[:, :, lo:hi]], axis=1
        )
        cover = win[:, slab_rows : slab_rows + 1]
        centre = proj_ext[:, 1 : ext_rows + 1]
        after = proj_ext[:, 2 : ext_rows + 2]
        before = proj_ext[:, 0:ext_rows]
        projection = mid_w * centre + next_w * after + prev_w * before
        coverage = mid_w * cover + next_w * cover + prev_w * cover
        res = (meas_ext - projection) / jnp.maximum(coverage, 1.0)
        return jnp.where(valid[None, :, None], res, 0.0)

    residual = residual_rows(shard_win, B, B + shard_width, measured_ext)[:, 1 : slab_rows + 1]
    meas_band = jnp.stack(
        [lax.dynamic_slice(meas_full[v], (jnp.int32(0), my_start[v]), (ext_rows, B)) for v in range(view_count)]
    )
    res_band = residual_rows(band_win, 0, B, meas_band)
    back_band = (
        axial_weight[0][:, :, None] * res_band[:, 0:slab_rows]
        + axial_weight[1][:, :, None] * res_band[:, 1 : slab_rows + 1]
        + axial_weight[2][:, :, None] * res_band[:, 2 : slab_rows + 2]
    )

    own_rows = first_row + jnp.arange(slab_rows, dtype=jnp.int32)
    row_weight = (
        jnp.where(own_rows[None, :] > 0, axial_weight[0], 0.0)
        + axial_weight[1]
        + jnp.where(own_rows[None, :] < total_rows - 1, axial_weight[2], 0.0)
    )
    volume_next = backward_update(back_band, volume, amplitude, column_offset, column_width, row_weight)
    return (volume_next, residual)


def solution(mesh):
    return jax.shard_map(
        local,
        mesh=mesh,
        in_specs=(
            P("gz", "xy"),
            P(None, "gz", "xy"),
            P(None, "xy"),
            P(None, "xy"),
            P(None, "xy"),
            P(None, "xy"),
            P(None, None, "gz"),
        ),
        out_specs=(P("gz", "xy"), P(None, "gz", "xy")),
        check_vma=False,
    )
```

```python
import jax
import jax.numpy as jnp
from jax import lax
from jax.experimental import pallas as pl
from jax.experimental.pallas import tpu as pltpu
from jax.sharding import PartitionSpec as P

B = 512
RELAX = 0.9
CHUNK = 512
INTERPRET = False


def _band_mask(off, wid, rows, width):
    u = lax.broadcasted_iota(jnp.int32, (rows, width), 0)
    inside = (u >= off) & (u < off + wid)
    return jnp.where(inside, 1.0, 0.0).astype(jnp.bfloat16)


def _split(x):
    hi = x.astype(jnp.bfloat16)
    lo = (x - hi.astype(jnp.float32)).astype(jnp.bfloat16)
    return hi, lo


def _forward_kernel(vol_ref, amp_ref, off_ref, wid_ref, out_ref):
    slab_rows, columns = vol_ref.shape
    view_count = amp_ref.shape[0]
    band = out_ref.shape[2]
    out_ref[...] = jnp.zeros(out_ref.shape, jnp.float32)
    row = lax.broadcasted_iota(jnp.int32, (slab_rows, CHUNK), 0)

    def body(j, carry):
        c0 = pl.multiple_of(j * CHUNK, CHUNK)
        cells = vol_ref[:, pl.ds(c0, CHUNK)]
        for v in range(view_count):
            amp = amp_ref[pl.ds(v, 1), pl.ds(c0, CHUNK)]
            off = off_ref[pl.ds(v, 1), pl.ds(c0, CHUNK)]
            wid = wid_ref[pl.ds(v, 1), pl.ds(c0, CHUNK)]
            x = jnp.concatenate([cells * amp, jnp.where(row == 0, amp, 0.0)], axis=0)
            hi, lo = _split(x)
            lhs = jnp.concatenate([hi, lo], axis=0)
            mask = _band_mask(off, wid, band, CHUNK)
            out_ref[v] += lax.dot_general(
                lhs, mask, (((1,), (1,)), ((), ())), preferred_element_type=jnp.float32
            )
        return carry

    lax.fori_loop(0, columns // CHUNK, body, 0)


def forward_band(volume, amplitude, column_offset, column_width):
    slab_rows = volume.shape[0]
    view_count = amplitude.shape[0]
    acc = pl.pallas_call(
        _forward_kernel,
        out_shape=jax.ShapeDtypeStruct((view_count, 4 * slab_rows, B), jnp.float32),
        cost_estimate=pl.CostEstimate(
            flops=2 * view_count * 4 * slab_rows * B * volume.shape[1],
            transcendentals=0,
            bytes_accessed=4 * (volume.size + 3 * amplitude.size),
        ),
        interpret=INTERPRET,
    )(volume, amplitude, column_offset, column_width)
    summed = acc[:, : 2 * slab_rows] + acc[:, 2 * slab_rows :]
    return summed[:, : slab_rows + 1]


def _backward_kernel(back_ref, vol_ref, amp_ref, off_ref, wid_ref, rw_ref, out_ref, split_ref):
    slab_rows, columns = vol_ref.shape
    view_count, _, band = back_ref.shape
    for v in range(view_count):
        hi, lo = _split(back_ref[v])
        split_ref[v] = jnp.concatenate([hi, lo], axis=0)

    def body(j, carry):
        c0 = pl.multiple_of(j * CHUNK, CHUNK)
        correction = None
        normalizer = None
        for v in range(view_count):
            amp = amp_ref[pl.ds(v, 1), pl.ds(c0, CHUNK)]
            off = off_ref[pl.ds(v, 1), pl.ds(c0, CHUNK)]
            wid = wid_ref[pl.ds(v, 1), pl.ds(c0, CHUNK)]
            mask = _band_mask(off, wid, band, CHUNK)
            r = jnp.dot(split_ref[v], mask, preferred_element_type=jnp.float32)
            part = amp * (r[:slab_rows] + r[slab_rows:])
            mass = rw_ref[v] * (amp * wid.astype(jnp.float32))
            correction = part if correction is None else correction + part
            normalizer = mass if normalizer is None else normalizer + mass
        cells = vol_ref[:, pl.ds(c0, CHUNK)]
        out_ref[:, pl.ds(c0, CHUNK)] = cells + RELAX * correction / normalizer
        return carry

    lax.fori_loop(0, columns // CHUNK, body, 0)


def backward_update(back_band, volume, amplitude, column_offset, column_width, row_weight):
    view_count, slab_rows, band = back_band.shape
    return pl.pallas_call(
        _backward_kernel,
        out_shape=jax.ShapeDtypeStruct(volume.shape, jnp.float32),
        scratch_shapes=[pltpu.VMEM((view_count, 2 * slab_rows, band), jnp.bfloat16)],
        cost_estimate=pl.CostEstimate(
            flops=2 * view_count * 2 * slab_rows * band * volume.shape[1],
            transcendentals=0,
            bytes_accessed=4 * (2 * volume.size + 3 * amplitude.size),
        ),
        interpret=INTERPRET,
    )(back_band, volume, amplitude, column_offset, column_width, row_weight[:, :, None])


def _bit_count(count):
    bits = count.bit_length() - 1
    assert 1 << bits == count
    return bits


def all_gather_tiles(x, count):
    rows, width = x.shape
    bits = _bit_count(count)
    idx = lax.axis_index("xy")
    y = x
    for step, j in enumerate(reversed(range(bits))):
        bit = (idx >> j) & 1
        other = lax.ppermute(y, "xy", [(i, i ^ (1 << j)) for i in range(count)])
        low = jnp.where(bit == 0, y, other)
        high = jnp.where(bit == 0, other, y)
        y = jnp.stack([low, high], axis=step)
    return y.reshape(count, rows, width)


def _window_kernel(starts_ref, spots_ref, bands_ref, band_out, shard_out):
    tiles, views, rows, band = bands_ref.shape
    for out_ref, slot in ((band_out, 0), (shard_out, 1)):
        width = out_ref.shape[2]
        length = band + 2 * width
        gap = jnp.zeros((rows, width), jnp.float32)
        for v in range(views):
            spot = spots_ref[slot, v]
            total = None
            for t in range(tiles):
                shift = jnp.clip(spot - starts_ref[t, v] + width, 0, band + width)
                ext = jnp.concatenate([gap, bands_ref[t, v], gap], axis=1)
                rolled = pltpu.roll(ext, (length - shift) % length, 1)
                piece = rolled[:, :width]
                total = piece if total is None else total + piece
            out_ref[v] = total


def window_sums(bands, starts, band_spots, shard_spot, shard_width):
    tiles, views, rows, band = bands.shape
    spots = jnp.stack([jnp.stack(band_spots), jnp.stack([shard_spot] * views)]).astype(jnp.int32)
    smem = pl.BlockSpec(memory_space=pltpu.SMEM)
    return pl.pallas_call(
        _window_kernel,
        out_shape=(
            jax.ShapeDtypeStruct((views, rows, band), jnp.float32),
            jax.ShapeDtypeStruct((views, rows, shard_width), jnp.float32),
        ),
        in_specs=[smem, smem, pl.BlockSpec(memory_space=pltpu.VMEM)],
        interpret=INTERPRET,
    )(starts, spots, bands)


def local(volume, measured, band_start, column_offset, column_width, amplitude, axial_weight):
    slab_rows = volume.shape[0]
    view_count = amplitude.shape[0]
    xy_count = lax.axis_size("xy")
    gz_count = lax.axis_size("gz")
    shard_width = measured.shape[2]
    detector_width = shard_width * xy_count
    total_rows = slab_rows * gz_count
    first_row = lax.axis_index("gz") * slab_rows
    up_pairs = [(i, i + 1) for i in range(gz_count - 1)]
    down_pairs = [(i + 1, i) for i in range(gz_count - 1)]
    ext_rows = slab_rows + 2

    def pack(meas_rows, weight_cols):
        flat = jnp.transpose(weight_cols, (1, 0, 2)).reshape(view_count, 1, -1)
        flat = jnp.pad(flat, ((0, 0), (0, 0), (0, shard_width - flat.shape[2])))
        return jnp.concatenate([meas_rows, flat], axis=1)

    def unpack(packed):
        cols = packed[:, 1, : 3 * 2].reshape(view_count, 3, 2)
        return packed[:, :1], jnp.transpose(cols, (1, 0, 2))

    from_below = lax.ppermute(
        pack(measured[:, slab_rows - 1 :], axial_weight[:, :, slab_rows - 2 :]), "gz", up_pairs
    )
    from_above = lax.ppermute(pack(measured[:, :1], axial_weight[:, :, :2]), "gz", down_pairs)
    meas_below, weight_below = unpack(from_below)
    meas_above, weight_above = unpack(from_above)
    measured_ext = jnp.concatenate([meas_below, measured, meas_above], axis=1)
    weight_ext = jnp.concatenate([weight_below, axial_weight, weight_above], axis=2)
    meas_tiles = all_gather_tiles(measured_ext.reshape(view_count * ext_rows, shard_width), xy_count)
    meas_full = jnp.transpose(meas_tiles, (1, 0, 2)).reshape(view_count, ext_rows, detector_width)

    band_rows = forward_band(volume, amplitude, column_offset, column_width)
    band_height = slab_rows + 1
    start_row = jnp.pad(band_start[:, 0].astype(jnp.float32), (0, B - view_count))[None]
    payload = jnp.concatenate([band_rows.reshape(view_count * band_height, B), start_row], axis=0)
    gathered = all_gather_tiles(payload, xy_count)
    starts = gathered[:, view_count * band_height, :view_count].astype(jnp.int32)
    bands = gathered[:, : view_count * band_height].reshape(xy_count, view_count, band_height, B)
    my_start = [band_start[v, 0] for v in range(view_count)]
    shard_pos = lax.axis_index("xy") * shard_width
    band_win, shard_win = window_sums(bands, starts, my_start, shard_pos, shard_width)

    edge_up = jnp.concatenate([band_win[:, slab_rows - 2 : slab_rows], shard_win[:, slab_rows - 2 : slab_rows]], axis=2)
    edge_down = jnp.concatenate([band_win[:, :2], shard_win[:, :2]], axis=2)
    halo_below = lax.ppermute(edge_up, "gz", up_pairs)
    halo_above = lax.ppermute(edge_down, "gz", down_pairs)

    mid_w = weight_ext[1, :, 1 : ext_rows + 1][:, :, None]
    next_w = weight_ext[0, :, 2 : ext_rows + 2][:, :, None]
    prev_w = weight_ext[2, :, 0:ext_rows][:, :, None]
    global_rows = first_row - 1 + jnp.arange(ext_rows, dtype=jnp.int32)
    valid = (global_rows >= 0) & (global_rows < total_rows)

    def residual_rows(win, lo, hi, meas_ext):
        proj_ext = jnp.concatenate(
            [halo_below[:, :, lo:hi], win[:, :slab_rows], halo_above[:, :, lo:hi]], axis=1
        )
        cover = win[:, slab_rows : slab_rows + 1]
        centre = proj_ext[:, 1 : ext_rows + 1]
        after = proj_ext[:, 2 : ext_rows + 2]
        before = proj_ext[:, 0:ext_rows]
        projection = mid_w * centre + next_w * after + prev_w * before
        coverage = mid_w * cover + next_w * cover + prev_w * cover
        res = (meas_ext - projection) / jnp.maximum(coverage, 1.0)
        return jnp.where(valid[None, :, None], res, 0.0)

    residual = residual_rows(shard_win, B, B + shard_width, measured_ext)[:, 1 : slab_rows + 1]
    meas_band = jnp.stack(
        [lax.dynamic_slice(meas_full[v], (jnp.int32(0), my_start[v]), (ext_rows, B)) for v in range(view_count)]
    )
    res_band = residual_rows(band_win, 0, B, meas_band)
    back_band = (
        axial_weight[0][:, :, None] * res_band[:, 0:slab_rows]
        + axial_weight[1][:, :, None] * res_band[:, 1 : slab_rows + 1]
        + axial_weight[2][:, :, None] * res_band[:, 2 : slab_rows + 2]
    )

    own_rows = first_row + jnp.arange(slab_rows, dtype=jnp.int32)
    row_weight = (
        jnp.where(own_rows[None, :] > 0, axial_weight[0], 0.0)
        + axial_weight[1]
        + jnp.where(own_rows[None, :] < total_rows - 1, axial_weight[2], 0.0)
    )
    volume_next = backward_update(back_band, volume, amplitude, column_offset, column_width, row_weight)
    return (volume_next, residual)


def solution(mesh):
    return jax.shard_map(
        local,
        mesh=mesh,
        in_specs=(
            P("gz", "xy"),
            P(None, "gz", "xy"),
            P(None, "xy"),
            P(None, "xy"),
            P(None, "xy"),
            P(None, "xy"),
            P(None, None, "gz"),
        ),
        out_specs=(P("gz", "xy"), P(None, "gz", "xy")),
        check_vma=False,
    )
```

```python
import jax
import jax.numpy as jnp
from jax import lax
from jax.experimental import pallas as pl
from jax.experimental.pallas import tpu as pltpu
from jax.sharding import PartitionSpec as P

B = 512
RELAX = 0.9
CHUNK = 512
INTERPRET = False


def _band_mask(off, wid, rows, width):
    u = lax.broadcasted_iota(jnp.int32, (rows, width), 0)
    inside = (u >= off) & (u < off + wid)
    return jnp.where(inside, 1.0, 0.0).astype(jnp.bfloat16)


def _split(x):
    hi = x.astype(jnp.bfloat16)
    lo = (x - hi.astype(jnp.float32)).astype(jnp.bfloat16)
    return hi, lo


def _forward_kernel(vol_ref, amp_ref, off_ref, wid_ref, out_ref):
    slab_rows, columns = vol_ref.shape
    view_count = amp_ref.shape[0]
    band = out_ref.shape[2]
    out_ref[...] = jnp.zeros(out_ref.shape, jnp.float32)
    row = lax.broadcasted_iota(jnp.int32, (slab_rows, CHUNK), 0)

    def body(j, carry):
        c0 = pl.multiple_of(j * CHUNK, CHUNK)
        cells = vol_ref[:, pl.ds(c0, CHUNK)]
        for v in range(view_count):
            amp = amp_ref[pl.ds(v, 1), pl.ds(c0, CHUNK)]
            off = off_ref[pl.ds(v, 1), pl.ds(c0, CHUNK)]
            wid = wid_ref[pl.ds(v, 1), pl.ds(c0, CHUNK)]
            x = jnp.concatenate([cells * amp, jnp.where(row == 0, amp, 0.0)], axis=0)
            hi, lo = _split(x)
            lhs = jnp.concatenate([hi, lo], axis=0)
            mask = _band_mask(off, wid, band, CHUNK)
            out_ref[v] += lax.dot_general(
                lhs, mask, (((1,), (1,)), ((), ())), preferred_element_type=jnp.float32
            )
        return carry

    lax.fori_loop(0, columns // CHUNK, body, 0)


def forward_band(volume, amplitude, column_offset, column_width):
    slab_rows = volume.shape[0]
    view_count = amplitude.shape[0]
    acc = pl.pallas_call(
        _forward_kernel,
        out_shape=jax.ShapeDtypeStruct((view_count, 4 * slab_rows, B), jnp.float32),
        cost_estimate=pl.CostEstimate(
            flops=2 * view_count * 4 * slab_rows * B * volume.shape[1],
            transcendentals=0,
            bytes_accessed=4 * (volume.size + 3 * amplitude.size),
        ),
        interpret=INTERPRET,
    )(volume, amplitude, column_offset, column_width)
    summed = acc[:, : 2 * slab_rows] + acc[:, 2 * slab_rows :]
    return summed[:, : slab_rows + 1]


def _backward_kernel(back_ref, vol_ref, amp_ref, off_ref, wid_ref, rw_ref, out_ref, split_ref):
    slab_rows, columns = vol_ref.shape
    view_count, _, band = back_ref.shape
    for v in range(view_count):
        hi, lo = _split(back_ref[v])
        split_ref[v] = jnp.concatenate([hi, lo], axis=0)

    def body(j, carry):
        c0 = pl.multiple_of(j * CHUNK, CHUNK)
        correction = None
        normalizer = None
        for v in range(view_count):
            amp = amp_ref[pl.ds(v, 1), pl.ds(c0, CHUNK)]
            off = off_ref[pl.ds(v, 1), pl.ds(c0, CHUNK)]
            wid = wid_ref[pl.ds(v, 1), pl.ds(c0, CHUNK)]
            mask = _band_mask(off, wid, band, CHUNK)
            r = jnp.dot(split_ref[v], mask, preferred_element_type=jnp.float32)
            part = amp * (r[:slab_rows] + r[slab_rows:])
            mass = rw_ref[v] * (amp * wid.astype(jnp.float32))
            correction = part if correction is None else correction + part
            normalizer = mass if normalizer is None else normalizer + mass
        cells = vol_ref[:, pl.ds(c0, CHUNK)]
        out_ref[:, pl.ds(c0, CHUNK)] = cells + RELAX * correction / normalizer
        return carry

    lax.fori_loop(0, columns // CHUNK, body, 0)


def backward_update(back_band, volume, amplitude, column_offset, column_width, row_weight):
    view_count, slab_rows, band = back_band.shape
    return pl.pallas_call(
        _backward_kernel,
        out_shape=jax.ShapeDtypeStruct(volume.shape, jnp.float32),
        scratch_shapes=[pltpu.VMEM((view_count, 2 * slab_rows, band), jnp.bfloat16)],
        cost_estimate=pl.CostEstimate(
            flops=2 * view_count * 2 * slab_rows * band * volume.shape[1],
            transcendentals=0,
            bytes_accessed=4 * (2 * volume.size + 3 * amplitude.size),
        ),
        interpret=INTERPRET,
    )(back_band, volume, amplitude, column_offset, column_width, row_weight[:, :, None])


def _bit_count(count):
    bits = count.bit_length() - 1
    assert 1 << bits == count
    return bits


def all_gather_tiles(x, count):
    rows, width = x.shape
    bits = _bit_count(count)
    idx = lax.axis_index("xy")
    y = x
    for step, j in enumerate(reversed(range(bits))):
        bit = (idx >> j) & 1
        other = lax.ppermute(y, "xy", [(i, i ^ (1 << j)) for i in range(count)])
        low = jnp.where(bit == 0, y, other)
        high = jnp.where(bit == 0, other, y)
        y = jnp.stack([low, high], axis=step)
    return y.reshape(count, rows, width)


def _window_kernel(starts_ref, spots_ref, bands_ref, band_out, shard_out):
    tiles, views, rows, band = bands_ref.shape
    for out_ref, slot in ((band_out, 0), (shard_out, 1)):
        width = out_ref.shape[2]
        length = band + 2 * width
        gap = jnp.zeros((rows, width), jnp.float32)
        for v in range(views):
            spot = spots_ref[slot, v]
            total = None
            for t in range(tiles):
                shift = jnp.clip(spot - starts_ref[t, v] + width, 0, band + width)
                ext = jnp.concatenate([gap, bands_ref[t, v], gap], axis=1)
                rolled = pltpu.roll(ext, (length - shift) % length, 1)
                piece = rolled[:, :width]
                total = piece if total is None else total + piece
            out_ref[v] = total


def window_sums(bands, starts, band_spots, shard_spot, shard_width):
    tiles, views, rows, band = bands.shape
    spots = jnp.stack([jnp.stack(band_spots), jnp.stack([shard_spot] * views)]).astype(jnp.int32)
    smem = pl.BlockSpec(memory_space=pltpu.SMEM)
    return pl.pallas_call(
        _window_kernel,
        out_shape=(
            jax.ShapeDtypeStruct((views, rows, band), jnp.float32),
            jax.ShapeDtypeStruct((views, rows, shard_width), jnp.float32),
        ),
        in_specs=[smem, smem, pl.BlockSpec(memory_space=pltpu.VMEM)],
        interpret=INTERPRET,
    )(starts, spots, bands)


def local(volume, measured, band_start, column_offset, column_width, amplitude, axial_weight):
    slab_rows = volume.shape[0]
    view_count = amplitude.shape[0]
    xy_count = lax.axis_size("xy")
    gz_count = lax.axis_size("gz")
    shard_width = measured.shape[2]
    detector_width = shard_width * xy_count
    total_rows = slab_rows * gz_count
    first_row = lax.axis_index("gz") * slab_rows
    up_pairs = [(i, i + 1) for i in range(gz_count - 1)]
    down_pairs = [(i + 1, i) for i in range(gz_count - 1)]
    ext_rows = slab_rows + 2
    band_height = slab_rows + 1
    band_part = view_count * band_height
    meas_part = view_count * slab_rows * shard_width // B

    band_rows = forward_band(volume, amplitude, column_offset, column_width)
    start_row = jnp.pad(band_start[:, 0].astype(jnp.float32), (0, B - view_count))[None]
    payload = jnp.concatenate(
        [band_rows.reshape(band_part, B), measured.reshape(meas_part, B), start_row], axis=0
    )
    gathered = all_gather_tiles(payload, xy_count)
    starts = gathered[:, band_part + meas_part, :view_count].astype(jnp.int32)
    bands = gathered[:, :band_part].reshape(xy_count, view_count, band_height, B)
    meas_tiles = gathered[:, band_part : band_part + meas_part].reshape(
        xy_count, view_count, slab_rows, shard_width
    )
    meas_full = jnp.transpose(meas_tiles, (1, 2, 0, 3)).reshape(view_count, slab_rows, detector_width)
    my_start = [band_start[v, 0] for v in range(view_count)]
    shard_pos = lax.axis_index("xy") * shard_width
    band_win, shard_win = window_sums(bands, starts, my_start, shard_pos, shard_width)
    meas_band = jnp.stack(
        [lax.dynamic_slice(meas_full[v], (jnp.int32(0), my_start[v]), (slab_rows, B)) for v in range(view_count)]
    )

    def halo_payload(p_rows, m_row, weight_cols):
        p = jnp.concatenate([band_win[:, p_rows], shard_win[:, p_rows]], axis=2)
        m = jnp.concatenate([meas_band[:, m_row], measured[:, m_row]], axis=2)
        w = jnp.transpose(weight_cols, (1, 0, 2)).reshape(view_count, 1, -1)
        w = jnp.pad(w, ((0, 0), (0, 0), (0, B + shard_width - w.shape[2])))
        return jnp.concatenate([p, m, w], axis=1)

    halo_below = lax.ppermute(
        halo_payload(slice(slab_rows - 2, slab_rows), slice(slab_rows - 1, slab_rows), axial_weight[:, :, slab_rows - 2 :]),
        "gz",
        up_pairs,
    )
    halo_above = lax.ppermute(
        halo_payload(slice(0, 2), slice(0, 1), axial_weight[:, :, :2]), "gz", down_pairs
    )

    def halo_weights(halo):
        return jnp.transpose(halo[:, 3, : 3 * 2].reshape(view_count, 3, 2), (1, 0, 2))

    weight_ext = jnp.concatenate([halo_weights(halo_below), axial_weight, halo_weights(halo_above)], axis=2)
    mid_w = weight_ext[1, :, 1 : ext_rows + 1][:, :, None]
    next_w = weight_ext[0, :, 2 : ext_rows + 2][:, :, None]
    prev_w = weight_ext[2, :, 0:ext_rows][:, :, None]
    global_rows = first_row - 1 + jnp.arange(ext_rows, dtype=jnp.int32)
    valid = (global_rows >= 0) & (global_rows < total_rows)

    def residual_rows(win, meas, lo, hi):
        proj_ext = jnp.concatenate(
            [halo_below[:, 0:2, lo:hi], win[:, :slab_rows], halo_above[:, 0:2, lo:hi]], axis=1
        )
        meas_ext = jnp.concatenate([halo_below[:, 2:3, lo:hi], meas, halo_above[:, 2:3, lo:hi]], axis=1)
        cover = win[:, slab_rows : slab_rows + 1]
        centre = proj_ext[:, 1 : ext_rows + 1]
        after = proj_ext[:, 2 : ext_rows + 2]
        before = proj_ext[:, 0:ext_rows]
        projection = mid_w * centre + next_w * after + prev_w * before
        coverage = mid_w * cover + next_w * cover + prev_w * cover
        res = (meas_ext - projection) / jnp.maximum(coverage, 1.0)
        return jnp.where(valid[None, :, None], res, 0.0)

    residual = residual_rows(shard_win, measured, B, B + shard_width)[:, 1 : slab_rows + 1]
    res_band = residual_rows(band_win, meas_band, 0, B)
    back_band = (
        axial_weight[0][:, :, None] * res_band[:, 0:slab_rows]
        + axial_weight[1][:, :, None] * res_band[:, 1 : slab_rows + 1]
        + axial_weight[2][:, :, None] * res_band[:, 2 : slab_rows + 2]
    )

    own_rows = first_row + jnp.arange(slab_rows, dtype=jnp.int32)
    row_weight = (
        jnp.where(own_rows[None, :] > 0, axial_weight[0], 0.0)
        + axial_weight[1]
        + jnp.where(own_rows[None, :] < total_rows - 1, axial_weight[2], 0.0)
    )
    volume_next = backward_update(back_band, volume, amplitude, column_offset, column_width, row_weight)
    return (volume_next, residual)


def solution(mesh):
    return jax.shard_map(
        local,
        mesh=mesh,
        in_specs=(
            P("gz", "xy"),
            P(None, "gz", "xy"),
            P(None, "xy"),
            P(None, "xy"),
            P(None, "xy"),
            P(None, "xy"),
            P(None, None, "gz"),
        ),
        out_specs=(P("gz", "xy"), P(None, "gz", "xy")),
        check_vma=False,
    )
```

```python
import jax
import jax.numpy as jnp
from jax import lax
from jax.experimental import pallas as pl
from jax.experimental.pallas import tpu as pltpu
from jax.sharding import PartitionSpec as P

B = 512
RELAX = 0.9
CHUNK = 2048
INTERPRET = False


def _band_mask(off, wid, rows, width):
    u = lax.broadcasted_iota(jnp.int32, (rows, width), 0)
    inside = (u - off).astype(jnp.uint32) < wid.astype(jnp.uint32)
    return jnp.where(inside, 1.0, 0.0).astype(jnp.bfloat16)


def _split(x):
    hi = x.astype(jnp.bfloat16)
    lo = (x - hi.astype(jnp.float32)).astype(jnp.bfloat16)
    return hi, lo


def _forward_kernel(vol_ref, amp_ref, off_ref, wid_ref, out_ref):
    slab_rows, columns = vol_ref.shape
    view_count = amp_ref.shape[0]
    band = out_ref.shape[2]
    out_ref[...] = jnp.zeros(out_ref.shape, jnp.float32)
    row = lax.broadcasted_iota(jnp.int32, (slab_rows, CHUNK), 0)

    def body(j, carry):
        c0 = pl.multiple_of(j * CHUNK, CHUNK)
        cells = vol_ref[:, pl.ds(c0, CHUNK)]
        for v in range(view_count):
            amp = amp_ref[pl.ds(v, 1), pl.ds(c0, CHUNK)]
            off = off_ref[pl.ds(v, 1), pl.ds(c0, CHUNK)]
            wid = wid_ref[pl.ds(v, 1), pl.ds(c0, CHUNK)]
            x = jnp.concatenate([cells * amp, jnp.where(row == 0, amp, 0.0)], axis=0)
            hi, lo = _split(x)
            lhs = jnp.concatenate([hi, lo], axis=0)
            mask = _band_mask(off, wid, band, CHUNK)
            out_ref[v] += lax.dot_general(
                lhs, mask, (((1,), (1,)), ((), ())), preferred_element_type=jnp.float32
            )
        return carry

    lax.fori_loop(0, columns // CHUNK, body, 0)


def forward_band(volume, amplitude, column_offset, column_width):
    slab_rows = volume.shape[0]
    view_count = amplitude.shape[0]
    acc = pl.pallas_call(
        _forward_kernel,
        out_shape=jax.ShapeDtypeStruct((view_count, 4 * slab_rows, B), jnp.float32),
        interpret=INTERPRET,
    )(volume, amplitude, column_offset, column_width)
    summed = acc[:, : 2 * slab_rows] + acc[:, 2 * slab_rows :]
    return summed[:, : slab_rows + 1]


def _backward_kernel(back_ref, vol_ref, amp_ref, off_ref, wid_ref, rw_ref, out_ref, split_ref):
    slab_rows, columns = vol_ref.shape
    view_count, _, band = back_ref.shape
    for v in range(view_count):
        hi, lo = _split(back_ref[v])
        split_ref[v] = jnp.concatenate([hi, lo], axis=0)

    def body(j, carry):
        c0 = pl.multiple_of(j * CHUNK, CHUNK)
        correction = None
        normalizer = None
        for v in range(view_count):
            amp = amp_ref[pl.ds(v, 1), pl.ds(c0, CHUNK)]
            off = off_ref[pl.ds(v, 1), pl.ds(c0, CHUNK)]
            wid = wid_ref[pl.ds(v, 1), pl.ds(c0, CHUNK)]
            mask = _band_mask(off, wid, band, CHUNK)
            r = jnp.dot(split_ref[v], mask, preferred_element_type=jnp.float32)
            part = amp * (r[:slab_rows] + r[slab_rows:])
            mass = rw_ref[v] * (amp * wid.astype(jnp.float32))
            correction = part if correction is None else correction + part
            normalizer = mass if normalizer is None else normalizer + mass
        cells = vol_ref[:, pl.ds(c0, CHUNK)]
        out_ref[:, pl.ds(c0, CHUNK)] = cells + RELAX * correction / normalizer
        return carry

    lax.fori_loop(0, columns // CHUNK, body, 0)


def backward_update(back_band, volume, amplitude, column_offset, column_width, row_weight):
    view_count, slab_rows, band = back_band.shape
    return pl.pallas_call(
        _backward_kernel,
        out_shape=jax.ShapeDtypeStruct(volume.shape, jnp.float32),
        scratch_shapes=[pltpu.VMEM((view_count, 2 * slab_rows, band), jnp.bfloat16)],
        interpret=INTERPRET,
    )(back_band, volume, amplitude, column_offset, column_width, row_weight[:, :, None])


def _bit_count(count):
    bits = count.bit_length() - 1
    assert 1 << bits == count
    return bits


def reduce_scatter_xy(x, count):
    rows = x.shape[0]
    width = x.shape[1] // count
    bits = _bit_count(count)
    idx = lax.axis_index("xy")
    y = jnp.transpose(x.reshape(rows, count, width), (1, 0, 2)).reshape((2,) * bits + (rows, width))
    for j in range(bits):
        axis = bits - 1 - j
        bit = (idx >> j) & 1
        keep = lax.dynamic_index_in_dim(y, bit, axis, keepdims=False)
        send = lax.dynamic_index_in_dim(y, 1 - bit, axis, keepdims=False)
        y = keep + lax.ppermute(send, "xy", [(i, i ^ (1 << j)) for i in range(count)])
    return y


def all_gather_xy(x, count):
    rows, width = x.shape
    bits = _bit_count(count)
    idx = lax.axis_index("xy")
    y = x
    for step, j in enumerate(reversed(range(bits))):
        bit = (idx >> j) & 1
        other = lax.ppermute(y, "xy", [(i, i ^ (1 << j)) for i in range(count)])
        low = jnp.where(bit == 0, y, other)
        high = jnp.where(bit == 0, other, y)
        y = jnp.stack([low, high], axis=step)
    return jnp.transpose(y.reshape(count, rows, width), (1, 0, 2)).reshape(rows, count * width)


def local(volume, measured, band_start, column_offset, column_width, amplitude, axial_weight):
    slab_rows = volume.shape[0]
    view_count = amplitude.shape[0]
    xy_count = lax.axis_size("xy")
    gz_count = lax.axis_size("gz")
    shard_width = measured.shape[2]
    detector_width = shard_width * xy_count
    total_rows = slab_rows * gz_count
    first_row = lax.axis_index("gz") * slab_rows
    up_pairs = [(i, i + 1) for i in range(gz_count - 1)]
    down_pairs = [(i + 1, i) for i in range(gz_count - 1)]

    def pack(meas_rows, weight_cols):
        flat = jnp.transpose(weight_cols, (1, 0, 2)).reshape(view_count, 1, -1)
        flat = jnp.pad(flat, ((0, 0), (0, 0), (0, shard_width - flat.shape[2])))
        return jnp.concatenate([meas_rows, flat], axis=1)

    def unpack(packed):
        cols = packed[:, 1, : 3 * 2].reshape(view_count, 3, 2)
        return packed[:, :1], jnp.transpose(cols, (1, 0, 2))

    from_below = lax.ppermute(
        pack(measured[:, slab_rows - 1 :], axial_weight[:, :, slab_rows - 2 :]), "gz", up_pairs
    )
    from_above = lax.ppermute(pack(measured[:, :1], axial_weight[:, :, :2]), "gz", down_pairs)
    meas_below, weight_below = unpack(from_below)
    meas_above, weight_above = unpack(from_above)
    measured_ext = jnp.concatenate([meas_below, measured, meas_above], axis=1)
    weight_ext = jnp.concatenate([weight_below, axial_weight, weight_above], axis=2)

    band_rows = forward_band(volume, amplitude, column_offset, column_width)
    band_height = slab_rows + 1
    placed = jnp.zeros((view_count * band_height, detector_width), jnp.float32)
    for v in range(view_count):
        placed = lax.dynamic_update_slice(placed, band_rows[v], (jnp.int32(v * band_height), band_start[v, 0]))
    reduced = reduce_scatter_xy(placed, xy_count).reshape(view_count, band_height, shard_width)
    proj_cols = reduced[:, :slab_rows]
    cover = reduced[:, slab_rows : slab_rows + 1]
    proj_ext = jnp.concatenate(
        [
            lax.ppermute(proj_cols[:, slab_rows - 2 :], "gz", up_pairs),
            proj_cols,
            lax.ppermute(proj_cols[:, :2], "gz", down_pairs),
        ],
        axis=1,
    )

    ext_rows = slab_rows + 2
    mid_w = weight_ext[1, :, 1 : ext_rows + 1][:, :, None]
    next_w = weight_ext[0, :, 2 : ext_rows + 2][:, :, None]
    prev_w = weight_ext[2, :, 0:ext_rows][:, :, None]
    centre = proj_ext[:, 1 : ext_rows + 1]
    after = proj_ext[:, 2 : ext_rows + 2]
    before = proj_ext[:, 0:ext_rows]
    projection = mid_w * centre + next_w * after + prev_w * before
    coverage = mid_w * cover + next_w * cover + prev_w * cover
    residual_ext = (measured_ext - projection) / jnp.maximum(coverage, 1.0)
    global_rows = first_row - 1 + jnp.arange(ext_rows, dtype=jnp.int32)
    valid = (global_rows >= 0) & (global_rows < total_rows)
    residual_ext = jnp.where(valid[None, :, None], residual_ext, 0.0)
    residual = residual_ext[:, 1 : slab_rows + 1]

    back_rows = (
        axial_weight[0][:, :, None] * residual_ext[:, 0:slab_rows]
        + axial_weight[1][:, :, None] * residual
        + axial_weight[2][:, :, None] * residual_ext[:, 2 : slab_rows + 2]
    )
    back_full = all_gather_xy(back_rows.reshape(view_count * slab_rows, shard_width), xy_count)
    back_full = back_full.reshape(view_count, slab_rows, detector_width)
    back_band = jnp.stack(
        [
            lax.dynamic_slice(back_full[v], (jnp.int32(0), band_start[v, 0]), (slab_rows, B))
            for v in range(view_count)
        ]
    )

    own_rows = first_row + jnp.arange(slab_rows, dtype=jnp.int32)
    row_weight = (
        jnp.where(own_rows[None, :] > 0, axial_weight[0], 0.0)
        + axial_weight[1]
        + jnp.where(own_rows[None, :] < total_rows - 1, axial_weight[2], 0.0)
    )
    volume_next = backward_update(back_band, volume, amplitude, column_offset, column_width, row_weight)
    return (volume_next, residual)


def solution(mesh):
    return jax.shard_map(
        local,
        mesh=mesh,
        in_specs=(
            P("gz", "xy"),
            P(None, "gz", "xy"),
            P(None, "xy"),
            P(None, "xy"),
            P(None, "xy"),
            P(None, "xy"),
            P(None, None, "gz"),
        ),
        out_specs=(P("gz", "xy"), P(None, "gz", "xy")),
        check_vma=False,
    )
```

```python
import jax
import jax.numpy as jnp
from jax import lax
from jax.experimental import pallas as pl
from jax.experimental.pallas import tpu as pltpu
from jax.sharding import PartitionSpec as P

B = 512
RELAX = 0.9
CHUNK = 2048
INTERPRET = False


def _band_mask(off, wid, rows, width):
    u = lax.broadcasted_iota(jnp.int32, (rows, width), 0)
    inside = (u - off).astype(jnp.uint32) < wid.astype(jnp.uint32)
    return jnp.where(inside, 1.0, 0.0).astype(jnp.bfloat16)


def _split(x):
    hi = x.astype(jnp.bfloat16)
    lo = (x - hi.astype(jnp.float32)).astype(jnp.bfloat16)
    return hi, lo


def _forward_kernel(vol_ref, amp_ref, off_ref, wid_ref, out_ref):
    slab_rows, columns = vol_ref.shape
    view_count = amp_ref.shape[0]
    band = out_ref.shape[2]
    out_ref[...] = jnp.zeros(out_ref.shape, jnp.float32)
    row = lax.broadcasted_iota(jnp.int32, (slab_rows, CHUNK), 0)

    def body(j, carry):
        c0 = pl.multiple_of(j * CHUNK, CHUNK)
        cells = vol_ref[:, pl.ds(c0, CHUNK)]
        for v in range(view_count):
            amp = amp_ref[pl.ds(v, 1), pl.ds(c0, CHUNK)]
            off = off_ref[pl.ds(v, 1), pl.ds(c0, CHUNK)]
            wid = wid_ref[pl.ds(v, 1), pl.ds(c0, CHUNK)]
            x = jnp.concatenate([cells * amp, jnp.where(row == 0, amp, 0.0)], axis=0)
            hi, lo = _split(x)
            lhs = jnp.concatenate([hi, lo], axis=0)
            mask = _band_mask(off, wid, band, CHUNK)
            out_ref[v] += lax.dot_general(
                lhs, mask, (((1,), (1,)), ((), ())), preferred_element_type=jnp.float32
            )
        return carry

    lax.fori_loop(0, columns // CHUNK, body, 0)


def forward_band(volume, amplitude, column_offset, column_width):
    slab_rows = volume.shape[0]
    view_count = amplitude.shape[0]
    acc = pl.pallas_call(
        _forward_kernel,
        out_shape=jax.ShapeDtypeStruct((view_count, 4 * slab_rows, B), jnp.float32),
        interpret=INTERPRET,
    )(volume, amplitude, column_offset, column_width)
    summed = acc[:, : 2 * slab_rows] + acc[:, 2 * slab_rows :]
    return summed[:, : slab_rows + 1]


def _backward_kernel(back_ref, vol_ref, amp_ref, off_ref, wid_ref, rw_ref, out_ref, split_ref):
    slab_rows, columns = vol_ref.shape
    view_count, _, band = back_ref.shape
    for v in range(view_count):
        hi, lo = _split(back_ref[v])
        split_ref[v] = jnp.concatenate([hi, lo], axis=0)

    def body(j, carry):
        c0 = pl.multiple_of(j * CHUNK, CHUNK)
        correction = None
        normalizer = None
        for v in range(view_count):
            amp = amp_ref[pl.ds(v, 1), pl.ds(c0, CHUNK)]
            off = off_ref[pl.ds(v, 1), pl.ds(c0, CHUNK)]
            wid = wid_ref[pl.ds(v, 1), pl.ds(c0, CHUNK)]
            mask = _band_mask(off, wid, band, CHUNK)
            r = jnp.dot(split_ref[v], mask, preferred_element_type=jnp.float32)
            part = amp * (r[:slab_rows] + r[slab_rows:])
            mass = rw_ref[v] * (amp * wid.astype(jnp.float32))
            correction = part if correction is None else correction + part
            normalizer = mass if normalizer is None else normalizer + mass
        cells = vol_ref[:, pl.ds(c0, CHUNK)]
        out_ref[:, pl.ds(c0, CHUNK)] = cells + RELAX * correction / normalizer
        return carry

    lax.fori_loop(0, columns // CHUNK, body, 0)


def backward_update(back_band, volume, amplitude, column_offset, column_width, row_weight):
    view_count, slab_rows, band = back_band.shape
    return pl.pallas_call(
        _backward_kernel,
        out_shape=jax.ShapeDtypeStruct(volume.shape, jnp.float32),
        scratch_shapes=[pltpu.VMEM((view_count, 2 * slab_rows, band), jnp.bfloat16)],
        interpret=INTERPRET,
    )(back_band, volume, amplitude, column_offset, column_width, row_weight[:, :, None])


def _bit_count(count):
    bits = count.bit_length() - 1
    assert 1 << bits == count
    return bits


def reduce_scatter_xy(x, count):
    rows = x.shape[0]
    width = x.shape[1] // count
    bits = _bit_count(count)
    idx = lax.axis_index("xy")
    y = jnp.transpose(x.reshape(rows, count, width), (1, 0, 2)).reshape((2,) * bits + (rows, width))
    for j in range(bits):
        axis = bits - 1 - j
        bit = (idx >> j) & 1
        keep = lax.dynamic_index_in_dim(y, bit, axis, keepdims=False)
        send = lax.dynamic_index_in_dim(y, 1 - bit, axis, keepdims=False)
        y = keep + lax.ppermute(send, "xy", [(i, i ^ (1 << j)) for i in range(count)])
    return y


def all_gather_xy(x, count):
    rows, width = x.shape
    bits = _bit_count(count)
    idx = lax.axis_index("xy")
    y = x
    for step, j in enumerate(reversed(range(bits))):
        bit = (idx >> j) & 1
        other = lax.ppermute(y, "xy", [(i, i ^ (1 << j)) for i in range(count)])
        low = jnp.where(bit == 0, y, other)
        high = jnp.where(bit == 0, other, y)
        y = jnp.stack([low, high], axis=step)
    return jnp.transpose(y.reshape(count, rows, width), (1, 0, 2)).reshape(rows, count * width)


def local(volume, measured, band_start, column_offset, column_width, amplitude, axial_weight):
    slab_rows = volume.shape[0]
    view_count = amplitude.shape[0]
    xy_count = lax.axis_size("xy")
    gz_count = lax.axis_size("gz")
    shard_width = measured.shape[2]
    detector_width = shard_width * xy_count
    total_rows = slab_rows * gz_count
    first_row = lax.axis_index("gz") * slab_rows
    up_pairs = [(i, i + 1) for i in range(gz_count - 1)]
    down_pairs = [(i + 1, i) for i in range(gz_count - 1)]

    def pack(meas_rows, weight_cols):
        flat = jnp.transpose(weight_cols, (1, 0, 2)).reshape(view_count, 1, -1)
        flat = jnp.pad(flat, ((0, 0), (0, 0), (0, shard_width - flat.shape[2])))
        return jnp.concatenate([meas_rows, flat], axis=1)

    def unpack(packed):
        cols = packed[:, 1, : 3 * 2].reshape(view_count, 3, 2)
        return packed[:, :1], jnp.transpose(cols, (1, 0, 2))


    band_rows = forward_band(volume, amplitude, column_offset, column_width)
    band_height = slab_rows + 1
    placed = jnp.zeros((view_count * band_height, detector_width), jnp.float32)
    for v in range(view_count):
        placed = lax.dynamic_update_slice(placed, band_rows[v], (jnp.int32(v * band_height), band_start[v, 0]))
    reduced = reduce_scatter_xy(placed, xy_count).reshape(view_count, band_height, shard_width)
    proj_cols = reduced[:, :slab_rows]
    cover = reduced[:, slab_rows : slab_rows + 1]
    halo_below = lax.ppermute(
        jnp.concatenate(
            [proj_cols[:, slab_rows - 2 :], pack(measured[:, slab_rows - 1 :], axial_weight[:, :, slab_rows - 2 :])],
            axis=1,
        ),
        "gz",
        up_pairs,
    )
    halo_above = lax.ppermute(
        jnp.concatenate([proj_cols[:, :2], pack(measured[:, :1], axial_weight[:, :, :2])], axis=1),
        "gz",
        down_pairs,
    )
    proj_ext = jnp.concatenate([halo_below[:, :2], proj_cols, halo_above[:, :2]], axis=1)
    meas_below, weight_below = unpack(halo_below[:, 2:])
    meas_above, weight_above = unpack(halo_above[:, 2:])
    measured_ext = jnp.concatenate([meas_below, measured, meas_above], axis=1)
    weight_ext = jnp.concatenate([weight_below, axial_weight, weight_above], axis=2)

    ext_rows = slab_rows + 2
    mid_w = weight_ext[1, :, 1 : ext_rows + 1][:, :, None]
    next_w = weight_ext[0, :, 2 : ext_rows + 2][:, :, None]
    prev_w = weight_ext[2, :, 0:ext_rows][:, :, None]
    centre = proj_ext[:, 1 : ext_rows + 1]
    after = proj_ext[:, 2 : ext_rows + 2]
    before = proj_ext[:, 0:ext_rows]
    projection = mid_w * centre + next_w * after + prev_w * before
    coverage = mid_w * cover + next_w * cover + prev_w * cover
    residual_ext = (measured_ext - projection) / jnp.maximum(coverage, 1.0)
    global_rows = first_row - 1 + jnp.arange(ext_rows, dtype=jnp.int32)
    valid = (global_rows >= 0) & (global_rows < total_rows)
    residual_ext = jnp.where(valid[None, :, None], residual_ext, 0.0)
    residual = residual_ext[:, 1 : slab_rows + 1]

    back_rows = (
        axial_weight[0][:, :, None] * residual_ext[:, 0:slab_rows]
        + axial_weight[1][:, :, None] * residual
        + axial_weight[2][:, :, None] * residual_ext[:, 2 : slab_rows + 2]
    )
    back_full = all_gather_xy(back_rows.reshape(view_count * slab_rows, shard_width), xy_count)
    back_full = back_full.reshape(view_count, slab_rows, detector_width)
    back_band = jnp.stack(
        [
            lax.dynamic_slice(back_full[v], (jnp.int32(0), band_start[v, 0]), (slab_rows, B))
            for v in range(view_count)
        ]
    )

    own_rows = first_row + jnp.arange(slab_rows, dtype=jnp.int32)
    row_weight = (
        jnp.where(own_rows[None, :] > 0, axial_weight[0], 0.0)
        + axial_weight[1]
        + jnp.where(own_rows[None, :] < total_rows - 1, axial_weight[2], 0.0)
    )
    volume_next = backward_update(back_band, volume, amplitude, column_offset, column_width, row_weight)
    return (volume_next, residual)


def solution(mesh):
    return jax.shard_map(
        local,
        mesh=mesh,
        in_specs=(
            P("gz", "xy"),
            P(None, "gz", "xy"),
            P(None, "xy"),
            P(None, "xy"),
            P(None, "xy"),
            P(None, "xy"),
            P(None, None, "gz"),
        ),
        out_specs=(P("gz", "xy"), P(None, "gz", "xy")),
        check_vma=False,
    )
```

```python
import jax
import jax.numpy as jnp
from jax import lax
from jax.experimental import pallas as pl
from jax.experimental.pallas import tpu as pltpu
from jax.sharding import PartitionSpec as P

B = 512
RELAX = 0.9
CHUNK = 2048
INTERPRET = False


def _band_mask(off, wid, rows, width):
    u = lax.broadcasted_iota(jnp.int32, (rows, width), 0)
    inside = (u - off).astype(jnp.uint32) < wid.astype(jnp.uint32)
    return jnp.where(inside, 1.0, 0.0).astype(jnp.bfloat16)


def _split(x):
    hi = x.astype(jnp.bfloat16)
    lo = (x - hi.astype(jnp.float32)).astype(jnp.bfloat16)
    return hi, lo


def _forward_kernel(start_ref, vol_ref, amp_ref, off_ref, wid_ref, out_ref, acc_ref):
    slab_rows, columns = vol_ref.shape
    view_count = amp_ref.shape[0]
    band = acc_ref.shape[2]
    chunks, _, shard_width = out_ref.shape
    detector_width = chunks * shard_width
    acc_ref[...] = jnp.zeros(acc_ref.shape, jnp.float32)
    row = lax.broadcasted_iota(jnp.int32, (slab_rows, CHUNK), 0)

    def body(j, carry):
        c0 = pl.multiple_of(j * CHUNK, CHUNK)
        cells = vol_ref[:, pl.ds(c0, CHUNK)]
        for v in range(view_count):
            amp = amp_ref[pl.ds(v, 1), pl.ds(c0, CHUNK)]
            off = off_ref[pl.ds(v, 1), pl.ds(c0, CHUNK)]
            wid = wid_ref[pl.ds(v, 1), pl.ds(c0, CHUNK)]
            x = jnp.concatenate([cells * amp, jnp.where(row == 0, amp, 0.0)], axis=0)
            hi, lo = _split(x)
            lhs = jnp.concatenate([hi, lo], axis=0)
            mask = _band_mask(off, wid, band, CHUNK)
            acc_ref[v] += lax.dot_general(
                lhs, mask, (((1,), (1,)), ((), ())), preferred_element_type=jnp.float32
            )
        return carry

    lax.fori_loop(0, columns // CHUNK, body, 0)
    height = slab_rows + 1
    placed = []
    for v in range(view_count):
        acc = acc_ref[v]
        summed = (acc[: 2 * slab_rows] + acc[2 * slab_rows :])[:height]
        ext = jnp.concatenate([summed, jnp.zeros((height, detector_width - band), jnp.float32)], axis=1)
        placed.append(pltpu.roll(ext, start_ref[v, 0], 1))
    joined = jnp.concatenate(placed, axis=0)
    for k in range(chunks):
        out_ref[k] = joined[:, k * shard_width : (k + 1) * shard_width]


def forward_band(volume, amplitude, column_offset, column_width, band_start, chunks, shard_width):
    slab_rows = volume.shape[0]
    view_count = amplitude.shape[0]
    smem = pl.BlockSpec(memory_space=pltpu.SMEM)
    vmem = pl.BlockSpec(memory_space=pltpu.VMEM)
    return pl.pallas_call(
        _forward_kernel,
        out_shape=jax.ShapeDtypeStruct((chunks, view_count * (slab_rows + 1), shard_width), jnp.float32),
        in_specs=[smem, vmem, vmem, vmem, vmem],
        scratch_shapes=[pltpu.VMEM((view_count, 4 * slab_rows, B), jnp.float32)],
        cost_estimate=pl.CostEstimate(
            flops=2 * view_count * 4 * slab_rows * B * volume.shape[1],
            transcendentals=0,
            bytes_accessed=4 * (volume.size + 3 * amplitude.size),
        ),
        interpret=INTERPRET,
    )(band_start, volume, amplitude, column_offset, column_width)


def _backward_kernel(back_ref, vol_ref, amp_ref, off_ref, wid_ref, rw_ref, out_ref, split_ref):
    slab_rows, columns = vol_ref.shape
    view_count, _, band = back_ref.shape
    for v in range(view_count):
        hi, lo = _split(back_ref[v])
        split_ref[v] = jnp.concatenate([hi, lo], axis=0)

    def body(j, carry):
        c0 = pl.multiple_of(j * CHUNK, CHUNK)
        correction = None
        normalizer = None
        for v in range(view_count):
            amp = amp_ref[pl.ds(v, 1), pl.ds(c0, CHUNK)]
            off = off_ref[pl.ds(v, 1), pl.ds(c0, CHUNK)]
            wid = wid_ref[pl.ds(v, 1), pl.ds(c0, CHUNK)]
            mask = _band_mask(off, wid, band, CHUNK)
            r = jnp.dot(split_ref[v], mask, preferred_element_type=jnp.float32)
            part = amp * (r[:slab_rows] + r[slab_rows:])
            mass = rw_ref[v] * (amp * wid.astype(jnp.float32))
            correction = part if correction is None else correction + part
            normalizer = mass if normalizer is None else normalizer + mass
        cells = vol_ref[:, pl.ds(c0, CHUNK)]
        out_ref[:, pl.ds(c0, CHUNK)] = cells + RELAX * correction / normalizer
        return carry

    lax.fori_loop(0, columns // CHUNK, body, 0)


def backward_update(back_band, volume, amplitude, column_offset, column_width, row_weight):
    view_count, slab_rows, band = back_band.shape
    return pl.pallas_call(
        _backward_kernel,
        out_shape=jax.ShapeDtypeStruct(volume.shape, jnp.float32),
        scratch_shapes=[pltpu.VMEM((view_count, 2 * slab_rows, band), jnp.bfloat16)],
        interpret=INTERPRET,
    )(back_band, volume, amplitude, column_offset, column_width, row_weight[:, :, None])


def _bit_count(count):
    bits = count.bit_length() - 1
    assert 1 << bits == count
    return bits


def reduce_scatter_xy(x, count):
    _, rows, width = x.shape
    bits = _bit_count(count)
    idx = lax.axis_index("xy")
    y = x.reshape((2,) * bits + (rows, width))
    for j in range(bits):
        axis = bits - 1 - j
        bit = (idx >> j) & 1
        keep = lax.dynamic_index_in_dim(y, bit, axis, keepdims=False)
        send = lax.dynamic_index_in_dim(y, 1 - bit, axis, keepdims=False)
        y = keep + lax.ppermute(send, "xy", [(i, i ^ (1 << j)) for i in range(count)])
    return y


def all_gather_xy(x, count):
    rows, width = x.shape
    bits = _bit_count(count)
    idx = lax.axis_index("xy")
    y = x
    for step, j in enumerate(reversed(range(bits))):
        bit = (idx >> j) & 1
        other = lax.ppermute(y, "xy", [(i, i ^ (1 << j)) for i in range(count)])
        low = jnp.where(bit == 0, y, other)
        high = jnp.where(bit == 0, other, y)
        y = jnp.stack([low, high], axis=step)
    return jnp.transpose(y.reshape(count, rows, width), (1, 0, 2)).reshape(rows, count * width)


def local(volume, measured, band_start, column_offset, column_width, amplitude, axial_weight):
    slab_rows = volume.shape[0]
    view_count = amplitude.shape[0]
    xy_count = lax.axis_size("xy")
    gz_count = lax.axis_size("gz")
    shard_width = measured.shape[2]
    detector_width = shard_width * xy_count
    total_rows = slab_rows * gz_count
    first_row = lax.axis_index("gz") * slab_rows
    up_pairs = [(i, i + 1) for i in range(gz_count - 1)]
    down_pairs = [(i + 1, i) for i in range(gz_count - 1)]

    def pack(meas_rows, weight_cols):
        flat = jnp.transpose(weight_cols, (1, 0, 2)).reshape(view_count, 1, -1)
        flat = jnp.pad(flat, ((0, 0), (0, 0), (0, shard_width - flat.shape[2])))
        return jnp.concatenate([meas_rows, flat], axis=1)

    def unpack(packed):
        cols = packed[:, 1, : 3 * 2].reshape(view_count, 3, 2)
        return packed[:, :1], jnp.transpose(cols, (1, 0, 2))

    from_below = lax.ppermute(
        pack(measured[:, slab_rows - 1 :], axial_weight[:, :, slab_rows - 2 :]), "gz", up_pairs
    )
    from_above = lax.ppermute(pack(measured[:, :1], axial_weight[:, :, :2]), "gz", down_pairs)
    meas_below, weight_below = unpack(from_below)
    meas_above, weight_above = unpack(from_above)
    measured_ext = jnp.concatenate([meas_below, measured, meas_above], axis=1)
    weight_ext = jnp.concatenate([weight_below, axial_weight, weight_above], axis=2)

    placed = forward_band(volume, amplitude, column_offset, column_width, band_start, xy_count, shard_width)
    band_height = slab_rows + 1
    reduced = reduce_scatter_xy(placed, xy_count).reshape(view_count, band_height, shard_width)
    proj_cols = reduced[:, :slab_rows]
    cover = reduced[:, slab_rows : slab_rows + 1]
    proj_ext = jnp.concatenate(
        [
            lax.ppermute(proj_cols[:, slab_rows - 2 :], "gz", up_pairs),
            proj_cols,
            lax.ppermute(proj_cols[:, :2], "gz", down_pairs),
        ],
        axis=1,
    )

    ext_rows = slab_rows + 2
    mid_w = weight_ext[1, :, 1 : ext_rows + 1][:, :, None]
    next_w = weight_ext[0, :, 2 : ext_rows + 2][:, :, None]
    prev_w = weight_ext[2, :, 0:ext_rows][:, :, None]
    centre = proj_ext[:, 1 : ext_rows + 1]
    after = proj_ext[:, 2 : ext_rows + 2]
    before = proj_ext[:, 0:ext_rows]
    projection = mid_w * centre + next_w * after + prev_w * before
    coverage = mid_w * cover + next_w * cover + prev_w * cover
    residual_ext = (measured_ext - projection) / jnp.maximum(coverage, 1.0)
    global_rows = first_row - 1 + jnp.arange(ext_rows, dtype=jnp.int32)
    valid = (global_rows >= 0) & (global_rows < total_rows)
    residual_ext = jnp.where(valid[None, :, None], residual_ext, 0.0)
    residual = residual_ext[:, 1 : slab_rows + 1]

    back_rows = (
        axial_weight[0][:, :, None] * residual_ext[:, 0:slab_rows]
        + axial_weight[1][:, :, None] * residual
        + axial_weight[2][:, :, None] * residual_ext[:, 2 : slab_rows + 2]
    )
    back_full = all_gather_xy(back_rows.reshape(view_count * slab_rows, shard_width), xy_count)
    back_full = back_full.reshape(view_count, slab_rows, detector_width)
    back_band = jnp.stack(
        [
            lax.dynamic_slice(back_full[v], (jnp.int32(0), band_start[v, 0]), (slab_rows, B))
            for v in range(view_count)
        ]
    )

    own_rows = first_row + jnp.arange(slab_rows, dtype=jnp.int32)
    row_weight = (
        jnp.where(own_rows[None, :] > 0, axial_weight[0], 0.0)
        + axial_weight[1]
        + jnp.where(own_rows[None, :] < total_rows - 1, axial_weight[2], 0.0)
    )
    volume_next = backward_update(back_band, volume, amplitude, column_offset, column_width, row_weight)
    return (volume_next, residual)


def solution(mesh):
    return jax.shard_map(
        local,
        mesh=mesh,
        in_specs=(
            P("gz", "xy"),
            P(None, "gz", "xy"),
            P(None, "xy"),
            P(None, "xy"),
            P(None, "xy"),
            P(None, "xy"),
            P(None, None, "gz"),
        ),
        out_specs=(P("gz", "xy"), P(None, "gz", "xy")),
        check_vma=False,
    )
```

```python
import jax
import jax.numpy as jnp
from jax import lax
from jax.experimental import pallas as pl
from jax.experimental.pallas import tpu as pltpu
from jax.sharding import PartitionSpec as P

B = 512
RELAX = 0.9
CHUNK = 2048
INTERPRET = False


def _band_mask(off, wid, rows, width):
    u = lax.broadcasted_iota(jnp.int32, (rows, width), 0)
    inside = (u - off).astype(jnp.uint32) < wid.astype(jnp.uint32)
    return jnp.where(inside, 1.0, 0.0).astype(jnp.bfloat16)


def _split(x):
    hi = x.astype(jnp.bfloat16)
    lo = (x - hi.astype(jnp.float32)).astype(jnp.bfloat16)
    return hi, lo


def _forward_kernel(start_ref, vol_ref, amp_ref, off_ref, wid_ref, out_ref, acc_ref):
    slab_rows, columns = vol_ref.shape
    view_count = amp_ref.shape[0]
    band = acc_ref.shape[2]
    chunks, _, shard_width = out_ref.shape
    detector_width = chunks * shard_width
    acc_ref[...] = jnp.zeros(acc_ref.shape, jnp.float32)
    row = lax.broadcasted_iota(jnp.int32, (slab_rows, CHUNK), 0)

    def body(j, carry):
        c0 = pl.multiple_of(j * CHUNK, CHUNK)
        cells = vol_ref[:, pl.ds(c0, CHUNK)]
        for v in range(view_count):
            amp = amp_ref[pl.ds(v, 1), pl.ds(c0, CHUNK)]
            off = off_ref[pl.ds(v, 1), pl.ds(c0, CHUNK)]
            wid = wid_ref[pl.ds(v, 1), pl.ds(c0, CHUNK)]
            x = jnp.concatenate([cells * amp, jnp.where(row == 0, amp, 0.0)], axis=0)
            hi, lo = _split(x)
            lhs = jnp.concatenate([hi, lo], axis=0)
            mask = _band_mask(off, wid, band, CHUNK)
            acc_ref[v] += lax.dot_general(
                lhs, mask, (((1,), (1,)), ((), ())), preferred_element_type=jnp.float32
            )
        return carry

    lax.fori_loop(0, columns // CHUNK, body, 0)
    height = slab_rows + 1
    placed = []
    for v in range(view_count):
        acc = acc_ref[v]
        summed = (acc[: 2 * slab_rows] + acc[2 * slab_rows :])[:height]
        ext = jnp.concatenate([summed, jnp.zeros((height, detector_width - band), jnp.float32)], axis=1)
        placed.append(pltpu.roll(ext, start_ref[v, 0], 1))
    joined = jnp.concatenate(placed, axis=0)
    for k in range(chunks):
        out_ref[k] = joined[:, k * shard_width : (k + 1) * shard_width]


def forward_band(volume, amplitude, column_offset, column_width, band_start, chunks, shard_width):
    slab_rows = volume.shape[0]
    view_count = amplitude.shape[0]
    smem = pl.BlockSpec(memory_space=pltpu.SMEM)
    vmem = pl.BlockSpec(memory_space=pltpu.VMEM)
    return pl.pallas_call(
        _forward_kernel,
        out_shape=jax.ShapeDtypeStruct((chunks, view_count * (slab_rows + 1), shard_width), jnp.float32),
        in_specs=[smem, vmem, vmem, vmem, vmem],
        scratch_shapes=[pltpu.VMEM((view_count, 4 * slab_rows, B), jnp.float32)],
        cost_estimate=pl.CostEstimate(
            flops=2 * view_count * 4 * slab_rows * B * volume.shape[1],
            transcendentals=0,
            bytes_accessed=4 * (volume.size + 3 * amplitude.size),
        ),
        interpret=INTERPRET,
    )(band_start, volume, amplitude, column_offset, column_width)


def _backward_kernel(back_ref, vol_ref, amp_ref, off_ref, wid_ref, rw_ref, out_ref, split_ref):
    slab_rows, columns = vol_ref.shape
    view_count, _, band = back_ref.shape
    for v in range(view_count):
        hi, lo = _split(back_ref[v])
        split_ref[v] = jnp.concatenate([hi, lo], axis=0)

    def body(j, carry):
        c0 = pl.multiple_of(j * CHUNK, CHUNK)
        correction = None
        normalizer = None
        for v in range(view_count):
            amp = amp_ref[pl.ds(v, 1), pl.ds(c0, CHUNK)]
            off = off_ref[pl.ds(v, 1), pl.ds(c0, CHUNK)]
            wid = wid_ref[pl.ds(v, 1), pl.ds(c0, CHUNK)]
            mask = _band_mask(off, wid, band, CHUNK)
            r = jnp.dot(split_ref[v], mask, preferred_element_type=jnp.float32)
            part = amp * (r[:slab_rows] + r[slab_rows:])
            mass = rw_ref[v] * (amp * wid.astype(jnp.float32))
            correction = part if correction is None else correction + part
            normalizer = mass if normalizer is None else normalizer + mass
        cells = vol_ref[:, pl.ds(c0, CHUNK)]
        out_ref[:, pl.ds(c0, CHUNK)] = cells + RELAX * correction / normalizer
        return carry

    lax.fori_loop(0, columns // CHUNK, body, 0)


def backward_update(back_band, volume, amplitude, column_offset, column_width, row_weight):
    view_count, slab_rows, band = back_band.shape
    return pl.pallas_call(
        _backward_kernel,
        out_shape=jax.ShapeDtypeStruct(volume.shape, jnp.float32),
        scratch_shapes=[pltpu.VMEM((view_count, 2 * slab_rows, band), jnp.bfloat16)],
        interpret=INTERPRET,
    )(back_band, volume, amplitude, column_offset, column_width, row_weight[:, :, None])


def _bit_count(count):
    bits = count.bit_length() - 1
    assert 1 << bits == count
    return bits


def reduce_scatter_xy(x, count):
    _, rows, width = x.shape
    bits = _bit_count(count)
    idx = lax.axis_index("xy")
    y = x.reshape((2,) * bits + (rows, width))
    for j in range(bits):
        axis = bits - 1 - j
        bit = (idx >> j) & 1
        keep = lax.dynamic_index_in_dim(y, bit, axis, keepdims=False)
        send = lax.dynamic_index_in_dim(y, 1 - bit, axis, keepdims=False)
        y = keep + lax.ppermute(send, "xy", [(i, i ^ (1 << j)) for i in range(count)])
    return y


def all_gather_xy(x, count):
    rows, width = x.shape
    bits = _bit_count(count)
    idx = lax.axis_index("xy")
    y = x
    for step, j in enumerate(reversed(range(bits))):
        bit = (idx >> j) & 1
        other = lax.ppermute(y, "xy", [(i, i ^ (1 << j)) for i in range(count)])
        low = jnp.where(bit == 0, y, other)
        high = jnp.where(bit == 0, other, y)
        y = jnp.stack([low, high], axis=step)
    return jnp.transpose(y.reshape(count, rows, width), (1, 0, 2)).reshape(rows, count * width)


def gather_band(rows, count, own_starts, partner_starts, band):
    views, slab_rows, width = rows.shape
    bits = _bit_count(count)
    idx = lax.axis_index("xy")
    y = rows
    for step, j in enumerate(reversed(range(1, bits))):
        bit = (idx >> j) & 1
        other = lax.ppermute(y, "xy", [(i, i ^ (1 << j)) for i in range(count)])
        low = jnp.where(bit == 0, y, other)
        high = jnp.where(bit == 0, other, y)
        y = jnp.stack([low, high], axis=step)
    half = count // 2
    y = y.reshape(half, views, slab_rows, width)
    parity = idx & 1
    needed = band // width + 1
    sent = (needed + 1) // 2

    def first_index(start, block_parity):
        k0 = start // width
        return jnp.minimum((k0 + (k0 + block_parity) % 2) // 2, half - sent)

    send = jnp.stack(
        [lax.dynamic_slice_in_dim(y[:, v], first_index(partner_starts[v], parity), sent, 0) for v in range(views)]
    )
    recv = lax.ppermute(send, "xy", [(i, i ^ 1) for i in range(count)])
    out = []
    for v in range(views):
        start = own_starts[v]
        k0 = start // width
        base = first_index(start, 1 - parity)
        pieces = []
        for i in range(needed):
            k = k0 + i
            own = lax.dynamic_index_in_dim(y[:, v], jnp.minimum(k // 2, half - 1), 0, keepdims=False)
            got = lax.dynamic_index_in_dim(recv[v], jnp.clip(k // 2 - base, 0, sent - 1), 0, keepdims=False)
            pieces.append(jnp.where(k % 2 == parity, own, got))
        window = jnp.concatenate(pieces, axis=1)
        out.append(lax.dynamic_slice(window, (jnp.int32(0), start - k0 * width), (slab_rows, band)))
    return jnp.stack(out)


def local(volume, measured, band_start, column_offset, column_width, amplitude, axial_weight):
    slab_rows = volume.shape[0]
    view_count = amplitude.shape[0]
    xy_count = lax.axis_size("xy")
    gz_count = lax.axis_size("gz")
    shard_width = measured.shape[2]
    detector_width = shard_width * xy_count
    total_rows = slab_rows * gz_count
    first_row = lax.axis_index("gz") * slab_rows
    up_pairs = [(i, i + 1) for i in range(gz_count - 1)]
    down_pairs = [(i + 1, i) for i in range(gz_count - 1)]

    def pack(meas_rows, weight_cols):
        flat = jnp.transpose(weight_cols, (1, 0, 2)).reshape(view_count, 1, -1)
        flat = jnp.pad(flat, ((0, 0), (0, 0), (0, shard_width - flat.shape[2])))
        return jnp.concatenate([meas_rows, flat], axis=1)

    def unpack(packed):
        cols = packed[:, 1, : 3 * 2].reshape(view_count, 3, 2)
        return packed[:, :1], jnp.transpose(cols, (1, 0, 2))

    from_below = lax.ppermute(
        pack(measured[:, slab_rows - 1 :], axial_weight[:, :, slab_rows - 2 :]), "gz", up_pairs
    )
    from_above = lax.ppermute(pack(measured[:, :1], axial_weight[:, :, :2]), "gz", down_pairs)
    meas_below, weight_below = unpack(from_below)
    meas_above, weight_above = unpack(from_above)
    measured_ext = jnp.concatenate([meas_below, measured, meas_above], axis=1)
    weight_ext = jnp.concatenate([weight_below, axial_weight, weight_above], axis=2)

    partner_start = lax.ppermute(band_start, "xy", [(i, i ^ 1) for i in range(xy_count)])
    placed = forward_band(volume, amplitude, column_offset, column_width, band_start, xy_count, shard_width)
    band_height = slab_rows + 1
    reduced = reduce_scatter_xy(placed, xy_count).reshape(view_count, band_height, shard_width)
    proj_cols = reduced[:, :slab_rows]
    cover = reduced[:, slab_rows : slab_rows + 1]
    proj_ext = jnp.concatenate(
        [
            lax.ppermute(proj_cols[:, slab_rows - 2 :], "gz", up_pairs),
            proj_cols,
            lax.ppermute(proj_cols[:, :2], "gz", down_pairs),
        ],
        axis=1,
    )

    ext_rows = slab_rows + 2
    mid_w = weight_ext[1, :, 1 : ext_rows + 1][:, :, None]
    next_w = weight_ext[0, :, 2 : ext_rows + 2][:, :, None]
    prev_w = weight_ext[2, :, 0:ext_rows][:, :, None]
    centre = proj_ext[:, 1 : ext_rows + 1]
    after = proj_ext[:, 2 : ext_rows + 2]
    before = proj_ext[:, 0:ext_rows]
    projection = mid_w * centre + next_w * after + prev_w * before
    coverage = mid_w * cover + next_w * cover + prev_w * cover
    residual_ext = (measured_ext - projection) / jnp.maximum(coverage, 1.0)
    global_rows = first_row - 1 + jnp.arange(ext_rows, dtype=jnp.int32)
    valid = (global_rows >= 0) & (global_rows < total_rows)
    residual_ext = jnp.where(valid[None, :, None], residual_ext, 0.0)
    residual = residual_ext[:, 1 : slab_rows + 1]

    back_rows = (
        axial_weight[0][:, :, None] * residual_ext[:, 0:slab_rows]
        + axial_weight[1][:, :, None] * residual
        + axial_weight[2][:, :, None] * residual_ext[:, 2 : slab_rows + 2]
    )
    back_band = gather_band(
        back_rows, xy_count, [band_start[v, 0] for v in range(view_count)],
        [partner_start[v, 0] for v in range(view_count)], B,
    )

    own_rows = first_row + jnp.arange(slab_rows, dtype=jnp.int32)
    row_weight = (
        jnp.where(own_rows[None, :] > 0, axial_weight[0], 0.0)
        + axial_weight[1]
        + jnp.where(own_rows[None, :] < total_rows - 1, axial_weight[2], 0.0)
    )
    volume_next = backward_update(back_band, volume, amplitude, column_offset, column_width, row_weight)
    return (volume_next, residual)


def solution(mesh):
    return jax.shard_map(
        local,
        mesh=mesh,
        in_specs=(
            P("gz", "xy"),
            P(None, "gz", "xy"),
            P(None, "xy"),
            P(None, "xy"),
            P(None, "xy"),
            P(None, "xy"),
            P(None, None, "gz"),
        ),
        out_specs=(P("gz", "xy"), P(None, "gz", "xy")),
        check_vma=False,
    )
```

```python
import jax
import jax.numpy as jnp
from jax import lax
from jax.experimental import pallas as pl
from jax.experimental.pallas import tpu as pltpu
from jax.sharding import PartitionSpec as P

B = 512
RELAX = 0.9
CHUNK = 2048
INTERPRET = False


def _band_mask(off, wid, rows, width):
    u = lax.broadcasted_iota(jnp.int32, (rows, width), 0)
    inside = (u - off).astype(jnp.uint32) < wid.astype(jnp.uint32)
    return jnp.where(inside, 1.0, 0.0).astype(jnp.bfloat16)


def _split(x):
    hi = x.astype(jnp.bfloat16)
    lo = (x - hi.astype(jnp.float32)).astype(jnp.bfloat16)
    return hi, lo


def _forward_kernel(start_ref, vol_ref, amp_ref, off_ref, wid_ref, out_ref, acc_ref):
    slab_rows, columns = vol_ref.shape
    view_count = amp_ref.shape[0]
    band = acc_ref.shape[2]
    chunks, _, shard_width = out_ref.shape
    detector_width = chunks * shard_width
    acc_ref[...] = jnp.zeros(acc_ref.shape, jnp.float32)
    row = lax.broadcasted_iota(jnp.int32, (slab_rows, CHUNK), 0)

    def body(j, carry):
        c0 = pl.multiple_of(j * CHUNK, CHUNK)
        cells = vol_ref[:, pl.ds(c0, CHUNK)]
        for v in range(view_count):
            amp = amp_ref[pl.ds(v, 1), pl.ds(c0, CHUNK)]
            off = off_ref[pl.ds(v, 1), pl.ds(c0, CHUNK)]
            wid = wid_ref[pl.ds(v, 1), pl.ds(c0, CHUNK)]
            cells_hi, cells_lo = _split(cells * amp)
            amp_hi, amp_lo = _split(amp)
            amp_rows = jnp.where(
                row == 0,
                amp_hi.astype(jnp.float32),
                jnp.where(row == 1, amp_lo.astype(jnp.float32), 0.0),
            ).astype(jnp.bfloat16)
            lhs = jnp.concatenate([cells_hi, cells_lo, amp_rows], axis=0)
            mask = _band_mask(off, wid, band, CHUNK)
            acc_ref[v] += lax.dot_general(
                lhs, mask, (((1,), (1,)), ((), ())), preferred_element_type=jnp.float32
            )
        return carry

    lax.fori_loop(0, columns // CHUNK, body, 0)
    height = slab_rows + 1
    placed = []
    for v in range(view_count):
        acc = acc_ref[v]
        summed = jnp.concatenate(
            [
                acc[:slab_rows] + acc[slab_rows : 2 * slab_rows],
                acc[2 * slab_rows : 2 * slab_rows + 1] + acc[2 * slab_rows + 1 : 2 * slab_rows + 2],
            ],
            axis=0,
        )
        ext = jnp.concatenate([summed, jnp.zeros((height, detector_width - band), jnp.float32)], axis=1)
        placed.append(pltpu.roll(ext, start_ref[v, 0], 1))
    joined = jnp.concatenate(placed, axis=0)
    for k in range(chunks):
        out_ref[k] = joined[:, k * shard_width : (k + 1) * shard_width]


def forward_band(volume, amplitude, column_offset, column_width, band_start, chunks, shard_width):
    slab_rows = volume.shape[0]
    view_count = amplitude.shape[0]
    smem = pl.BlockSpec(memory_space=pltpu.SMEM)
    vmem = pl.BlockSpec(memory_space=pltpu.VMEM)
    return pl.pallas_call(
        _forward_kernel,
        out_shape=jax.ShapeDtypeStruct((chunks, view_count * (slab_rows + 1), shard_width), jnp.float32),
        in_specs=[smem, vmem, vmem, vmem, vmem],
        scratch_shapes=[pltpu.VMEM((view_count, 3 * slab_rows, B), jnp.float32)],
        cost_estimate=pl.CostEstimate(
            flops=2 * view_count * 3 * slab_rows * B * volume.shape[1],
            transcendentals=0,
            bytes_accessed=4 * (volume.size + 3 * amplitude.size),
        ),
        interpret=INTERPRET,
    )(band_start, volume, amplitude, column_offset, column_width)


def _backward_kernel(back_ref, vol_ref, amp_ref, off_ref, wid_ref, rw_ref, out_ref, split_ref):
    slab_rows, columns = vol_ref.shape
    view_count, _, band = back_ref.shape
    for v in range(view_count):
        hi, lo = _split(back_ref[v])
        split_ref[v] = jnp.concatenate([hi, lo], axis=0)

    def body(j, carry):
        c0 = pl.multiple_of(j * CHUNK, CHUNK)
        correction = None
        normalizer = None
        for v in range(view_count):
            amp = amp_ref[pl.ds(v, 1), pl.ds(c0, CHUNK)]
            off = off_ref[pl.ds(v, 1), pl.ds(c0, CHUNK)]
            wid = wid_ref[pl.ds(v, 1), pl.ds(c0, CHUNK)]
            mask = _band_mask(off, wid, band, CHUNK)
            r = jnp.dot(split_ref[v], mask, preferred_element_type=jnp.float32)
            part = amp * (r[:slab_rows] + r[slab_rows:])
            mass = rw_ref[v] * (amp * wid.astype(jnp.float32))
            correction = part if correction is None else correction + part
            normalizer = mass if normalizer is None else normalizer + mass
        cells = vol_ref[:, pl.ds(c0, CHUNK)]
        out_ref[:, pl.ds(c0, CHUNK)] = cells + RELAX * correction / normalizer
        return carry

    lax.fori_loop(0, columns // CHUNK, body, 0)


def backward_update(back_band, volume, amplitude, column_offset, column_width, row_weight):
    view_count, slab_rows, band = back_band.shape
    return pl.pallas_call(
        _backward_kernel,
        out_shape=jax.ShapeDtypeStruct(volume.shape, jnp.float32),
        scratch_shapes=[pltpu.VMEM((view_count, 2 * slab_rows, band), jnp.bfloat16)],
        interpret=INTERPRET,
    )(back_band, volume, amplitude, column_offset, column_width, row_weight[:, :, None])


def _bit_count(count):
    bits = count.bit_length() - 1
    assert 1 << bits == count
    return bits


def reduce_scatter_xy(x, count):
    _, rows, width = x.shape
    bits = _bit_count(count)
    idx = lax.axis_index("xy")
    y = x.reshape((2,) * bits + (rows, width))
    for j in range(bits):
        axis = bits - 1 - j
        bit = (idx >> j) & 1
        keep = lax.dynamic_index_in_dim(y, bit, axis, keepdims=False)
        send = lax.dynamic_index_in_dim(y, 1 - bit, axis, keepdims=False)
        y = keep + lax.ppermute(send, "xy", [(i, i ^ (1 << j)) for i in range(count)])
    return y


def all_gather_xy(x, count):
    rows, width = x.shape
    bits = _bit_count(count)
    idx = lax.axis_index("xy")
    y = x
    for step, j in enumerate(reversed(range(bits))):
        bit = (idx >> j) & 1
        other = lax.ppermute(y, "xy", [(i, i ^ (1 << j)) for i in range(count)])
        low = jnp.where(bit == 0, y, other)
        high = jnp.where(bit == 0, other, y)
        y = jnp.stack([low, high], axis=step)
    return jnp.transpose(y.reshape(count, rows, width), (1, 0, 2)).reshape(rows, count * width)


def local(volume, measured, band_start, column_offset, column_width, amplitude, axial_weight):
    slab_rows = volume.shape[0]
    view_count = amplitude.shape[0]
    xy_count = lax.axis_size("xy")
    gz_count = lax.axis_size("gz")
    shard_width = measured.shape[2]
    detector_width = shard_width * xy_count
    total_rows = slab_rows * gz_count
    first_row = lax.axis_index("gz") * slab_rows
    up_pairs = [(i, i + 1) for i in range(gz_count - 1)]
    down_pairs = [(i + 1, i) for i in range(gz_count - 1)]

    def pack(meas_rows, weight_cols):
        flat = jnp.transpose(weight_cols, (1, 0, 2)).reshape(view_count, 1, -1)
        flat = jnp.pad(flat, ((0, 0), (0, 0), (0, shard_width - flat.shape[2])))
        return jnp.concatenate([meas_rows, flat], axis=1)

    def unpack(packed):
        cols = packed[:, 1, : 3 * 2].reshape(view_count, 3, 2)
        return packed[:, :1], jnp.transpose(cols, (1, 0, 2))

    from_below = lax.ppermute(
        pack(measured[:, slab_rows - 1 :], axial_weight[:, :, slab_rows - 2 :]), "gz", up_pairs
    )
    from_above = lax.ppermute(pack(measured[:, :1], axial_weight[:, :, :2]), "gz", down_pairs)
    meas_below, weight_below = unpack(from_below)
    meas_above, weight_above = unpack(from_above)
    measured_ext = jnp.concatenate([meas_below, measured, meas_above], axis=1)
    weight_ext = jnp.concatenate([weight_below, axial_weight, weight_above], axis=2)

    placed = forward_band(volume, amplitude, column_offset, column_width, band_start, xy_count, shard_width)
    band_height = slab_rows + 1
    reduced = reduce_scatter_xy(placed, xy_count).reshape(view_count, band_height, shard_width)
    proj_cols = reduced[:, :slab_rows]
    cover = reduced[:, slab_rows : slab_rows + 1]
    proj_ext = jnp.concatenate(
        [
            lax.ppermute(proj_cols[:, slab_rows - 2 :], "gz", up_pairs),
            proj_cols,
            lax.ppermute(proj_cols[:, :2], "gz", down_pairs),
        ],
        axis=1,
    )

    ext_rows = slab_rows + 2
    mid_w = weight_ext[1, :, 1 : ext_rows + 1][:, :, None]
    next_w = weight_ext[0, :, 2 : ext_rows + 2][:, :, None]
    prev_w = weight_ext[2, :, 0:ext_rows][:, :, None]
    centre = proj_ext[:, 1 : ext_rows + 1]
    after = proj_ext[:, 2 : ext_rows + 2]
    before = proj_ext[:, 0:ext_rows]
    projection = mid_w * centre + next_w * after + prev_w * before
    coverage = mid_w * cover + next_w * cover + prev_w * cover
    residual_ext = (measured_ext - projection) / jnp.maximum(coverage, 1.0)
    global_rows = first_row - 1 + jnp.arange(ext_rows, dtype=jnp.int32)
    valid = (global_rows >= 0) & (global_rows < total_rows)
    residual_ext = jnp.where(valid[None, :, None], residual_ext, 0.0)
    residual = residual_ext[:, 1 : slab_rows + 1]

    back_rows = (
        axial_weight[0][:, :, None] * residual_ext[:, 0:slab_rows]
        + axial_weight[1][:, :, None] * residual
        + axial_weight[2][:, :, None] * residual_ext[:, 2 : slab_rows + 2]
    )
    back_full = all_gather_xy(back_rows.reshape(view_count * slab_rows, shard_width), xy_count)
    back_full = back_full.reshape(view_count, slab_rows, detector_width)
    back_band = jnp.stack(
        [
            lax.dynamic_slice(back_full[v], (jnp.int32(0), band_start[v, 0]), (slab_rows, B))
            for v in range(view_count)
        ]
    )

    own_rows = first_row + jnp.arange(slab_rows, dtype=jnp.int32)
    row_weight = (
        jnp.where(own_rows[None, :] > 0, axial_weight[0], 0.0)
        + axial_weight[1]
        + jnp.where(own_rows[None, :] < total_rows - 1, axial_weight[2], 0.0)
    )
    volume_next = backward_update(back_band, volume, amplitude, column_offset, column_width, row_weight)
    return (volume_next, residual)


def solution(mesh):
    return jax.shard_map(
        local,
        mesh=mesh,
        in_specs=(
            P("gz", "xy"),
            P(None, "gz", "xy"),
            P(None, "xy"),
            P(None, "xy"),
            P(None, "xy"),
            P(None, "xy"),
            P(None, None, "gz"),
        ),
        out_specs=(P("gz", "xy"), P(None, "gz", "xy")),
        check_vma=False,
    )
```

```python
import jax
import jax.numpy as jnp
from jax import lax
from jax.experimental import pallas as pl
from jax.experimental.pallas import tpu as pltpu
from jax.sharding import PartitionSpec as P

B = 512
RELAX = 0.9
CHUNK = 2048
INTERPRET = False


def _band_mask(off, wid, rows, width):
    u = lax.broadcasted_iota(jnp.int32, (rows, width), 0)
    inside = (u - off).astype(jnp.uint32) < wid.astype(jnp.uint32)
    return jnp.where(inside, 1.0, 0.0).astype(jnp.bfloat16)


def _split(x):
    hi = x.astype(jnp.bfloat16)
    lo = (x - hi.astype(jnp.float32)).astype(jnp.bfloat16)
    return hi, lo


def _forward_kernel(start_ref, vol_ref, amp_ref, off_ref, wid_ref, out_ref, acc_ref):
    slab_rows, columns = vol_ref.shape
    view_count = amp_ref.shape[0]
    band = acc_ref.shape[2]
    chunks, _, shard_width = out_ref.shape
    detector_width = chunks * shard_width
    acc_ref[...] = jnp.zeros(acc_ref.shape, jnp.float32)
    row = lax.broadcasted_iota(jnp.int32, (slab_rows, CHUNK), 0)

    def body(j, carry):
        c0 = pl.multiple_of(j * CHUNK, CHUNK)
        cells = vol_ref[:, pl.ds(c0, CHUNK)]
        for v in range(view_count):
            amp = amp_ref[pl.ds(v, 1), pl.ds(c0, CHUNK)]
            off = off_ref[pl.ds(v, 1), pl.ds(c0, CHUNK)]
            wid = wid_ref[pl.ds(v, 1), pl.ds(c0, CHUNK)]
            cells_hi, cells_lo = _split(cells * amp)
            amp_hi, amp_lo = _split(amp)
            amp_rows = jnp.where(
                row == 0,
                amp_hi.astype(jnp.float32),
                jnp.where(row == 1, amp_lo.astype(jnp.float32), 0.0),
            ).astype(jnp.bfloat16)
            lhs = jnp.concatenate([cells_hi, cells_lo, amp_rows], axis=0)
            mask = _band_mask(off, wid, band, CHUNK)
            acc_ref[v] += lax.dot_general(
                lhs, mask, (((1,), (1,)), ((), ())), preferred_element_type=jnp.float32
            )
        return carry

    lax.fori_loop(0, columns // CHUNK, body, 0)
    height = slab_rows + 1
    placed = []
    for v in range(view_count):
        acc = acc_ref[v]
        summed = jnp.concatenate(
            [
                acc[:slab_rows] + acc[slab_rows : 2 * slab_rows],
                acc[2 * slab_rows : 2 * slab_rows + 1] + acc[2 * slab_rows + 1 : 2 * slab_rows + 2],
            ],
            axis=0,
        )
        ext = jnp.concatenate([summed, jnp.zeros((height, detector_width - band), jnp.float32)], axis=1)
        placed.append(pltpu.roll(ext, start_ref[v, 0], 1))
    joined = jnp.concatenate(placed, axis=0)
    for k in range(chunks):
        out_ref[k] = joined[:, k * shard_width : (k + 1) * shard_width]


def forward_band(volume, amplitude, column_offset, column_width, band_start, chunks, shard_width):
    slab_rows = volume.shape[0]
    view_count = amplitude.shape[0]
    smem = pl.BlockSpec(memory_space=pltpu.SMEM)
    vmem = pl.BlockSpec(memory_space=pltpu.VMEM)
    return pl.pallas_call(
        _forward_kernel,
        out_shape=jax.ShapeDtypeStruct((chunks, view_count * (slab_rows + 1), shard_width), jnp.float32),
        in_specs=[smem, vmem, vmem, vmem, vmem],
        scratch_shapes=[pltpu.VMEM((view_count, 3 * slab_rows, B), jnp.float32)],
        cost_estimate=pl.CostEstimate(
            flops=2 * view_count * 3 * slab_rows * B * volume.shape[1],
            transcendentals=0,
            bytes_accessed=4 * (volume.size + 3 * amplitude.size),
        ),
        interpret=INTERPRET,
    )(band_start, volume, amplitude, column_offset, column_width)


def _backward_kernel(back_ref, vol_ref, amp_ref, off_ref, wid_ref, rw_ref, out_ref, split_ref):
    slab_rows, columns = vol_ref.shape
    view_count, _, band = back_ref.shape
    for v in range(view_count):
        hi, lo = _split(back_ref[v])
        split_ref[v] = jnp.concatenate([hi, lo], axis=0)

    def body(j, carry):
        c0 = pl.multiple_of(j * CHUNK, CHUNK)
        correction = None
        normalizer = None
        for v in range(view_count):
            amp = amp_ref[pl.ds(v, 1), pl.ds(c0, CHUNK)]
            off = off_ref[pl.ds(v, 1), pl.ds(c0, CHUNK)]
            wid = wid_ref[pl.ds(v, 1), pl.ds(c0, CHUNK)]
            mask = _band_mask(off, wid, band, CHUNK)
            r = jnp.dot(split_ref[v], mask, preferred_element_type=jnp.float32)
            part = amp * (r[:slab_rows] + r[slab_rows:])
            mass = rw_ref[v] * (amp * wid.astype(jnp.float32))
            correction = part if correction is None else correction + part
            normalizer = mass if normalizer is None else normalizer + mass
        cells = vol_ref[:, pl.ds(c0, CHUNK)]
        out_ref[:, pl.ds(c0, CHUNK)] = cells + RELAX * correction / normalizer
        return carry

    lax.fori_loop(0, columns // CHUNK, body, 0)


def backward_update(back_band, volume, amplitude, column_offset, column_width, row_weight):
    view_count, slab_rows, band = back_band.shape
    return pl.pallas_call(
        _backward_kernel,
        out_shape=jax.ShapeDtypeStruct(volume.shape, jnp.float32),
        scratch_shapes=[pltpu.VMEM((view_count, 2 * slab_rows, band), jnp.bfloat16)],
        interpret=INTERPRET,
    )(back_band, volume, amplitude, column_offset, column_width, row_weight[:, :, None])


def _bit_count(count):
    bits = count.bit_length() - 1
    assert 1 << bits == count
    return bits


def reduce_scatter_xy(x, count):
    _, rows, width = x.shape
    bits = _bit_count(count)
    idx = lax.axis_index("xy")
    y = x.reshape((2,) * bits + (rows, width))
    for j in range(bits):
        axis = bits - 1 - j
        bit = (idx >> j) & 1
        keep = lax.dynamic_index_in_dim(y, bit, axis, keepdims=False)
        send = lax.dynamic_index_in_dim(y, 1 - bit, axis, keepdims=False)
        y = keep + lax.ppermute(send, "xy", [(i, i ^ (1 << j)) for i in range(count)])
    return y


def all_gather_xy(x, count):
    rows, width = x.shape
    bits = _bit_count(count)
    idx = lax.axis_index("xy")
    y = x
    for step, j in enumerate(reversed(range(bits))):
        bit = (idx >> j) & 1
        other = lax.ppermute(y, "xy", [(i, i ^ (1 << j)) for i in range(count)])
        low = jnp.where(bit == 0, y, other)
        high = jnp.where(bit == 0, other, y)
        y = jnp.stack([low, high], axis=step)
    return jnp.transpose(y.reshape(count, rows, width), (1, 0, 2)).reshape(rows, count * width)


def local(volume, measured, band_start, column_offset, column_width, amplitude, axial_weight):
    slab_rows = volume.shape[0]
    view_count = amplitude.shape[0]
    xy_count = lax.axis_size("xy")
    gz_count = lax.axis_size("gz")
    shard_width = measured.shape[2]
    detector_width = shard_width * xy_count
    total_rows = slab_rows * gz_count
    first_row = lax.axis_index("gz") * slab_rows
    up_pairs = [(i, i + 1) for i in range(gz_count - 1)]
    down_pairs = [(i + 1, i) for i in range(gz_count - 1)]

    def pack(meas_rows, weight_cols):
        flat = jnp.transpose(weight_cols, (1, 0, 2)).reshape(view_count, 1, -1)
        flat = jnp.pad(flat, ((0, 0), (0, 0), (0, shard_width - flat.shape[2])))
        return jnp.concatenate([meas_rows, flat], axis=1)

    def unpack(packed):
        cols = packed[:, 1, : 3 * 2].reshape(view_count, 3, 2)
        return packed[:, :1], jnp.transpose(cols, (1, 0, 2))

    gz_index = lax.axis_index("gz")

    def exchange(upward, downward):
        if gz_count != 2:
            return lax.ppermute(upward, "gz", up_pairs), lax.ppermute(downward, "gz", down_pairs)
        got = lax.ppermute(jnp.where(gz_index == 0, upward, downward), "gz", [(0, 1), (1, 0)])
        return jnp.where(gz_index == 1, got, 0.0), jnp.where(gz_index == 0, got, 0.0)

    from_below, from_above = exchange(
        pack(measured[:, slab_rows - 1 :], axial_weight[:, :, slab_rows - 2 :]),
        pack(measured[:, :1], axial_weight[:, :, :2]),
    )
    meas_below, weight_below = unpack(from_below)
    meas_above, weight_above = unpack(from_above)
    measured_ext = jnp.concatenate([meas_below, measured, meas_above], axis=1)
    weight_ext = jnp.concatenate([weight_below, axial_weight, weight_above], axis=2)

    placed = forward_band(volume, amplitude, column_offset, column_width, band_start, xy_count, shard_width)
    band_height = slab_rows + 1
    reduced = reduce_scatter_xy(placed, xy_count).reshape(view_count, band_height, shard_width)
    proj_cols = reduced[:, :slab_rows]
    cover = reduced[:, slab_rows : slab_rows + 1]
    proj_below, proj_above = exchange(proj_cols[:, slab_rows - 2 :], proj_cols[:, :2])
    proj_ext = jnp.concatenate([proj_below, proj_cols, proj_above], axis=1)

    ext_rows = slab_rows + 2
    mid_w = weight_ext[1, :, 1 : ext_rows + 1][:, :, None]
    next_w = weight_ext[0, :, 2 : ext_rows + 2][:, :, None]
    prev_w = weight_ext[2, :, 0:ext_rows][:, :, None]
    centre = proj_ext[:, 1 : ext_rows + 1]
    after = proj_ext[:, 2 : ext_rows + 2]
    before = proj_ext[:, 0:ext_rows]
    projection = mid_w * centre + next_w * after + prev_w * before
    coverage = mid_w * cover + next_w * cover + prev_w * cover
    residual_ext = (measured_ext - projection) / jnp.maximum(coverage, 1.0)
    global_rows = first_row - 1 + jnp.arange(ext_rows, dtype=jnp.int32)
    valid = (global_rows >= 0) & (global_rows < total_rows)
    residual_ext = jnp.where(valid[None, :, None], residual_ext, 0.0)
    residual = residual_ext[:, 1 : slab_rows + 1]

    back_rows = (
        axial_weight[0][:, :, None] * residual_ext[:, 0:slab_rows]
        + axial_weight[1][:, :, None] * residual
        + axial_weight[2][:, :, None] * residual_ext[:, 2 : slab_rows + 2]
    )
    back_full = all_gather_xy(back_rows.reshape(view_count * slab_rows, shard_width), xy_count)
    back_full = back_full.reshape(view_count, slab_rows, detector_width)
    back_band = jnp.stack(
        [
            lax.dynamic_slice(back_full[v], (jnp.int32(0), band_start[v, 0]), (slab_rows, B))
            for v in range(view_count)
        ]
    )

    own_rows = first_row + jnp.arange(slab_rows, dtype=jnp.int32)
    row_weight = (
        jnp.where(own_rows[None, :] > 0, axial_weight[0], 0.0)
        + axial_weight[1]
        + jnp.where(own_rows[None, :] < total_rows - 1, axial_weight[2], 0.0)
    )
    volume_next = backward_update(back_band, volume, amplitude, column_offset, column_width, row_weight)
    return (volume_next, residual)


def solution(mesh):
    return jax.shard_map(
        local,
        mesh=mesh,
        in_specs=(
            P("gz", "xy"),
            P(None, "gz", "xy"),
            P(None, "xy"),
            P(None, "xy"),
            P(None, "xy"),
            P(None, "xy"),
            P(None, None, "gz"),
        ),
        out_specs=(P("gz", "xy"), P(None, "gz", "xy")),
        check_vma=False,
    )
```

```python
import jax
import jax.numpy as jnp
from jax import lax
from jax.experimental import pallas as pl
from jax.experimental.pallas import tpu as pltpu
from jax.sharding import PartitionSpec as P

B = 512
RELAX = 0.9
CHUNK = 2048
INTERPRET = False


def _band_mask(off, wid, rows, width):
    u = lax.broadcasted_iota(jnp.int32, (rows, width), 0)
    inside = (u - off).astype(jnp.uint32) < wid.astype(jnp.uint32)
    return jnp.where(inside, 1.0, 0.0).astype(jnp.bfloat16)


def _split(x):
    hi = x.astype(jnp.bfloat16)
    lo = (x - hi.astype(jnp.float32)).astype(jnp.bfloat16)
    return hi, lo


def _forward_kernel(start_ref, vol_ref, amp_ref, off_ref, wid_ref, out_ref, acc_ref):
    slab_rows, columns = vol_ref.shape
    view_count = amp_ref.shape[0]
    band = acc_ref.shape[2]
    chunks, _, shard_width = out_ref.shape
    detector_width = chunks * shard_width
    acc_ref[...] = jnp.zeros(acc_ref.shape, jnp.float32)
    row = lax.broadcasted_iota(jnp.int32, (slab_rows, CHUNK), 0)

    def body(j, carry):
        c0 = pl.multiple_of(j * CHUNK, CHUNK)
        cells = vol_ref[:, pl.ds(c0, CHUNK)]
        for v in range(view_count):
            amp = amp_ref[pl.ds(v, 1), pl.ds(c0, CHUNK)]
            off = off_ref[pl.ds(v, 1), pl.ds(c0, CHUNK)]
            wid = wid_ref[pl.ds(v, 1), pl.ds(c0, CHUNK)]
            cells_hi, cells_lo = _split(cells * amp)
            amp_hi, amp_lo = _split(amp)
            amp_rows = jnp.where(
                row == 0,
                amp_hi.astype(jnp.float32),
                jnp.where(row == 1, amp_lo.astype(jnp.float32), 0.0),
            ).astype(jnp.bfloat16)
            lhs = jnp.concatenate([cells_hi, cells_lo, amp_rows], axis=0)
            mask = _band_mask(off, wid, band, CHUNK)
            acc_ref[v] += lax.dot_general(
                lhs, mask, (((1,), (1,)), ((), ())), preferred_element_type=jnp.float32
            )
        return carry

    lax.fori_loop(0, columns // CHUNK, body, 0)
    height = slab_rows + 1
    placed = []
    for v in range(view_count):
        acc = acc_ref[v]
        summed = jnp.concatenate(
            [
                acc[:slab_rows] + acc[slab_rows : 2 * slab_rows],
                acc[2 * slab_rows : 2 * slab_rows + 1] + acc[2 * slab_rows + 1 : 2 * slab_rows + 2],
            ],
            axis=0,
        )
        ext = jnp.concatenate([summed, jnp.zeros((height, detector_width - band), jnp.float32)], axis=1)
        placed.append(pltpu.roll(ext, start_ref[v, 0], 1))
    joined = jnp.concatenate(placed, axis=0)
    for k in range(chunks):
        out_ref[k] = joined[:, k * shard_width : (k + 1) * shard_width]


def forward_band(volume, amplitude, column_offset, column_width, band_start, chunks, shard_width):
    slab_rows = volume.shape[0]
    view_count = amplitude.shape[0]
    smem = pl.BlockSpec(memory_space=pltpu.SMEM)
    vmem = pl.BlockSpec(memory_space=pltpu.VMEM)
    return pl.pallas_call(
        _forward_kernel,
        out_shape=jax.ShapeDtypeStruct((chunks, view_count * (slab_rows + 1), shard_width), jnp.float32),
        in_specs=[smem, vmem, vmem, vmem, vmem],
        scratch_shapes=[pltpu.VMEM((view_count, 3 * slab_rows, B), jnp.float32)],
        cost_estimate=pl.CostEstimate(
            flops=2 * view_count * 3 * slab_rows * B * volume.shape[1],
            transcendentals=0,
            bytes_accessed=4 * (volume.size + 3 * amplitude.size),
        ),
        interpret=INTERPRET,
    )(band_start, volume, amplitude, column_offset, column_width)


def _backward_kernel(back_ref, vol_ref, amp_ref, off_ref, wid_ref, rw_ref, out_ref, split_ref):
    slab_rows, columns = vol_ref.shape
    view_count, _, band = back_ref.shape
    for v in range(view_count):
        hi, lo = _split(back_ref[v])
        split_ref[v] = jnp.concatenate([hi, lo], axis=0)

    def body(j, carry):
        c0 = pl.multiple_of(j * CHUNK, CHUNK)
        correction = None
        normalizer = None
        for v in range(view_count):
            amp = amp_ref[pl.ds(v, 1), pl.ds(c0, CHUNK)]
            off = off_ref[pl.ds(v, 1), pl.ds(c0, CHUNK)]
            wid = wid_ref[pl.ds(v, 1), pl.ds(c0, CHUNK)]
            mask = _band_mask(off, wid, band, CHUNK)
            r = jnp.dot(split_ref[v], mask, preferred_element_type=jnp.float32)
            part = amp * (r[:slab_rows] + r[slab_rows:])
            mass = rw_ref[v] * (amp * wid.astype(jnp.float32))
            correction = part if correction is None else correction + part
            normalizer = mass if normalizer is None else normalizer + mass
        cells = vol_ref[:, pl.ds(c0, CHUNK)]
        out_ref[:, pl.ds(c0, CHUNK)] = cells + RELAX * correction / normalizer
        return carry

    lax.fori_loop(0, columns // CHUNK, body, 0)


def backward_update(back_band, volume, amplitude, column_offset, column_width, row_weight):
    view_count, slab_rows, band = back_band.shape
    return pl.pallas_call(
        _backward_kernel,
        out_shape=jax.ShapeDtypeStruct(volume.shape, jnp.float32),
        scratch_shapes=[pltpu.VMEM((view_count, 2 * slab_rows, band), jnp.bfloat16)],
        interpret=INTERPRET,
    )(back_band, volume, amplitude, column_offset, column_width, row_weight[:, :, None])


def _bit_count(count):
    bits = count.bit_length() - 1
    assert 1 << bits == count
    return bits


def reduce_scatter_xy(x, count):
    _, rows, width = x.shape
    bits = _bit_count(count)
    idx = lax.axis_index("xy")
    y = x.reshape((2,) * bits + (rows, width))
    for j in range(bits):
        axis = bits - 1 - j
        bit = (idx >> j) & 1
        keep = lax.dynamic_index_in_dim(y, bit, axis, keepdims=False)
        send = lax.dynamic_index_in_dim(y, 1 - bit, axis, keepdims=False)
        y = keep + lax.ppermute(send, "xy", [(i, i ^ (1 << j)) for i in range(count)])
    return y


def all_gather_xy(x, count):
    rows, width = x.shape
    bits = _bit_count(count)
    idx = lax.axis_index("xy")
    y = x
    for step, j in enumerate(reversed(range(bits))):
        bit = (idx >> j) & 1
        other = lax.ppermute(y, "xy", [(i, i ^ (1 << j)) for i in range(count)])
        low = jnp.where(bit == 0, y, other)
        high = jnp.where(bit == 0, other, y)
        y = jnp.stack([low, high], axis=step)
    return jnp.transpose(y.reshape(count, rows, width), (1, 0, 2)).reshape(rows, count * width)


def local(volume, measured, band_start, column_offset, column_width, amplitude, axial_weight):
    slab_rows = volume.shape[0]
    view_count = amplitude.shape[0]
    xy_count = lax.axis_size("xy")
    gz_count = lax.axis_size("gz")
    shard_width = measured.shape[2]
    detector_width = shard_width * xy_count
    total_rows = slab_rows * gz_count
    first_row = lax.axis_index("gz") * slab_rows
    up_pairs = [(i, i + 1) for i in range(gz_count - 1)]
    down_pairs = [(i + 1, i) for i in range(gz_count - 1)]

    def pack(meas_rows, weight_cols):
        flat = jnp.transpose(weight_cols, (1, 0, 2)).reshape(view_count, 1, -1)
        flat = jnp.pad(flat, ((0, 0), (0, 0), (0, shard_width - flat.shape[2])))
        return jnp.concatenate([meas_rows, flat], axis=1)

    def unpack(packed):
        cols = packed[:, 1, : 3 * 2].reshape(view_count, 3, 2)
        return packed[:, :1], jnp.transpose(cols, (1, 0, 2))

    gz_index = lax.axis_index("gz")

    def exchange(upward, downward):
        if gz_count != 2:
            return lax.ppermute(upward, "gz", up_pairs), lax.ppermute(downward, "gz", down_pairs)
        got = lax.ppermute(jnp.where(gz_index == 0, upward, downward), "gz", [(0, 1), (1, 0)])
        return jnp.where(gz_index == 1, got, 0.0), jnp.where(gz_index == 0, got, 0.0)


    placed = forward_band(volume, amplitude, column_offset, column_width, band_start, xy_count, shard_width)
    band_height = slab_rows + 1
    reduced = reduce_scatter_xy(placed, xy_count).reshape(view_count, band_height, shard_width)
    proj_cols = reduced[:, :slab_rows]
    cover = reduced[:, slab_rows : slab_rows + 1]
    from_below, from_above = exchange(
        jnp.concatenate(
            [proj_cols[:, slab_rows - 2 :], pack(measured[:, slab_rows - 1 :], axial_weight[:, :, slab_rows - 2 :])],
            axis=1,
        ),
        jnp.concatenate([proj_cols[:, :2], pack(measured[:, :1], axial_weight[:, :, :2])], axis=1),
    )
    proj_ext = jnp.concatenate([from_below[:, :2], proj_cols, from_above[:, :2]], axis=1)
    meas_below, weight_below = unpack(from_below[:, 2:])
    meas_above, weight_above = unpack(from_above[:, 2:])
    measured_ext = jnp.concatenate([meas_below, measured, meas_above], axis=1)
    weight_ext = jnp.concatenate([weight_below, axial_weight, weight_above], axis=2)

    ext_rows = slab_rows + 2
    mid_w = weight_ext[1, :, 1 : ext_rows + 1][:, :, None]
    next_w = weight_ext[0, :, 2 : ext_rows + 2][:, :, None]
    prev_w = weight_ext[2, :, 0:ext_rows][:, :, None]
    centre = proj_ext[:, 1 : ext_rows + 1]
    after = proj_ext[:, 2 : ext_rows + 2]
    before = proj_ext[:, 0:ext_rows]
    projection = mid_w * centre + next_w * after + prev_w * before
    coverage = mid_w * cover + next_w * cover + prev_w * cover
    residual_ext = (measured_ext - projection) / jnp.maximum(coverage, 1.0)
    global_rows = first_row - 1 + jnp.arange(ext_rows, dtype=jnp.int32)
    valid = (global_rows >= 0) & (global_rows < total_rows)
    residual_ext = jnp.where(valid[None, :, None], residual_ext, 0.0)
    residual = residual_ext[:, 1 : slab_rows + 1]

    back_rows = (
        axial_weight[0][:, :, None] * residual_ext[:, 0:slab_rows]
        + axial_weight[1][:, :, None] * residual
        + axial_weight[2][:, :, None] * residual_ext[:, 2 : slab_rows + 2]
    )
    back_full = all_gather_xy(back_rows.reshape(view_count * slab_rows, shard_width), xy_count)
    back_full = back_full.reshape(view_count, slab_rows, detector_width)
    back_band = jnp.stack(
        [
            lax.dynamic_slice(back_full[v], (jnp.int32(0), band_start[v, 0]), (slab_rows, B))
            for v in range(view_count)
        ]
    )

    own_rows = first_row + jnp.arange(slab_rows, dtype=jnp.int32)
    row_weight = (
        jnp.where(own_rows[None, :] > 0, axial_weight[0], 0.0)
        + axial_weight[1]
        + jnp.where(own_rows[None, :] < total_rows - 1, axial_weight[2], 0.0)
    )
    volume_next = backward_update(back_band, volume, amplitude, column_offset, column_width, row_weight)
    return (volume_next, residual)


def solution(mesh):
    return jax.shard_map(
        local,
        mesh=mesh,
        in_specs=(
            P("gz", "xy"),
            P(None, "gz", "xy"),
            P(None, "xy"),
            P(None, "xy"),
            P(None, "xy"),
            P(None, "xy"),
            P(None, None, "gz"),
        ),
        out_specs=(P("gz", "xy"), P(None, "gz", "xy")),
        check_vma=False,
    )
```

```python
import jax
import jax.numpy as jnp
from jax import lax
from jax.experimental import pallas as pl
from jax.experimental.pallas import tpu as pltpu
from jax.sharding import PartitionSpec as P

B = 512
RELAX = 0.9
CHUNK = 2048
INTERPRET = False


def _band_mask(off, wid, rows, width):
    u = lax.broadcasted_iota(jnp.int32, (rows, width), 0)
    inside = (u - off).astype(jnp.uint32) < wid.astype(jnp.uint32)
    return jnp.where(inside, 1.0, 0.0).astype(jnp.bfloat16)


def _split(x):
    hi = x.astype(jnp.bfloat16)
    lo = (x - hi.astype(jnp.float32)).astype(jnp.bfloat16)
    return hi, lo


def _forward_kernel(start_ref, vol_ref, amp_ref, off_ref, wid_ref, out_ref, acc_ref):
    slab_rows, columns = vol_ref.shape
    view_count = amp_ref.shape[0]
    band = acc_ref.shape[2]
    chunks, _, shard_width = out_ref.shape
    detector_width = chunks * shard_width
    acc_ref[...] = jnp.zeros(acc_ref.shape, jnp.float32)
    row = lax.broadcasted_iota(jnp.int32, (slab_rows, CHUNK), 0)

    def body(j, carry):
        c0 = pl.multiple_of(j * CHUNK, CHUNK)
        cells = vol_ref[:, pl.ds(c0, CHUNK)]
        for v in range(view_count):
            amp = amp_ref[pl.ds(v, 1), pl.ds(c0, CHUNK)]
            off = off_ref[pl.ds(v, 1), pl.ds(c0, CHUNK)]
            wid = wid_ref[pl.ds(v, 1), pl.ds(c0, CHUNK)]
            cells_hi, cells_lo = _split(cells * amp)
            amp_hi, amp_lo = _split(amp)
            amp_rows = jnp.where(
                row == 0,
                amp_hi.astype(jnp.float32),
                jnp.where(row == 1, amp_lo.astype(jnp.float32), 0.0),
            ).astype(jnp.bfloat16)
            lhs = jnp.concatenate([cells_hi, cells_lo, amp_rows], axis=0)
            mask = _band_mask(off, wid, band, CHUNK)
            acc_ref[v] += lax.dot_general(
                lhs, mask, (((1,), (1,)), ((), ())), preferred_element_type=jnp.float32
            )
        return carry

    lax.fori_loop(0, columns // CHUNK, body, 0)
    height = slab_rows + 1
    placed = []
    for v in range(view_count):
        acc = acc_ref[v]
        summed = jnp.concatenate(
            [
                acc[:slab_rows] + acc[slab_rows : 2 * slab_rows],
                acc[2 * slab_rows : 2 * slab_rows + 1] + acc[2 * slab_rows + 1 : 2 * slab_rows + 2],
            ],
            axis=0,
        )
        ext = jnp.concatenate([summed, jnp.zeros((height, detector_width - band), jnp.float32)], axis=1)
        placed.append(pltpu.roll(ext, start_ref[v], 1))
    joined = jnp.concatenate(placed, axis=0)
    for k in range(chunks):
        out_ref[k] = joined[:, k * shard_width : (k + 1) * shard_width]


def forward_band(volume, amplitude, column_offset, column_width, band_start, chunks, shard_width):
    slab_rows = volume.shape[0]
    view_count = amplitude.shape[0]
    smem = pl.BlockSpec(memory_space=pltpu.SMEM)
    vmem = pl.BlockSpec(memory_space=pltpu.VMEM)
    return pl.pallas_call(
        _forward_kernel,
        out_shape=jax.ShapeDtypeStruct((chunks, view_count * (slab_rows + 1), shard_width), jnp.float32),
        in_specs=[smem, vmem, vmem, vmem, vmem],
        scratch_shapes=[pltpu.VMEM((view_count, 3 * slab_rows, B), jnp.float32)],
        cost_estimate=pl.CostEstimate(
            flops=2 * view_count * 3 * slab_rows * B * volume.shape[1],
            transcendentals=0,
            bytes_accessed=4 * (volume.size + 3 * amplitude.size),
        ),
        interpret=INTERPRET,
    )(band_start.reshape(-1), volume, amplitude, column_offset, column_width)


def _backward_kernel(back_ref, vol_ref, amp_ref, off_ref, wid_ref, rw_ref, out_ref, split_ref):
    slab_rows, columns = vol_ref.shape
    view_count, _, band = back_ref.shape
    for v in range(view_count):
        hi, lo = _split(back_ref[v])
        split_ref[v] = jnp.concatenate([hi, lo], axis=0)

    def body(j, carry):
        c0 = pl.multiple_of(j * CHUNK, CHUNK)
        correction = None
        normalizer = None
        for v in range(view_count):
            amp = amp_ref[pl.ds(v, 1), pl.ds(c0, CHUNK)]
            off = off_ref[pl.ds(v, 1), pl.ds(c0, CHUNK)]
            wid = wid_ref[pl.ds(v, 1), pl.ds(c0, CHUNK)]
            mask = _band_mask(off, wid, band, CHUNK)
            r = jnp.dot(split_ref[v], mask, preferred_element_type=jnp.float32)
            part = amp * (r[:slab_rows] + r[slab_rows:])
            mass = rw_ref[v] * (amp * wid.astype(jnp.float32))
            correction = part if correction is None else correction + part
            normalizer = mass if normalizer is None else normalizer + mass
        cells = vol_ref[:, pl.ds(c0, CHUNK)]
        out_ref[:, pl.ds(c0, CHUNK)] = cells + RELAX * correction / normalizer
        return carry

    lax.fori_loop(0, columns // CHUNK, body, 0)


def backward_update(back_band, volume, amplitude, column_offset, column_width, row_weight):
    view_count, slab_rows, band = back_band.shape
    return pl.pallas_call(
        _backward_kernel,
        out_shape=jax.ShapeDtypeStruct(volume.shape, jnp.float32),
        scratch_shapes=[pltpu.VMEM((view_count, 2 * slab_rows, band), jnp.bfloat16)],
        interpret=INTERPRET,
    )(back_band, volume, amplitude, column_offset, column_width, row_weight[:, :, None])


def _bit_count(count):
    bits = count.bit_length() - 1
    assert 1 << bits == count
    return bits


def reduce_scatter_xy(x, count):
    _, rows, width = x.shape
    bits = _bit_count(count)
    idx = lax.axis_index("xy")
    y = x.reshape((2,) * bits + (rows, width))
    for j in range(bits):
        axis = bits - 1 - j
        bit = (idx >> j) & 1
        keep = lax.dynamic_index_in_dim(y, bit, axis, keepdims=False)
        send = lax.dynamic_index_in_dim(y, 1 - bit, axis, keepdims=False)
        y = keep + lax.ppermute(send, "xy", [(i, i ^ (1 << j)) for i in range(count)])
    return y


def all_gather_xy(x, count):
    rows, width = x.shape
    bits = _bit_count(count)
    idx = lax.axis_index("xy")
    y = x
    for step, j in enumerate(reversed(range(bits))):
        bit = (idx >> j) & 1
        other = lax.ppermute(y, "xy", [(i, i ^ (1 << j)) for i in range(count)])
        low = jnp.where(bit == 0, y, other)
        high = jnp.where(bit == 0, other, y)
        y = jnp.stack([low, high], axis=step)
    return jnp.transpose(y.reshape(count, rows, width), (1, 0, 2)).reshape(rows, count * width)


def local(volume, measured, band_start, column_offset, column_width, amplitude, axial_weight):
    slab_rows = volume.shape[0]
    view_count = amplitude.shape[0]
    xy_count = lax.axis_size("xy")
    gz_count = lax.axis_size("gz")
    shard_width = measured.shape[2]
    detector_width = shard_width * xy_count
    total_rows = slab_rows * gz_count
    first_row = lax.axis_index("gz") * slab_rows
    up_pairs = [(i, i + 1) for i in range(gz_count - 1)]
    down_pairs = [(i + 1, i) for i in range(gz_count - 1)]

    def pack(meas_rows, weight_cols):
        flat = jnp.transpose(weight_cols, (1, 0, 2)).reshape(view_count, 1, -1)
        flat = jnp.pad(flat, ((0, 0), (0, 0), (0, shard_width - flat.shape[2])))
        return jnp.concatenate([meas_rows, flat], axis=1)

    def unpack(packed):
        cols = packed[:, 1, : 3 * 2].reshape(view_count, 3, 2)
        return packed[:, :1], jnp.transpose(cols, (1, 0, 2))

    gz_index = lax.axis_index("gz")

    def exchange(upward, downward):
        if gz_count != 2:
            return lax.ppermute(upward, "gz", up_pairs), lax.ppermute(downward, "gz", down_pairs)
        got = lax.ppermute(jnp.where(gz_index == 0, upward, downward), "gz", [(0, 1), (1, 0)])
        return jnp.where(gz_index == 1, got, 0.0), jnp.where(gz_index == 0, got, 0.0)

    from_below, from_above = exchange(
        pack(measured[:, slab_rows - 1 :], axial_weight[:, :, slab_rows - 2 :]),
        pack(measured[:, :1], axial_weight[:, :, :2]),
    )
    meas_below, weight_below = unpack(from_below)
    meas_above, weight_above = unpack(from_above)
    measured_ext = jnp.concatenate([meas_below, measured, meas_above], axis=1)
    weight_ext = jnp.concatenate([weight_below, axial_weight, weight_above], axis=2)

    placed = forward_band(volume, amplitude, column_offset, column_width, band_start, xy_count, shard_width)
    band_height = slab_rows + 1
    reduced = reduce_scatter_xy(placed, xy_count).reshape(view_count, band_height, shard_width)
    proj_cols = reduced[:, :slab_rows]
    cover = reduced[:, slab_rows : slab_rows + 1]
    proj_below, proj_above = exchange(proj_cols[:, slab_rows - 2 :], proj_cols[:, :2])
    proj_ext = jnp.concatenate([proj_below, proj_cols, proj_above], axis=1)

    ext_rows = slab_rows + 2
    mid_w = weight_ext[1, :, 1 : ext_rows + 1][:, :, None]
    next_w = weight_ext[0, :, 2 : ext_rows + 2][:, :, None]
    prev_w = weight_ext[2, :, 0:ext_rows][:, :, None]
    centre = proj_ext[:, 1 : ext_rows + 1]
    after = proj_ext[:, 2 : ext_rows + 2]
    before = proj_ext[:, 0:ext_rows]
    projection = mid_w * centre + next_w * after + prev_w * before
    coverage = mid_w * cover + next_w * cover + prev_w * cover
    residual_ext = (measured_ext - projection) / jnp.maximum(coverage, 1.0)
    global_rows = first_row - 1 + jnp.arange(ext_rows, dtype=jnp.int32)
    valid = (global_rows >= 0) & (global_rows < total_rows)
    residual_ext = jnp.where(valid[None, :, None], residual_ext, 0.0)
    residual = residual_ext[:, 1 : slab_rows + 1]

    back_rows = (
        axial_weight[0][:, :, None] * residual_ext[:, 0:slab_rows]
        + axial_weight[1][:, :, None] * residual
        + axial_weight[2][:, :, None] * residual_ext[:, 2 : slab_rows + 2]
    )
    back_full = all_gather_xy(back_rows.reshape(view_count * slab_rows, shard_width), xy_count)
    back_full = back_full.reshape(view_count, slab_rows, detector_width)
    back_band = jnp.stack(
        [
            lax.dynamic_slice(back_full[v], (jnp.int32(0), band_start[v, 0]), (slab_rows, B))
            for v in range(view_count)
        ]
    )

    own_rows = first_row + jnp.arange(slab_rows, dtype=jnp.int32)
    row_weight = (
        jnp.where(own_rows[None, :] > 0, axial_weight[0], 0.0)
        + axial_weight[1]
        + jnp.where(own_rows[None, :] < total_rows - 1, axial_weight[2], 0.0)
    )
    volume_next = backward_update(back_band, volume, amplitude, column_offset, column_width, row_weight)
    return (volume_next, residual)


def solution(mesh):
    return jax.shard_map(
        local,
        mesh=mesh,
        in_specs=(
            P("gz", "xy"),
            P(None, "gz", "xy"),
            P(None, "xy"),
            P(None, "xy"),
            P(None, "xy"),
            P(None, "xy"),
            P(None, None, "gz"),
        ),
        out_specs=(P("gz", "xy"), P(None, "gz", "xy")),
        check_vma=False,
    )
```

```python
import jax
import jax.numpy as jnp
from jax import lax
from jax.experimental import pallas as pl
from jax.experimental.pallas import tpu as pltpu
from jax.sharding import PartitionSpec as P

B = 512
RELAX = 0.9
CHUNK = 2048
INTERPRET = False


def _band_mask(off, wid, rows, width):
    u = lax.broadcasted_iota(jnp.int32, (rows, width), 0)
    inside = (u - off).astype(jnp.uint32) < wid.astype(jnp.uint32)
    return jnp.where(inside, 1.0, 0.0).astype(jnp.bfloat16)


def _split(x):
    hi = x.astype(jnp.bfloat16)
    lo = (x - hi.astype(jnp.float32)).astype(jnp.bfloat16)
    return hi, lo


def _forward_kernel(start_ref, vol_ref, amp_ref, off_ref, wid_ref, out_ref, acc_ref):
    slab_rows, columns = vol_ref.shape
    view_count = amp_ref.shape[0]
    band = acc_ref.shape[2]
    _, half, _, shard_width = out_ref.shape
    chunks = 2 * half
    detector_width = chunks * shard_width
    acc_ref[...] = jnp.zeros(acc_ref.shape, jnp.float32)
    row = lax.broadcasted_iota(jnp.int32, (slab_rows, CHUNK), 0)

    def body(j, carry):
        c0 = pl.multiple_of(j * CHUNK, CHUNK)
        cells = vol_ref[:, pl.ds(c0, CHUNK)]
        for v in range(view_count):
            amp = amp_ref[pl.ds(v, 1), pl.ds(c0, CHUNK)]
            off = off_ref[pl.ds(v, 1), pl.ds(c0, CHUNK)]
            wid = wid_ref[pl.ds(v, 1), pl.ds(c0, CHUNK)]
            cells_hi, cells_lo = _split(cells * amp)
            amp_hi, amp_lo = _split(amp)
            amp_rows = jnp.where(
                row == 0,
                amp_hi.astype(jnp.float32),
                jnp.where(row == 1, amp_lo.astype(jnp.float32), 0.0),
            ).astype(jnp.bfloat16)
            lhs = jnp.concatenate([cells_hi, cells_lo, amp_rows], axis=0)
            mask = _band_mask(off, wid, band, CHUNK)
            acc_ref[v] += lax.dot_general(
                lhs, mask, (((1,), (1,)), ((), ())), preferred_element_type=jnp.float32
            )
        return carry

    lax.fori_loop(0, columns // CHUNK, body, 0)
    height = slab_rows + 1
    placed = []
    for v in range(view_count):
        acc = acc_ref[v]
        summed = jnp.concatenate(
            [
                acc[:slab_rows] + acc[slab_rows : 2 * slab_rows],
                acc[2 * slab_rows : 2 * slab_rows + 1] + acc[2 * slab_rows + 1 : 2 * slab_rows + 2],
            ],
            axis=0,
        )
        ext = jnp.concatenate([summed, jnp.zeros((height, detector_width - band), jnp.float32)], axis=1)
        placed.append(pltpu.roll(ext, start_ref[v], 1))
    joined = jnp.concatenate(placed, axis=0)
    parity = lax.axis_index("xy") & 1
    for k in range(chunks):
        out_ref[(k % 2) ^ parity, k // 2] = joined[:, k * shard_width : (k + 1) * shard_width]


def forward_band(volume, amplitude, column_offset, column_width, band_start, chunks, shard_width):
    slab_rows = volume.shape[0]
    view_count = amplitude.shape[0]
    smem = pl.BlockSpec(memory_space=pltpu.SMEM)
    vmem = pl.BlockSpec(memory_space=pltpu.VMEM)
    return pl.pallas_call(
        _forward_kernel,
        out_shape=jax.ShapeDtypeStruct((2, chunks // 2, view_count * (slab_rows + 1), shard_width), jnp.float32),
        in_specs=[smem, vmem, vmem, vmem, vmem],
        scratch_shapes=[pltpu.VMEM((view_count, 3 * slab_rows, B), jnp.float32)],
        cost_estimate=pl.CostEstimate(
            flops=2 * view_count * 3 * slab_rows * B * volume.shape[1],
            transcendentals=0,
            bytes_accessed=4 * (volume.size + 3 * amplitude.size),
        ),
        interpret=INTERPRET,
    )(band_start.reshape(-1), volume, amplitude, column_offset, column_width)


def _backward_kernel(back_ref, vol_ref, amp_ref, off_ref, wid_ref, rw_ref, out_ref, split_ref):
    slab_rows, columns = vol_ref.shape
    view_count, _, band = back_ref.shape
    for v in range(view_count):
        hi, lo = _split(back_ref[v])
        split_ref[v] = jnp.concatenate([hi, lo], axis=0)

    def body(j, carry):
        c0 = pl.multiple_of(j * CHUNK, CHUNK)
        correction = None
        normalizer = None
        for v in range(view_count):
            amp = amp_ref[pl.ds(v, 1), pl.ds(c0, CHUNK)]
            off = off_ref[pl.ds(v, 1), pl.ds(c0, CHUNK)]
            wid = wid_ref[pl.ds(v, 1), pl.ds(c0, CHUNK)]
            mask = _band_mask(off, wid, band, CHUNK)
            r = jnp.dot(split_ref[v], mask, preferred_element_type=jnp.float32)
            part = amp * (r[:slab_rows] + r[slab_rows:])
            mass = rw_ref[v] * (amp * wid.astype(jnp.float32))
            correction = part if correction is None else correction + part
            normalizer = mass if normalizer is None else normalizer + mass
        cells = vol_ref[:, pl.ds(c0, CHUNK)]
        out_ref[:, pl.ds(c0, CHUNK)] = cells + RELAX * correction / normalizer
        return carry

    lax.fori_loop(0, columns // CHUNK, body, 0)


def backward_update(back_band, volume, amplitude, column_offset, column_width, row_weight):
    view_count, slab_rows, band = back_band.shape
    return pl.pallas_call(
        _backward_kernel,
        out_shape=jax.ShapeDtypeStruct(volume.shape, jnp.float32),
        scratch_shapes=[pltpu.VMEM((view_count, 2 * slab_rows, band), jnp.bfloat16)],
        interpret=INTERPRET,
    )(back_band, volume, amplitude, column_offset, column_width, row_weight[:, :, None])


def _bit_count(count):
    bits = count.bit_length() - 1
    assert 1 << bits == count
    return bits


def reduce_scatter_xy(halves, count):
    _, _, rows, width = halves.shape
    bits = _bit_count(count)
    idx = lax.axis_index("xy")
    y = halves[0] + lax.ppermute(halves[1], "xy", [(i, i ^ 1) for i in range(count)])
    y = y.reshape((2,) * (bits - 1) + (rows, width))
    for j in range(1, bits):
        axis = bits - 1 - j
        bit = (idx >> j) & 1
        keep = lax.dynamic_index_in_dim(y, bit, axis, keepdims=False)
        send = lax.dynamic_index_in_dim(y, 1 - bit, axis, keepdims=False)
        y = keep + lax.ppermute(send, "xy", [(i, i ^ (1 << j)) for i in range(count)])
    return y


def all_gather_xy(x, count):
    rows, width = x.shape
    bits = _bit_count(count)
    idx = lax.axis_index("xy")
    y = x
    for step, j in enumerate(reversed(range(bits))):
        bit = (idx >> j) & 1
        other = lax.ppermute(y, "xy", [(i, i ^ (1 << j)) for i in range(count)])
        low = jnp.where(bit == 0, y, other)
        high = jnp.where(bit == 0, other, y)
        y = jnp.stack([low, high], axis=step)
    return jnp.transpose(y.reshape(count, rows, width), (1, 0, 2)).reshape(rows, count * width)


def local(volume, measured, band_start, column_offset, column_width, amplitude, axial_weight):
    slab_rows = volume.shape[0]
    view_count = amplitude.shape[0]
    xy_count = lax.axis_size("xy")
    gz_count = lax.axis_size("gz")
    shard_width = measured.shape[2]
    detector_width = shard_width * xy_count
    total_rows = slab_rows * gz_count
    first_row = lax.axis_index("gz") * slab_rows
    up_pairs = [(i, i + 1) for i in range(gz_count - 1)]
    down_pairs = [(i + 1, i) for i in range(gz_count - 1)]

    def pack(meas_rows, weight_cols):
        flat = jnp.transpose(weight_cols, (1, 0, 2)).reshape(view_count, 1, -1)
        flat = jnp.pad(flat, ((0, 0), (0, 0), (0, shard_width - flat.shape[2])))
        return jnp.concatenate([meas_rows, flat], axis=1)

    def unpack(packed):
        cols = packed[:, 1, : 3 * 2].reshape(view_count, 3, 2)
        return packed[:, :1], jnp.transpose(cols, (1, 0, 2))

    gz_index = lax.axis_index("gz")

    def exchange(upward, downward):
        if gz_count != 2:
            return lax.ppermute(upward, "gz", up_pairs), lax.ppermute(downward, "gz", down_pairs)
        got = lax.ppermute(jnp.where(gz_index == 0, upward, downward), "gz", [(0, 1), (1, 0)])
        return jnp.where(gz_index == 1, got, 0.0), jnp.where(gz_index == 0, got, 0.0)

    from_below, from_above = exchange(
        pack(measured[:, slab_rows - 1 :], axial_weight[:, :, slab_rows - 2 :]),
        pack(measured[:, :1], axial_weight[:, :, :2]),
    )
    meas_below, weight_below = unpack(from_below)
    meas_above, weight_above = unpack(from_above)
    measured_ext = jnp.concatenate([meas_below, measured, meas_above], axis=1)
    weight_ext = jnp.concatenate([weight_below, axial_weight, weight_above], axis=2)

    placed = forward_band(volume, amplitude, column_offset, column_width, band_start, xy_count, shard_width)
    band_height = slab_rows + 1
    reduced = reduce_scatter_xy(placed, xy_count).reshape(view_count, band_height, shard_width)
    proj_cols = reduced[:, :slab_rows]
    cover = reduced[:, slab_rows : slab_rows + 1]
    proj_below, proj_above = exchange(proj_cols[:, slab_rows - 2 :], proj_cols[:, :2])
    proj_ext = jnp.concatenate([proj_below, proj_cols, proj_above], axis=1)

    ext_rows = slab_rows + 2
    mid_w = weight_ext[1, :, 1 : ext_rows + 1][:, :, None]
    next_w = weight_ext[0, :, 2 : ext_rows + 2][:, :, None]
    prev_w = weight_ext[2, :, 0:ext_rows][:, :, None]
    centre = proj_ext[:, 1 : ext_rows + 1]
    after = proj_ext[:, 2 : ext_rows + 2]
    before = proj_ext[:, 0:ext_rows]
    projection = mid_w * centre + next_w * after + prev_w * before
    coverage = mid_w * cover + next_w * cover + prev_w * cover
    residual_ext = (measured_ext - projection) / jnp.maximum(coverage, 1.0)
    global_rows = first_row - 1 + jnp.arange(ext_rows, dtype=jnp.int32)
    valid = (global_rows >= 0) & (global_rows < total_rows)
    residual_ext = jnp.where(valid[None, :, None], residual_ext, 0.0)
    residual = residual_ext[:, 1 : slab_rows + 1]

    back_rows = (
        axial_weight[0][:, :, None] * residual_ext[:, 0:slab_rows]
        + axial_weight[1][:, :, None] * residual
        + axial_weight[2][:, :, None] * residual_ext[:, 2 : slab_rows + 2]
    )
    back_full = all_gather_xy(back_rows.reshape(view_count * slab_rows, shard_width), xy_count)
    back_full = back_full.reshape(view_count, slab_rows, detector_width)
    back_band = jnp.stack(
        [
            lax.dynamic_slice(back_full[v], (jnp.int32(0), band_start[v, 0]), (slab_rows, B))
            for v in range(view_count)
        ]
    )

    own_rows = first_row + jnp.arange(slab_rows, dtype=jnp.int32)
    row_weight = (
        jnp.where(own_rows[None, :] > 0, axial_weight[0], 0.0)
        + axial_weight[1]
        + jnp.where(own_rows[None, :] < total_rows - 1, axial_weight[2], 0.0)
    )
    volume_next = backward_update(back_band, volume, amplitude, column_offset, column_width, row_weight)
    return (volume_next, residual)


def solution(mesh):
    return jax.shard_map(
        local,
        mesh=mesh,
        in_specs=(
            P("gz", "xy"),
            P(None, "gz", "xy"),
            P(None, "xy"),
            P(None, "xy"),
            P(None, "xy"),
            P(None, "xy"),
            P(None, None, "gz"),
        ),
        out_specs=(P("gz", "xy"), P(None, "gz", "xy")),
        check_vma=False,
    )
```

```python
import jax
import jax.numpy as jnp
from jax import lax
from jax.experimental import pallas as pl
from jax.experimental.pallas import tpu as pltpu
from jax.sharding import PartitionSpec as P

B = 512
RELAX = 0.9
CHUNK = 2048
INTERPRET = False


def _band_mask(off, wid, rows, width):
    u = lax.broadcasted_iota(jnp.int32, (rows, width), 0)
    inside = (u - off).astype(jnp.uint32) < wid.astype(jnp.uint32)
    return jnp.where(inside, 1.0, 0.0).astype(jnp.bfloat16)


def _split(x):
    hi = x.astype(jnp.bfloat16)
    lo = (x - hi.astype(jnp.float32)).astype(jnp.bfloat16)
    return hi, lo


def _forward_kernel(start_ref, vol_ref, amp_ref, off_ref, wid_ref, out_ref, acc_ref):
    slab_rows, columns = vol_ref.shape
    view_count = amp_ref.shape[0]
    band = acc_ref.shape[2]
    chunks, _, shard_width = out_ref.shape
    detector_width = chunks * shard_width
    acc_ref[...] = jnp.zeros(acc_ref.shape, jnp.float32)
    row = lax.broadcasted_iota(jnp.int32, (slab_rows, CHUNK), 0)

    def body(j, carry):
        c0 = pl.multiple_of(j * CHUNK, CHUNK)
        cells = vol_ref[:, pl.ds(c0, CHUNK)]
        for v in range(view_count):
            amp = amp_ref[pl.ds(v, 1), pl.ds(c0, CHUNK)]
            off = off_ref[pl.ds(v, 1), pl.ds(c0, CHUNK)]
            wid = wid_ref[pl.ds(v, 1), pl.ds(c0, CHUNK)]
            cells_hi, cells_lo = _split(cells * amp)
            amp_hi, amp_lo = _split(amp)
            amp_rows = jnp.where(
                row == 0,
                amp_hi.astype(jnp.float32),
                jnp.where(row == 1, amp_lo.astype(jnp.float32), 0.0),
            ).astype(jnp.bfloat16)
            lhs = jnp.concatenate([cells_hi, cells_lo, amp_rows], axis=0)
            mask = _band_mask(off, wid, band, CHUNK)
            acc_ref[v] += lax.dot_general(
                lhs, mask, (((1,), (1,)), ((), ())), preferred_element_type=jnp.float32
            )
        return carry

    lax.fori_loop(0, columns // CHUNK, body, 0)
    height = slab_rows + 1
    placed = []
    for v in range(view_count):
        acc = acc_ref[v]
        summed = jnp.concatenate(
            [
                acc[:slab_rows] + acc[slab_rows : 2 * slab_rows],
                acc[2 * slab_rows : 2 * slab_rows + 1] + acc[2 * slab_rows + 1 : 2 * slab_rows + 2],
            ],
            axis=0,
        )
        ext = jnp.concatenate([summed, jnp.zeros((height, detector_width - band), jnp.float32)], axis=1)
        placed.append(pltpu.roll(ext, start_ref[v], 1))
    joined = jnp.concatenate(placed, axis=0)
    for k in range(chunks):
        out_ref[k] = joined[:, k * shard_width : (k + 1) * shard_width]


def forward_band(volume, amplitude, column_offset, column_width, band_start, chunks, shard_width):
    slab_rows = volume.shape[0]
    view_count = amplitude.shape[0]
    smem = pl.BlockSpec(memory_space=pltpu.SMEM)
    vmem = pl.BlockSpec(memory_space=pltpu.VMEM)
    return pl.pallas_call(
        _forward_kernel,
        out_shape=jax.ShapeDtypeStruct((chunks, view_count * (slab_rows + 1), shard_width), jnp.float32),
        in_specs=[smem, vmem, vmem, vmem, vmem],
        scratch_shapes=[pltpu.VMEM((view_count, 3 * slab_rows, B), jnp.float32)],
        cost_estimate=pl.CostEstimate(
            flops=2 * view_count * 3 * slab_rows * B * volume.shape[1],
            transcendentals=0,
            bytes_accessed=4 * (volume.size + 3 * amplitude.size),
        ),
        interpret=INTERPRET,
    )(band_start.reshape(-1), volume, amplitude, column_offset, column_width)


def _backward_kernel(start_ref, back_ref, vol_ref, amp_ref, off_ref, wid_ref, rw_ref, out_ref, split_ref):
    slab_rows, columns = vol_ref.shape
    view_count, _, band = split_ref.shape
    chunks = back_ref.shape[0]
    detector_width = chunks * back_ref.shape[2]
    for v in range(view_count):
        rows = slice(v * slab_rows, (v + 1) * slab_rows)
        full = jnp.concatenate([back_ref[k, rows, :] for k in range(chunks)], axis=1)
        rolled = pltpu.roll(full, (detector_width - start_ref[v]) % detector_width, 1)
        hi, lo = _split(rolled[:, :band])
        split_ref[v] = jnp.concatenate([hi, lo], axis=0)

    def body(j, carry):
        c0 = pl.multiple_of(j * CHUNK, CHUNK)
        correction = None
        normalizer = None
        for v in range(view_count):
            amp = amp_ref[pl.ds(v, 1), pl.ds(c0, CHUNK)]
            off = off_ref[pl.ds(v, 1), pl.ds(c0, CHUNK)]
            wid = wid_ref[pl.ds(v, 1), pl.ds(c0, CHUNK)]
            mask = _band_mask(off, wid, band, CHUNK)
            r = jnp.dot(split_ref[v], mask, preferred_element_type=jnp.float32)
            part = amp * (r[:slab_rows] + r[slab_rows:])
            mass = rw_ref[v] * (amp * wid.astype(jnp.float32))
            correction = part if correction is None else correction + part
            normalizer = mass if normalizer is None else normalizer + mass
        cells = vol_ref[:, pl.ds(c0, CHUNK)]
        out_ref[:, pl.ds(c0, CHUNK)] = cells + RELAX * correction / normalizer
        return carry

    lax.fori_loop(0, columns // CHUNK, body, 0)


def backward_update(back_chunks, band_start, volume, amplitude, column_offset, column_width, row_weight):
    view_count = amplitude.shape[0]
    slab_rows = volume.shape[0]
    smem = pl.BlockSpec(memory_space=pltpu.SMEM)
    vmem = pl.BlockSpec(memory_space=pltpu.VMEM)
    return pl.pallas_call(
        _backward_kernel,
        out_shape=jax.ShapeDtypeStruct(volume.shape, jnp.float32),
        in_specs=[smem] + [vmem] * 6,
        scratch_shapes=[pltpu.VMEM((view_count, 2 * slab_rows, B), jnp.bfloat16)],
        interpret=INTERPRET,
    )(band_start.reshape(-1), back_chunks, volume, amplitude, column_offset, column_width, row_weight[:, :, None])


def _bit_count(count):
    bits = count.bit_length() - 1
    assert 1 << bits == count
    return bits


def reduce_scatter_xy(x, count):
    _, rows, width = x.shape
    bits = _bit_count(count)
    idx = lax.axis_index("xy")
    y = x.reshape((2,) * bits + (rows, width))
    for j in range(bits):
        axis = bits - 1 - j
        bit = (idx >> j) & 1
        keep = lax.dynamic_index_in_dim(y, bit, axis, keepdims=False)
        send = lax.dynamic_index_in_dim(y, 1 - bit, axis, keepdims=False)
        y = keep + lax.ppermute(send, "xy", [(i, i ^ (1 << j)) for i in range(count)])
    return y


def all_gather_xy(x, count):
    rows, width = x.shape
    bits = _bit_count(count)
    idx = lax.axis_index("xy")
    y = x
    for step, j in enumerate(reversed(range(bits))):
        bit = (idx >> j) & 1
        other = lax.ppermute(y, "xy", [(i, i ^ (1 << j)) for i in range(count)])
        low = jnp.where(bit == 0, y, other)
        high = jnp.where(bit == 0, other, y)
        y = jnp.stack([low, high], axis=step)
    return y.reshape(count, rows, width)


def local(volume, measured, band_start, column_offset, column_width, amplitude, axial_weight):
    slab_rows = volume.shape[0]
    view_count = amplitude.shape[0]
    xy_count = lax.axis_size("xy")
    gz_count = lax.axis_size("gz")
    shard_width = measured.shape[2]
    detector_width = shard_width * xy_count
    total_rows = slab_rows * gz_count
    first_row = lax.axis_index("gz") * slab_rows
    up_pairs = [(i, i + 1) for i in range(gz_count - 1)]
    down_pairs = [(i + 1, i) for i in range(gz_count - 1)]

    def pack(meas_rows, weight_cols):
        flat = jnp.transpose(weight_cols, (1, 0, 2)).reshape(view_count, 1, -1)
        flat = jnp.pad(flat, ((0, 0), (0, 0), (0, shard_width - flat.shape[2])))
        return jnp.concatenate([meas_rows, flat], axis=1)

    def unpack(packed):
        cols = packed[:, 1, : 3 * 2].reshape(view_count, 3, 2)
        return packed[:, :1], jnp.transpose(cols, (1, 0, 2))

    gz_index = lax.axis_index("gz")

    def exchange(upward, downward):
        if gz_count != 2:
            return lax.ppermute(upward, "gz", up_pairs), lax.ppermute(downward, "gz", down_pairs)
        got = lax.ppermute(jnp.where(gz_index == 0, upward, downward), "gz", [(0, 1), (1, 0)])
        return jnp.where(gz_index == 1, got, 0.0), jnp.where(gz_index == 0, got, 0.0)

    from_below, from_above = exchange(
        pack(measured[:, slab_rows - 1 :], axial_weight[:, :, slab_rows - 2 :]),
        pack(measured[:, :1], axial_weight[:, :, :2]),
    )
    meas_below, weight_below = unpack(from_below)
    meas_above, weight_above = unpack(from_above)
    measured_ext = jnp.concatenate([meas_below, measured, meas_above], axis=1)
    weight_ext = jnp.concatenate([weight_below, axial_weight, weight_above], axis=2)

    placed = forward_band(volume, amplitude, column_offset, column_width, band_start, xy_count, shard_width)
    band_height = slab_rows + 1
    reduced = reduce_scatter_xy(placed, xy_count).reshape(view_count, band_height, shard_width)
    proj_cols = reduced[:, :slab_rows]
    cover = reduced[:, slab_rows : slab_rows + 1]
    proj_below, proj_above = exchange(proj_cols[:, slab_rows - 2 :], proj_cols[:, :2])
    proj_ext = jnp.concatenate([proj_below, proj_cols, proj_above], axis=1)

    ext_rows = slab_rows + 2
    mid_w = weight_ext[1, :, 1 : ext_rows + 1][:, :, None]
    next_w = weight_ext[0, :, 2 : ext_rows + 2][:, :, None]
    prev_w = weight_ext[2, :, 0:ext_rows][:, :, None]
    centre = proj_ext[:, 1 : ext_rows + 1]
    after = proj_ext[:, 2 : ext_rows + 2]
    before = proj_ext[:, 0:ext_rows]
    projection = mid_w * centre + next_w * after + prev_w * before
    coverage = mid_w * cover + next_w * cover + prev_w * cover
    residual_ext = (measured_ext - projection) / jnp.maximum(coverage, 1.0)
    global_rows = first_row - 1 + jnp.arange(ext_rows, dtype=jnp.int32)
    valid = (global_rows >= 0) & (global_rows < total_rows)
    residual_ext = jnp.where(valid[None, :, None], residual_ext, 0.0)
    residual = residual_ext[:, 1 : slab_rows + 1]

    back_rows = (
        axial_weight[0][:, :, None] * residual_ext[:, 0:slab_rows]
        + axial_weight[1][:, :, None] * residual
        + axial_weight[2][:, :, None] * residual_ext[:, 2 : slab_rows + 2]
    )
    back_chunks = all_gather_xy(back_rows.reshape(view_count * slab_rows, shard_width), xy_count)

    own_rows = first_row + jnp.arange(slab_rows, dtype=jnp.int32)
    row_weight = (
        jnp.where(own_rows[None, :] > 0, axial_weight[0], 0.0)
        + axial_weight[1]
        + jnp.where(own_rows[None, :] < total_rows - 1, axial_weight[2], 0.0)
    )
    volume_next = backward_update(back_chunks, band_start, volume, amplitude, column_offset, column_width, row_weight)
    return (volume_next, residual)


def solution(mesh):
    return jax.shard_map(
        local,
        mesh=mesh,
        in_specs=(
            P("gz", "xy"),
            P(None, "gz", "xy"),
            P(None, "xy"),
            P(None, "xy"),
            P(None, "xy"),
            P(None, "xy"),
            P(None, None, "gz"),
        ),
        out_specs=(P("gz", "xy"), P(None, "gz", "xy")),
        check_vma=False,
    )
```

```python
import jax
import jax.numpy as jnp
from jax import lax
from jax.experimental import pallas as pl
from jax.experimental.pallas import tpu as pltpu
from jax.sharding import PartitionSpec as P

B = 512
RELAX = 0.9
CHUNK = 2048
INTERPRET = False


def _band_mask(off, wid, rows, width):
    u = lax.broadcasted_iota(jnp.int32, (rows, width), 0)
    inside = (u - off).astype(jnp.uint32) < wid.astype(jnp.uint32)
    return jnp.where(inside, 1.0, 0.0).astype(jnp.bfloat16)


def _split(x):
    hi = x.astype(jnp.bfloat16)
    lo = (x - hi.astype(jnp.float32)).astype(jnp.bfloat16)
    return hi, lo


def _forward_kernel(start_ref, vol_ref, amp_ref, off_ref, wid_ref, out_ref, acc_ref):
    slab_rows, columns = vol_ref.shape
    view_count = amp_ref.shape[0]
    band = acc_ref.shape[2]
    chunks, _, shard_width = out_ref.shape
    detector_width = chunks * shard_width
    acc_ref[...] = jnp.zeros(acc_ref.shape, jnp.float32)
    row = lax.broadcasted_iota(jnp.int32, (slab_rows, CHUNK), 0)

    def body(j, carry):
        c0 = pl.multiple_of(j * CHUNK, CHUNK)
        cells = vol_ref[:, pl.ds(c0, CHUNK)]
        for v in range(view_count):
            amp = amp_ref[pl.ds(v, 1), pl.ds(c0, CHUNK)]
            off = off_ref[pl.ds(v, 1), pl.ds(c0, CHUNK)]
            wid = wid_ref[pl.ds(v, 1), pl.ds(c0, CHUNK)]
            cells_hi, cells_lo = _split(cells * amp)
            amp_hi, amp_lo = _split(amp)
            amp_rows = jnp.where(
                row == 0,
                amp_hi.astype(jnp.float32),
                jnp.where(row == 1, amp_lo.astype(jnp.float32), 0.0),
            ).astype(jnp.bfloat16)
            lhs = jnp.concatenate([cells_hi, cells_lo, amp_rows], axis=0)
            mask = _band_mask(off, wid, band, CHUNK)
            acc_ref[v] += lax.dot_general(
                lhs, mask, (((1,), (1,)), ((), ())), preferred_element_type=jnp.float32
            )
        return carry

    lax.fori_loop(0, columns // CHUNK, body, 0)
    height = slab_rows + 1
    placed = []
    for v in range(view_count):
        acc = acc_ref[v]
        summed = jnp.concatenate(
            [
                acc[:slab_rows] + acc[slab_rows : 2 * slab_rows],
                acc[2 * slab_rows : 2 * slab_rows + 1] + acc[2 * slab_rows + 1 : 2 * slab_rows + 2],
            ],
            axis=0,
        )
        ext = jnp.concatenate([summed, jnp.zeros((height, detector_width - band), jnp.float32)], axis=1)
        placed.append(pltpu.roll(ext, start_ref[v], 1))
    joined = jnp.concatenate(placed, axis=0)
    for k in range(chunks):
        out_ref[k] = joined[:, k * shard_width : (k + 1) * shard_width]


def forward_band(volume, amplitude, column_offset, column_width, band_start, chunks, shard_width):
    slab_rows = volume.shape[0]
    view_count = amplitude.shape[0]
    smem = pl.BlockSpec(memory_space=pltpu.SMEM)
    vmem = pl.BlockSpec(memory_space=pltpu.VMEM)
    return pl.pallas_call(
        _forward_kernel,
        out_shape=jax.ShapeDtypeStruct((chunks, view_count * (slab_rows + 1), shard_width), jnp.float32),
        in_specs=[smem, vmem, vmem, vmem, vmem],
        scratch_shapes=[pltpu.VMEM((view_count, 3 * slab_rows, B), jnp.float32)],
        cost_estimate=pl.CostEstimate(
            flops=2 * view_count * 3 * slab_rows * B * volume.shape[1],
            transcendentals=0,
            bytes_accessed=4 * (volume.size + 3 * amplitude.size),
        ),
        interpret=INTERPRET,
    )(band_start.reshape(-1), volume, amplitude, column_offset, column_width)


def _backward_kernel(start_ref, own_ref, got_ref, vol_ref, amp_ref, off_ref, wid_ref, rw_ref, out_ref, split_ref):
    slab_rows, columns = vol_ref.shape
    view_count, _, band = split_ref.shape
    chunks = 2 * own_ref.shape[0]
    detector_width = chunks * own_ref.shape[2]
    parity = lax.axis_index("xy") & 1
    for v in range(view_count):
        rows = slice(v * slab_rows, (v + 1) * slab_rows)
        full = jnp.concatenate(
            [
                jnp.where((k & 1) == parity, own_ref[k // 2, rows, :], got_ref[k // 2, rows, :])
                for k in range(chunks)
            ],
            axis=1,
        )
        rolled = pltpu.roll(full, (detector_width - start_ref[v]) % detector_width, 1)
        hi, lo = _split(rolled[:, :band])
        split_ref[v] = jnp.concatenate([hi, lo], axis=0)

    def body(j, carry):
        c0 = pl.multiple_of(j * CHUNK, CHUNK)
        correction = None
        normalizer = None
        for v in range(view_count):
            amp = amp_ref[pl.ds(v, 1), pl.ds(c0, CHUNK)]
            off = off_ref[pl.ds(v, 1), pl.ds(c0, CHUNK)]
            wid = wid_ref[pl.ds(v, 1), pl.ds(c0, CHUNK)]
            mask = _band_mask(off, wid, band, CHUNK)
            r = jnp.dot(split_ref[v], mask, preferred_element_type=jnp.float32)
            part = amp * (r[:slab_rows] + r[slab_rows:])
            mass = rw_ref[v] * (amp * wid.astype(jnp.float32))
            correction = part if correction is None else correction + part
            normalizer = mass if normalizer is None else normalizer + mass
        cells = vol_ref[:, pl.ds(c0, CHUNK)]
        out_ref[:, pl.ds(c0, CHUNK)] = cells + RELAX * correction / normalizer
        return carry

    lax.fori_loop(0, columns // CHUNK, body, 0)


def backward_update(back_halves, band_start, volume, amplitude, column_offset, column_width, row_weight):
    view_count = amplitude.shape[0]
    slab_rows = volume.shape[0]
    smem = pl.BlockSpec(memory_space=pltpu.SMEM)
    vmem = pl.BlockSpec(memory_space=pltpu.VMEM)
    return pl.pallas_call(
        _backward_kernel,
        out_shape=jax.ShapeDtypeStruct(volume.shape, jnp.float32),
        in_specs=[smem] + [vmem] * 7,
        scratch_shapes=[pltpu.VMEM((view_count, 2 * slab_rows, B), jnp.bfloat16)],
        interpret=INTERPRET,
    )(band_start.reshape(-1), *back_halves, volume, amplitude, column_offset, column_width, row_weight[:, :, None])


def _bit_count(count):
    bits = count.bit_length() - 1
    assert 1 << bits == count
    return bits


def reduce_scatter_xy(x, count):
    _, rows, width = x.shape
    bits = _bit_count(count)
    idx = lax.axis_index("xy")
    y = x.reshape((2,) * bits + (rows, width))
    for j in range(bits):
        axis = bits - 1 - j
        bit = (idx >> j) & 1
        keep = lax.dynamic_index_in_dim(y, bit, axis, keepdims=False)
        send = lax.dynamic_index_in_dim(y, 1 - bit, axis, keepdims=False)
        y = keep + lax.ppermute(send, "xy", [(i, i ^ (1 << j)) for i in range(count)])
    return y


def all_gather_xy(x, count):
    rows, width = x.shape
    bits = _bit_count(count)
    idx = lax.axis_index("xy")
    y = x
    for step, j in enumerate(reversed(range(1, bits))):
        bit = (idx >> j) & 1
        other = lax.ppermute(y, "xy", [(i, i ^ (1 << j)) for i in range(count)])
        low = jnp.where(bit == 0, y, other)
        high = jnp.where(bit == 0, other, y)
        y = jnp.stack([low, high], axis=step)
    y = y.reshape(count // 2, rows, width)
    return y, lax.ppermute(y, "xy", [(i, i ^ 1) for i in range(count)])


def local(volume, measured, band_start, column_offset, column_width, amplitude, axial_weight):
    slab_rows = volume.shape[0]
    view_count = amplitude.shape[0]
    xy_count = lax.axis_size("xy")
    gz_count = lax.axis_size("gz")
    shard_width = measured.shape[2]
    detector_width = shard_width * xy_count
    total_rows = slab_rows * gz_count
    first_row = lax.axis_index("gz") * slab_rows
    up_pairs = [(i, i + 1) for i in range(gz_count - 1)]
    down_pairs = [(i + 1, i) for i in range(gz_count - 1)]

    def pack(meas_rows, weight_cols):
        flat = jnp.transpose(weight_cols, (1, 0, 2)).reshape(view_count, 1, -1)
        flat = jnp.pad(flat, ((0, 0), (0, 0), (0, shard_width - flat.shape[2])))
        return jnp.concatenate([meas_rows, flat], axis=1)

    def unpack(packed):
        cols = packed[:, 1, : 3 * 2].reshape(view_count, 3, 2)
        return packed[:, :1], jnp.transpose(cols, (1, 0, 2))

    gz_index = lax.axis_index("gz")

    def exchange(upward, downward):
        if gz_count != 2:
            return lax.ppermute(upward, "gz", up_pairs), lax.ppermute(downward, "gz", down_pairs)
        got = lax.ppermute(jnp.where(gz_index == 0, upward, downward), "gz", [(0, 1), (1, 0)])
        return jnp.where(gz_index == 1, got, 0.0), jnp.where(gz_index == 0, got, 0.0)

    from_below, from_above = exchange(
        pack(measured[:, slab_rows - 1 :], axial_weight[:, :, slab_rows - 2 :]),
        pack(measured[:, :1], axial_weight[:, :, :2]),
    )
    meas_below, weight_below = unpack(from_below)
    meas_above, weight_above = unpack(from_above)
    measured_ext = jnp.concatenate([meas_below, measured, meas_above], axis=1)
    weight_ext = jnp.concatenate([weight_below, axial_weight, weight_above], axis=2)

    placed = forward_band(volume, amplitude, column_offset, column_width, band_start, xy_count, shard_width)
    band_height = slab_rows + 1
    reduced = reduce_scatter_xy(placed, xy_count).reshape(view_count, band_height, shard_width)
    proj_cols = reduced[:, :slab_rows]
    cover = reduced[:, slab_rows : slab_rows + 1]
    proj_below, proj_above = exchange(proj_cols[:, slab_rows - 2 :], proj_cols[:, :2])
    proj_ext = jnp.concatenate([proj_below, proj_cols, proj_above], axis=1)

    ext_rows = slab_rows + 2
    mid_w = weight_ext[1, :, 1 : ext_rows + 1][:, :, None]
    next_w = weight_ext[0, :, 2 : ext_rows + 2][:, :, None]
    prev_w = weight_ext[2, :, 0:ext_rows][:, :, None]
    centre = proj_ext[:, 1 : ext_rows + 1]
    after = proj_ext[:, 2 : ext_rows + 2]
    before = proj_ext[:, 0:ext_rows]
    projection = mid_w * centre + next_w * after + prev_w * before
    coverage = mid_w * cover + next_w * cover + prev_w * cover
    residual_ext = (measured_ext - projection) / jnp.maximum(coverage, 1.0)
    global_rows = first_row - 1 + jnp.arange(ext_rows, dtype=jnp.int32)
    valid = (global_rows >= 0) & (global_rows < total_rows)
    residual_ext = jnp.where(valid[None, :, None], residual_ext, 0.0)
    residual = residual_ext[:, 1 : slab_rows + 1]

    back_rows = (
        axial_weight[0][:, :, None] * residual_ext[:, 0:slab_rows]
        + axial_weight[1][:, :, None] * residual
        + axial_weight[2][:, :, None] * residual_ext[:, 2 : slab_rows + 2]
    )
    back_halves = all_gather_xy(back_rows.reshape(view_count * slab_rows, shard_width), xy_count)

    own_rows = first_row + jnp.arange(slab_rows, dtype=jnp.int32)
    row_weight = (
        jnp.where(own_rows[None, :] > 0, axial_weight[0], 0.0)
        + axial_weight[1]
        + jnp.where(own_rows[None, :] < total_rows - 1, axial_weight[2], 0.0)
    )
    volume_next = backward_update(back_halves, band_start, volume, amplitude, column_offset, column_width, row_weight)
    return (volume_next, residual)


def solution(mesh):
    return jax.shard_map(
        local,
        mesh=mesh,
        in_specs=(
            P("gz", "xy"),
            P(None, "gz", "xy"),
            P(None, "xy"),
            P(None, "xy"),
            P(None, "xy"),
            P(None, "xy"),
            P(None, None, "gz"),
        ),
        out_specs=(P("gz", "xy"), P(None, "gz", "xy")),
        check_vma=False,
    )
```

```python
import jax
import jax.numpy as jnp
from jax import lax
from jax.experimental import pallas as pl
from jax.experimental.pallas import tpu as pltpu
from jax.sharding import PartitionSpec as P

B = 512
RELAX = 0.9
CHUNK = 2048
FORWARD_CHUNK = 4096
INTERPRET = False


def _band_mask(off, wid, rows, width):
    u = lax.broadcasted_iota(jnp.int32, (rows, width), 0)
    inside = (u - off).astype(jnp.uint32) < wid.astype(jnp.uint32)
    return jnp.where(inside, 1.0, 0.0).astype(jnp.bfloat16)


def _split(x):
    hi = x.astype(jnp.bfloat16)
    lo = (x - hi.astype(jnp.float32)).astype(jnp.bfloat16)
    return hi, lo


def _forward_kernel(start_ref, vol_ref, amp_ref, off_ref, wid_ref, out_ref, acc_ref):
    slab_rows, columns = vol_ref.shape
    view_count = amp_ref.shape[0]
    band = acc_ref.shape[2]
    chunks, _, shard_width = out_ref.shape
    detector_width = chunks * shard_width
    acc_ref[...] = jnp.zeros(acc_ref.shape, jnp.float32)
    row = lax.broadcasted_iota(jnp.int32, (slab_rows, FORWARD_CHUNK), 0)

    def body(j, carry):
        c0 = pl.multiple_of(j * FORWARD_CHUNK, FORWARD_CHUNK)
        cells = vol_ref[:, pl.ds(c0, FORWARD_CHUNK)]
        for v in range(view_count):
            amp = amp_ref[pl.ds(v, 1), pl.ds(c0, FORWARD_CHUNK)]
            off = off_ref[pl.ds(v, 1), pl.ds(c0, FORWARD_CHUNK)]
            wid = wid_ref[pl.ds(v, 1), pl.ds(c0, FORWARD_CHUNK)]
            cells_hi, cells_lo = _split(cells * amp)
            amp_hi, amp_lo = _split(amp)
            amp_rows = jnp.where(
                row == 0,
                amp_hi.astype(jnp.float32),
                jnp.where(row == 1, amp_lo.astype(jnp.float32), 0.0),
            ).astype(jnp.bfloat16)
            lhs = jnp.concatenate([cells_hi, cells_lo, amp_rows], axis=0)
            mask = _band_mask(off, wid, band, FORWARD_CHUNK)
            acc_ref[v] += lax.dot_general(
                lhs, mask, (((1,), (1,)), ((), ())), preferred_element_type=jnp.float32
            )
        return carry

    lax.fori_loop(0, columns // FORWARD_CHUNK, body, 0)
    height = slab_rows + 1
    placed = []
    for v in range(view_count):
        acc = acc_ref[v]
        summed = jnp.concatenate(
            [
                acc[:slab_rows] + acc[slab_rows : 2 * slab_rows],
                acc[2 * slab_rows : 2 * slab_rows + 1] + acc[2 * slab_rows + 1 : 2 * slab_rows + 2],
            ],
            axis=0,
        )
        ext = jnp.concatenate([summed, jnp.zeros((height, detector_width - band), jnp.float32)], axis=1)
        placed.append(pltpu.roll(ext, start_ref[v], 1))
    joined = jnp.concatenate(placed, axis=0)
    for k in range(chunks):
        out_ref[k] = joined[:, k * shard_width : (k + 1) * shard_width]


def forward_band(volume, amplitude, column_offset, column_width, band_start, chunks, shard_width):
    slab_rows = volume.shape[0]
    view_count = amplitude.shape[0]
    smem = pl.BlockSpec(memory_space=pltpu.SMEM)
    vmem = pl.BlockSpec(memory_space=pltpu.VMEM)
    return pl.pallas_call(
        _forward_kernel,
        out_shape=jax.ShapeDtypeStruct((chunks, view_count * (slab_rows + 1), shard_width), jnp.float32),
        in_specs=[smem, vmem, vmem, vmem, vmem],
        scratch_shapes=[pltpu.VMEM((view_count, 3 * slab_rows, B), jnp.float32)],
        cost_estimate=pl.CostEstimate(
            flops=2 * view_count * 3 * slab_rows * B * volume.shape[1],
            transcendentals=0,
            bytes_accessed=4 * (volume.size + 3 * amplitude.size),
        ),
        interpret=INTERPRET,
    )(band_start.reshape(-1), volume, amplitude, column_offset, column_width)


def _backward_kernel(start_ref, own_ref, got_ref, vol_ref, amp_ref, off_ref, wid_ref, rw_ref, out_ref, split_ref):
    slab_rows, columns = vol_ref.shape
    view_count, _, band = split_ref.shape
    chunks = 2 * own_ref.shape[0]
    detector_width = chunks * own_ref.shape[2]
    parity = lax.axis_index("xy") & 1
    for v in range(view_count):
        rows = slice(v * slab_rows, (v + 1) * slab_rows)
        full = jnp.concatenate(
            [
                jnp.where((k & 1) == parity, own_ref[k // 2, rows, :], got_ref[k // 2, rows, :])
                for k in range(chunks)
            ],
            axis=1,
        )
        rolled = pltpu.roll(full, (detector_width - start_ref[v]) % detector_width, 1)
        hi, lo = _split(rolled[:, :band])
        split_ref[v] = jnp.concatenate([hi, lo], axis=0)

    def body(j, carry):
        c0 = pl.multiple_of(j * CHUNK, CHUNK)
        correction = None
        normalizer = None
        for v in range(view_count):
            amp = amp_ref[pl.ds(v, 1), pl.ds(c0, CHUNK)]
            off = off_ref[pl.ds(v, 1), pl.ds(c0, CHUNK)]
            wid = wid_ref[pl.ds(v, 1), pl.ds(c0, CHUNK)]
            mask = _band_mask(off, wid, band, CHUNK)
            r = jnp.dot(split_ref[v], mask, preferred_element_type=jnp.float32)
            part = amp * (r[:slab_rows] + r[slab_rows:])
            mass = rw_ref[v] * (amp * wid.astype(jnp.float32))
            correction = part if correction is None else correction + part
            normalizer = mass if normalizer is None else normalizer + mass
        cells = vol_ref[:, pl.ds(c0, CHUNK)]
        out_ref[:, pl.ds(c0, CHUNK)] = cells + RELAX * correction / normalizer
        return carry

    lax.fori_loop(0, columns // CHUNK, body, 0)


def backward_update(back_halves, band_start, volume, amplitude, column_offset, column_width, row_weight):
    view_count = amplitude.shape[0]
    slab_rows = volume.shape[0]
    smem = pl.BlockSpec(memory_space=pltpu.SMEM)
    vmem = pl.BlockSpec(memory_space=pltpu.VMEM)
    return pl.pallas_call(
        _backward_kernel,
        out_shape=jax.ShapeDtypeStruct(volume.shape, jnp.float32),
        in_specs=[smem] + [vmem] * 7,
        scratch_shapes=[pltpu.VMEM((view_count, 2 * slab_rows, B), jnp.bfloat16)],
        interpret=INTERPRET,
    )(band_start.reshape(-1), *back_halves, volume, amplitude, column_offset, column_width, row_weight[:, :, None])


def _bit_count(count):
    bits = count.bit_length() - 1
    assert 1 << bits == count
    return bits


def reduce_scatter_xy(x, count):
    _, rows, width = x.shape
    bits = _bit_count(count)
    idx = lax.axis_index("xy")
    y = x.reshape((2,) * bits + (rows, width))
    for j in range(bits):
        axis = bits - 1 - j
        bit = (idx >> j) & 1
        keep = lax.dynamic_index_in_dim(y, bit, axis, keepdims=False)
        send = lax.dynamic_index_in_dim(y, 1 - bit, axis, keepdims=False)
        y = keep + lax.ppermute(send, "xy", [(i, i ^ (1 << j)) for i in range(count)])
    return y


def all_gather_xy(x, count):
    rows, width = x.shape
    bits = _bit_count(count)
    idx = lax.axis_index("xy")
    y = x
    for step, j in enumerate(reversed(range(1, bits))):
        bit = (idx >> j) & 1
        other = lax.ppermute(y, "xy", [(i, i ^ (1 << j)) for i in range(count)])
        low = jnp.where(bit == 0, y, other)
        high = jnp.where(bit == 0, other, y)
        y = jnp.stack([low, high], axis=step)
    y = y.reshape(count // 2, rows, width)
    return y, lax.ppermute(y, "xy", [(i, i ^ 1) for i in range(count)])


def local(volume, measured, band_start, column_offset, column_width, amplitude, axial_weight):
    slab_rows = volume.shape[0]
    view_count = amplitude.shape[0]
    xy_count = lax.axis_size("xy")
    gz_count = lax.axis_size("gz")
    shard_width = measured.shape[2]
    detector_width = shard_width * xy_count
    total_rows = slab_rows * gz_count
    first_row = lax.axis_index("gz") * slab_rows
    up_pairs = [(i, i + 1) for i in range(gz_count - 1)]
    down_pairs = [(i + 1, i) for i in range(gz_count - 1)]

    def pack(meas_rows, weight_cols):
        flat = jnp.transpose(weight_cols, (1, 0, 2)).reshape(view_count, 1, -1)
        flat = jnp.pad(flat, ((0, 0), (0, 0), (0, shard_width - flat.shape[2])))
        return jnp.concatenate([meas_rows, flat], axis=1)

    def unpack(packed):
        cols = packed[:, 1, : 3 * 2].reshape(view_count, 3, 2)
        return packed[:, :1], jnp.transpose(cols, (1, 0, 2))

    gz_index = lax.axis_index("gz")

    def exchange(upward, downward):
        if gz_count != 2:
            return lax.ppermute(upward, "gz", up_pairs), lax.ppermute(downward, "gz", down_pairs)
        got = lax.ppermute(jnp.where(gz_index == 0, upward, downward), "gz", [(0, 1), (1, 0)])
        return jnp.where(gz_index == 1, got, 0.0), jnp.where(gz_index == 0, got, 0.0)

    from_below, from_above = exchange(
        pack(measured[:, slab_rows - 1 :], axial_weight[:, :, slab_rows - 2 :]),
        pack(measured[:, :1], axial_weight[:, :, :2]),
    )
    meas_below, weight_below = unpack(from_below)
    meas_above, weight_above = unpack(from_above)
    measured_ext = jnp.concatenate([meas_below, measured, meas_above], axis=1)
    weight_ext = jnp.concatenate([weight_below, axial_weight, weight_above], axis=2)

    placed = forward_band(volume, amplitude, column_offset, column_width, band_start, xy_count, shard_width)
    band_height = slab_rows + 1
    reduced = reduce_scatter_xy(placed, xy_count).reshape(view_count, band_height, shard_width)
    proj_cols = reduced[:, :slab_rows]
    cover = reduced[:, slab_rows : slab_rows + 1]
    proj_below, proj_above = exchange(proj_cols[:, slab_rows - 2 :], proj_cols[:, :2])
    proj_ext = jnp.concatenate([proj_below, proj_cols, proj_above], axis=1)

    ext_rows = slab_rows + 2
    mid_w = weight_ext[1, :, 1 : ext_rows + 1][:, :, None]
    next_w = weight_ext[0, :, 2 : ext_rows + 2][:, :, None]
    prev_w = weight_ext[2, :, 0:ext_rows][:, :, None]
    centre = proj_ext[:, 1 : ext_rows + 1]
    after = proj_ext[:, 2 : ext_rows + 2]
    before = proj_ext[:, 0:ext_rows]
    projection = mid_w * centre + next_w * after + prev_w * before
    coverage = mid_w * cover + next_w * cover + prev_w * cover
    residual_ext = (measured_ext - projection) / jnp.maximum(coverage, 1.0)
    global_rows = first_row - 1 + jnp.arange(ext_rows, dtype=jnp.int32)
    valid = (global_rows >= 0) & (global_rows < total_rows)
    residual_ext = jnp.where(valid[None, :, None], residual_ext, 0.0)
    residual = residual_ext[:, 1 : slab_rows + 1]

    back_rows = (
        axial_weight[0][:, :, None] * residual_ext[:, 0:slab_rows]
        + axial_weight[1][:, :, None] * residual
        + axial_weight[2][:, :, None] * residual_ext[:, 2 : slab_rows + 2]
    )
    back_halves = all_gather_xy(back_rows.reshape(view_count * slab_rows, shard_width), xy_count)

    own_rows = first_row + jnp.arange(slab_rows, dtype=jnp.int32)
    row_weight = (
        jnp.where(own_rows[None, :] > 0, axial_weight[0], 0.0)
        + axial_weight[1]
        + jnp.where(own_rows[None, :] < total_rows - 1, axial_weight[2], 0.0)
    )
    volume_next = backward_update(back_halves, band_start, volume, amplitude, column_offset, column_width, row_weight)
    return (volume_next, residual)


def solution(mesh):
    return jax.shard_map(
        local,
        mesh=mesh,
        in_specs=(
            P("gz", "xy"),
            P(None, "gz", "xy"),
            P(None, "xy"),
            P(None, "xy"),
            P(None, "xy"),
            P(None, "xy"),
            P(None, None, "gz"),
        ),
        out_specs=(P("gz", "xy"), P(None, "gz", "xy")),
        check_vma=False,
    )
```
